32 devices in a mesh: fh: 2 (over y), wa: 4 (over x, core), ha: 4 (over z).
Axes of the slice: x: 2, y: 2, z: 4, core: 2. Of those that a mesh axis runs over, the one named last changes fastest.
Arguments:
- queries: bfloat16 [2, 4, 384, 1536], P('fh', 'wa', None, 'ha'), may hold values from -6 to 6
- key_states: bfloat16 [2, 4, 384, 1536], P('fh', 'wa', None, 'ha'), may hold values from -6 to 6
- value_states: bfloat16 [2, 4, 384, 1536], P('fh', 'wa', None, 'ha'), may hold values from -6 to 6
- valid_mask: int32 [2, 4, 384], P('fh', 'wa'), may hold values from 0 to 1, as said below
- out_weight: bfloat16 [1536, 3072], P('ha'), may hold values from -0.15625 to 0.15625
- out_cotangent: bfloat16 [2, 4, 384, 3072], P('fh', 'wa', 'ha'), may hold values from -6 to 6
Outputs:
- layer_out: bfloat16 [2, 4, 384, 3072], P('fh', 'wa', 'ha')
- grad_queries: bfloat16 [2, 4, 384, 1536], P('fh', 'wa', None, 'ha')
- grad_keys: bfloat16 [2, 4, 384, 1536], P('fh', 'wa', None, 'ha')
- grad_values: bfloat16 [2, 4, 384, 1536], P('fh', 'wa', None, 'ha')
- grad_weight: float32 [3072, 1536], P(('fh', 'wa'), 'ha')
The draws below stay inside these ranges and needn't reach their ends.
Inputs may be any that keep to these rules, and one draw needn't show every extreme that they name: `valid_mask`: within each tile of 384 tokens the valid tokens come first, and at least half of the tile is valid.
All inputs are finite; a program needn't handle non-finite values.
Results may differ from the reference program's by a relative error of at most 0.015.
Values may be sent and summed in bfloat16 or wider, within the bound.
No kernel may reach another device: no remote copies, remote signals or barrier semaphores. Data moves between devices by JAX's collectives and lax.ppermute only.
A program may use at most 128 MiB of HBM per device.

```python
import jax
import jax.numpy as jnp
from jax import lax

D = 3072
HEADS = 12
HD = 128
TILE = 384
FT = 1
COL = 384
HT = 2
WT = 4


def base_field(key, salt):
    shape = (HT, WT, COL, HEADS * HD)
    noise = jax.random.normal(jax.random.fold_in(key, salt), shape, jnp.float32)
    return jnp.clip(noise * 1.4, -6.0, 6.0)


def draw_queries(key, part):
    field = base_field(key, 11)
    return field.astype(jnp.bfloat16)


def draw_key_states(key, part):
    field = base_field(key, 21)
    return field.astype(jnp.bfloat16)


def draw_valid_mask(key, part):
    counts = jax.random.randint(key, (HT, WT, FT, 1), TILE // 2, TILE + 1)
    place = jnp.arange(TILE)
    return (place < counts).astype(jnp.int32).reshape(HT, WT, COL)


def raised(values, rng, source, target, parts, factor):
    owner, partner = [(jnp.arange(values.shape[axis_at]) // (values.shape[axis_at] // parts)).reshape([-1 if axis == axis_at else 1 for axis in range(values.ndim)]) for axis_at in (source, target)]
    chosen = jax.random.permutation(rng, parts)[partner]
    strong = (owner == chosen) | (owner == (partner + parts // 2) % parts)
    return jnp.where(strong, factor * values, values)


def shard_levels(stream_key, shape, split, smallest, top_value):
    gain = 1.0
    for dim, blocks in split:
        draws = jax.random.uniform(jax.random.fold_in(jax.random.fold_in(stream_key, 6), dim), (blocks,), jnp.float32, smallest / len(split), top_value / len(split))
        gain = gain * jnp.repeat(jnp.exp(draws), shape[dim] // blocks).reshape((-1,) + (1,) * (len(shape) - 1 - dim))
    return gain


def bell_draw(own_key, dims, width, reach, pieces=(), kind=jnp.bfloat16):
    entries = width * jax.random.normal(own_key, dims, jnp.float32)
    if pieces:
        entries = entries * shard_levels(own_key, dims, pieces, -0.22, 0.18)
    return jnp.clip(entries, -reach, reach).astype(kind)


def noise_with(key, shape, deviation, bound, split, heavy, kind=jnp.bfloat16):
    drawn = deviation * jax.random.normal(key, shape, jnp.float32)
    if split:
        drawn = drawn * shard_levels(key, shape, split, -0.22, 0.18)
    return jnp.clip(raised(drawn, jax.random.fold_in(key, 3), *heavy), -bound, bound).astype(kind)


def setup_inputs(seed: int = 0) -> dict:
    key_list = jax.random.split(jax.random.key(seed), 7)
    queries = draw_queries(jax.random.fold_in(key_list[6], 71), 0)
    key_states = draw_key_states(jax.random.fold_in(key_list[6], 71), 0)
    value_states = bell_draw(key_list[2], (HT, WT, COL, HEADS * HD), 1.0, 6.0, ((0, 2), (1, 4), (3, 4)))
    valid_mask = draw_valid_mask(jax.random.fold_in(key_list[6], 71), 0)
    out_weight = bell_draw(key_list[4], (HEADS * HD, D), (HEADS * HD) ** -0.5, 0.15625, ((0, 4),))
    out_cotangent = noise_with(key_list[5], (HT, WT, COL, D), 0.5, 6.0, ((0, 2), (1, 4), (2, 4)), (0, 3, 2, 2.0))
    return {"queries": queries, "key_states": key_states, "value_states": value_states, "valid_mask": valid_mask, "out_weight": out_weight, "out_cotangent": out_cotangent}


masked_score = -1.0e30


def int_starts(values_in):
    return tuple(jnp.asarray(value, dtype=jnp.int32) for value in values_in)


def window(padded, row_index, column_index):
    starts = int_starts((row_index, column_index) + (0,) * (padded.ndim - 2))
    block_shape = (3, 3) + padded.shape[2:]
    block = lax.dynamic_slice(padded, starts, block_shape)
    return block.reshape((9 * padded.shape[2],) + padded.shape[3:])


def rounded(values_in):
    return lax.optimization_barrier(values_in.astype(jnp.bfloat16)).astype(jnp.float32)


def reference(queries, key_states, value_states, valid_mask, out_weight, out_cotangent):
    score_scale = HD ** -0.5
    features = HEADS * HD
    tile_count = HT * WT
    spread = ((1, 1), (1, 1), (0, 0), (0, 0))
    key_pad = jnp.pad(key_states, spread)
    value_pad = jnp.pad(value_states, spread)
    flag_pad = jnp.pad(valid_mask, ((1, 1), (1, 1), (0, 0)))
    query_tiles = queries.reshape(tile_count, COL, HEADS, HD)
    tile_ids = jnp.arange(tile_count, dtype=jnp.int32)

    def tile_scores(tile_index):
        row_index = (tile_index // WT).astype(jnp.int32)
        column_index = (tile_index % WT).astype(jnp.int32)
        query_tile = query_tiles[tile_index].astype(jnp.float32)
        key_block = window(key_pad, row_index, column_index).astype(jnp.float32).reshape(9 * COL, HEADS, HD)
        value_block = window(value_pad, row_index, column_index).astype(jnp.float32).reshape(9 * COL, HEADS, HD)
        allowed = window(flag_pad, row_index, column_index) > 0
        scores = jnp.einsum("qhd,khd->hqk", query_tile, key_block) * score_scale
        scores = jnp.where(allowed[None, None, :], scores, masked_score)
        return query_tile, key_block, value_block, scores, row_index, column_index

    def forward_tile(tile_index):
        query_tile, key_block, value_block, scores, row_index, column_index = tile_scores(tile_index)
        row_max = jnp.max(scores, axis=2, keepdims=True)
        exp_terms = jnp.exp(scores - row_max)
        row_total = jnp.sum(exp_terms, axis=2, keepdims=True)
        soft_probs = rounded(exp_terms / row_total)
        attended = jnp.einsum("hqk,khd->qhd", soft_probs, value_block).astype(jnp.bfloat16)
        return attended.reshape(COL, features), row_max, row_total

    attended, row_maxes, row_totals = lax.map(forward_tile, tile_ids)
    attended_flat = attended.reshape(tile_count * COL, features)
    layer_out = jnp.dot(attended_flat, out_weight, preferred_element_type=jnp.float32).astype(jnp.bfloat16)
    layer_out = layer_out.reshape(HT, WT, COL, D)
    cotangent_flat = out_cotangent.reshape(tile_count * COL, D)
    grad_attended = jnp.dot(cotangent_flat, out_weight.T, preferred_element_type=jnp.float32).astype(jnp.bfloat16)
    grad_weight = jnp.dot(cotangent_flat.T, attended_flat, preferred_element_type=jnp.float32)
    row_dot = jnp.sum((grad_attended.astype(jnp.float32) * attended_flat.astype(jnp.float32)).reshape(tile_count, COL, HEADS, HD), axis=3)
    grad_tiles = grad_attended.reshape(tile_count, COL, HEADS, HD)

    def backward_tile(partials, tile_index):
        query_tile, key_block, value_block, scores, row_index, column_index = tile_scores(tile_index)
        weights = jnp.exp(scores - row_maxes[tile_index]) / row_totals[tile_index]
        soft_probs = rounded(weights)
        grad_tile = grad_tiles[tile_index].astype(jnp.float32)
        grad_probs = jnp.einsum("qhd,khd->hqk", grad_tile, value_block)
        grad_scores = rounded(weights * (grad_probs - jnp.transpose(row_dot[tile_index])[:, :, None]))
        grad_query = (jnp.einsum("hqk,khd->qhd", grad_scores, key_block) * score_scale).astype(jnp.bfloat16)
        key_part = jnp.einsum("hqk,qhd->khd", grad_scores, query_tile) * score_scale
        value_part = jnp.einsum("hqk,qhd->khd", soft_probs, grad_tile)
        both_parts = jnp.stack((key_part, value_part)).reshape(2, 3, 3, COL, features).astype(partials.dtype)
        starts = int_starts((0, row_index, column_index, 0, 0))
        block_shape = (2, 3, 3, COL, features)
        partials = lax.dynamic_update_slice(partials, lax.dynamic_slice(partials, starts, block_shape) + both_parts, starts)
        return partials, grad_query.reshape(COL, features)

    zero_buffer = jnp.zeros((2, HT + 2, WT + 2, COL, features), jnp.float32)
    partials, grad_rows = lax.scan(backward_tile, zero_buffer, tile_ids)
    grad_queries = grad_rows.reshape(HT, WT, COL, features)
    grad_keys = partials[0, 1:-1, 1:-1].astype(jnp.bfloat16)
    grad_values = partials[1, 1:-1, 1:-1].astype(jnp.bfloat16)
    return (layer_out, grad_queries, grad_keys, grad_values, grad_weight)
```

```python
import functools

import jax
import jax.numpy as jnp
from jax import lax
from jax.experimental import pallas as pl
from jax.experimental.pallas import tpu as pltpu
from jax.sharding import PartitionSpec as P

HD = 128
MASKED = -1e30
QCHUNK = 128
FLAG_ROWS = 16


def shift_pairs(count, steps):
    return [(source, source + steps) for source in range(count) if 0 <= source + steps < count]


def shifted(value, axis, steps):
    return lax.ppermute(value, axis, shift_pairs(lax.axis_size(axis), steps))


def cyclic(value, axis, steps):
    count = lax.axis_size(axis)
    return lax.ppermute(value, axis, [(i, (i + steps) % count) for i in range(count)])


def scores_of(mask_ref, q_ref, k_ref, scale):
    q = q_ref[...]
    k = k_ref[...].reshape(-1, HD)
    s = lax.dot_general(q, k, (((1,), (1,)), ((), ())), preferred_element_type=jnp.float32)
    s = s * scale
    return jnp.where(mask_ref[...] > 0, s, MASKED)


def forward_kernel(scale, mask_ref, q_ref, k_ref, v_ref, o_ref):
    s = scores_of(mask_ref, q_ref, k_ref, scale)
    m = jnp.max(s, axis=1, keepdims=True)
    e = jnp.exp(s - m)
    total = jnp.sum(e, axis=1, keepdims=True)
    p = (e / total).astype(jnp.bfloat16)
    v = v_ref[...].reshape(-1, HD)
    o_ref[...] = jnp.dot(p, v, preferred_element_type=jnp.float32).astype(o_ref.dtype)


def backward_kernel(scale, mask_ref, q_ref, k_ref, v_ref, o_ref, do_ref, dq_ref, dkv_ref):
    chunk = pl.program_id(1)
    s = scores_of(mask_ref, q_ref, k_ref, scale)
    m = jnp.max(s, axis=1, keepdims=True)
    e = jnp.exp(s - m)
    total = jnp.sum(e, axis=1, keepdims=True)
    w = e / total
    p = w.astype(jnp.bfloat16)
    do = do_ref[...]
    row_dot = jnp.sum(
        do.astype(jnp.float32) * o_ref[...].astype(jnp.float32), axis=1, keepdims=True
    )
    k = k_ref[...].reshape(-1, HD)
    v = v_ref[...].reshape(-1, HD)
    dp = lax.dot_general(do, v, (((1,), (1,)), ((), ())), preferred_element_type=jnp.float32)
    ds = (w * (dp - row_dot)).astype(jnp.bfloat16)
    dq = jnp.dot(ds, k, preferred_element_type=jnp.float32) * scale
    dq_ref[...] = dq.astype(dq_ref.dtype)
    contract0 = (((0,), (0,)), ((), ()))
    dk = lax.dot_general(ds, q_ref[...], contract0, preferred_element_type=jnp.float32) * scale
    dv = lax.dot_general(p, do, contract0, preferred_element_type=jnp.float32)
    tiles, tokens = k_ref.shape[0], k_ref.shape[1]
    dk = dk.reshape(tiles, tokens, HD)
    dv = dv.reshape(tiles, tokens, HD)

    @pl.when(chunk == 0)
    def _():
        dkv_ref[:, :tokens, :] = dk
        dkv_ref[:, tokens:, :] = dv

    @pl.when(chunk > 0)
    def _():
        dkv_ref[:, :tokens, :] += dk
        dkv_ref[:, tokens:, :] += dv


def attention_forward(mask, queries, window):
    tokens, features = queries.shape
    tiles = window.shape[0]
    heads = features // HD
    chunks = tokens // QCHUNK
    scale = HD ** (-0.5)
    return pl.pallas_call(
        functools.partial(forward_kernel, scale),
        grid=(heads, chunks),
        in_specs=[
            pl.BlockSpec((1, tiles * tokens), lambda h, c: (0, 0)),
            pl.BlockSpec((QCHUNK, HD), lambda h, c: (c, h)),
            pl.BlockSpec((tiles, tokens, HD), lambda h, c: (0, 0, h)),
            pl.BlockSpec((tiles, tokens, HD), lambda h, c: (0, 1, h)),
        ],
        out_specs=pl.BlockSpec((QCHUNK, HD), lambda h, c: (c, h)),
        out_shape=jax.ShapeDtypeStruct((tokens, features), jnp.bfloat16),
        name="tile_attention_forward",
    )(mask, queries, window, window)


def attention_backward(mask, queries, window, attended, grad_attended):
    tokens, features = queries.shape
    tiles = window.shape[0]
    heads = features // HD
    chunks = tokens // QCHUNK
    scale = HD ** (-0.5)
    return pl.pallas_call(
        functools.partial(backward_kernel, scale),
        grid=(heads, chunks),
        in_specs=[
            pl.BlockSpec((1, tiles * tokens), lambda h, c: (0, 0)),
            pl.BlockSpec((QCHUNK, HD), lambda h, c: (c, h)),
            pl.BlockSpec((tiles, tokens, HD), lambda h, c: (0, 0, h)),
            pl.BlockSpec((tiles, tokens, HD), lambda h, c: (0, 1, h)),
            pl.BlockSpec((QCHUNK, HD), lambda h, c: (c, h)),
            pl.BlockSpec((QCHUNK, HD), lambda h, c: (c, h)),
        ],
        out_specs=[
            pl.BlockSpec((QCHUNK, HD), lambda h, c: (c, h)),
            pl.BlockSpec((tiles, 2 * tokens, HD), lambda h, c: (0, 0, h)),
        ],
        out_shape=[
            jax.ShapeDtypeStruct((tokens, features), jnp.bfloat16),
            jax.ShapeDtypeStruct((tiles, 2 * tokens, features), jnp.float32),
        ],
        name="tile_attention_backward",
    )(mask, queries, window, window, attended, grad_attended)


def gather_over(piece, axis):
    count = lax.axis_size(axis)
    me = lax.axis_index(axis)
    received = [piece] + [cyclic(piece, axis, steps) for steps in range(1, count)]
    ordered = jnp.stack([received[(-k) % count] for k in range(count)])
    return jnp.roll(ordered, me, axis=0)


def scatter_sum(full, axis, dim):
    count = lax.axis_size(axis)
    me = lax.axis_index(axis)
    size = full.shape[dim] // count

    def part(index):
        return lax.dynamic_slice_in_dim(full, index * size, size, axis=dim)

    total = part(me).astype(jnp.float32)
    for steps in range(1, count):
        sent = part((me + steps) % count).astype(jnp.bfloat16)
        total = total + cyclic(sent, axis, steps).astype(jnp.float32)
    return total


def body(queries, key_states, value_states, valid_mask, out_weight, out_cotangent):
    tile_rows, tile_columns, tokens, features = queries.shape
    assert tile_rows == 1 and tile_columns == 1
    model_width = out_weight.shape[1]
    q = queries[0, 0]
    flag_rows = jnp.zeros((FLAG_ROWS, features), jnp.bfloat16)
    flag_rows = flag_rows.at[0, :tokens].set(valid_mask[0, 0].astype(jnp.bfloat16))
    packed = jnp.concatenate([key_states[0, 0], value_states[0, 0], flag_rows], axis=0)

    with jax.named_scope("halo_exchange"):
        column = jnp.stack([shifted(packed, "fh", 1), packed, shifted(packed, "fh", -1)])
        window = jnp.concatenate(
            [shifted(column, "wa", 1), column, shifted(column, "wa", -1)], axis=0
        )
    tiles = window.shape[0]
    mask = window[:, 2 * tokens, :tokens].reshape(1, tiles * tokens).astype(jnp.float32)

    with jax.named_scope("cotangent_gather"):
        cot_pieces = gather_over(out_cotangent[0, 0], "ha")
        cot_all = cot_pieces.reshape(-1, model_width)

    with jax.named_scope("attention_forward"):
        attended = attention_forward(mask, q, window)

    with jax.named_scope("output_projection"):
        projected = jnp.dot(attended, out_weight, preferred_element_type=jnp.float32)
        layer_out = scatter_sum(projected, "ha", 0).astype(jnp.bfloat16)

    with jax.named_scope("grad_attended"):
        grad_attended = lax.dot_general(
            cot_all, out_weight, (((1,), (1,)), ((), ())), preferred_element_type=jnp.float32
        ).astype(jnp.bfloat16)

    with jax.named_scope("attention_backward"):
        grad_q, partials = attention_backward(mask, q, window, attended, grad_attended)

    with jax.named_scope("grad_weight"):
        weight_part = lax.dot_general(
            cot_all, attended, (((0,), (0,)), ((), ())), preferred_element_type=jnp.float32
        )
        grad_weight = scatter_sum(scatter_sum(weight_part, "fh", 0), "wa", 0)

    with jax.named_scope("halo_reduction"):
        sides = partials.astype(jnp.bfloat16)
        middle = (
            partials[3:6]
            + shifted(sides[0:3], "wa", -1).astype(jnp.float32)
            + shifted(sides[6:9], "wa", 1).astype(jnp.float32)
        )
        middle_sides = middle.astype(jnp.bfloat16)
        own = (
            middle[1]
            + shifted(middle_sides[0], "fh", -1).astype(jnp.float32)
            + shifted(middle_sides[2], "fh", 1).astype(jnp.float32)
        )
    grad_keys = own[:tokens].astype(jnp.bfloat16)
    grad_values = own[tokens:].astype(jnp.bfloat16)
    expand = lambda x: x[None, None]
    return (
        expand(layer_out),
        expand(grad_q),
        expand(grad_keys),
        expand(grad_values),
        grad_weight,
    )


def solution(mesh):
    return jax.shard_map(
        body,
        mesh=mesh,
        in_specs=(
            P("fh", "wa", None, "ha"),
            P("fh", "wa", None, "ha"),
            P("fh", "wa", None, "ha"),
            P("fh", "wa", None),
            P("ha", None),
            P("fh", "wa", "ha", None),
        ),
        out_specs=(
            P("fh", "wa", "ha", None),
            P("fh", "wa", None, "ha"),
            P("fh", "wa", None, "ha"),
            P("fh", "wa", None, "ha"),
            P(("fh", "wa"), "ha"),
        ),
        check_vma=False,
    )
```

```python
import functools

import jax
import jax.numpy as jnp
from jax import lax
from jax.experimental import pallas as pl
from jax.experimental.pallas import tpu as pltpu
from jax.sharding import PartitionSpec as P

HD = 128
MASKED = -1e30
FORWARD_CHUNK = 384
BACKWARD_CHUNK = 192
FLAG_ROWS = 16


def shift_pairs(count, steps):
    return [(source, source + steps) for source in range(count) if 0 <= source + steps < count]


def shifted(value, axis, steps):
    return lax.ppermute(value, axis, shift_pairs(lax.axis_size(axis), steps))


def cyclic(value, axis, steps):
    count = lax.axis_size(axis)
    return lax.ppermute(value, axis, [(i, (i + steps) % count) for i in range(count)])


def scores_of(mask_ref, q_ref, k_ref, scale):
    q = q_ref[...]
    k = k_ref[...].reshape(-1, HD)
    s = lax.dot_general(q, k, (((1,), (1,)), ((), ())), preferred_element_type=jnp.float32)
    return s * scale + mask_ref[...]


def forward_kernel(scale, mask_ref, q_ref, k_ref, v_ref, o_ref):
    s = scores_of(mask_ref, q_ref, k_ref, scale)
    m = jnp.max(s, axis=1, keepdims=True)
    e = jnp.exp(s - m)
    total = jnp.sum(e, axis=1, keepdims=True)
    p = (e * (1.0 / total)).astype(jnp.bfloat16)
    v = v_ref[...].reshape(-1, HD)
    o_ref[...] = jnp.dot(p, v, preferred_element_type=jnp.float32).astype(o_ref.dtype)


def backward_kernel(scale, mask_ref, q_ref, k_ref, v_ref, o_ref, do_ref, dq_ref, side_ref, mid_ref, acc_ref):
    chunk = pl.program_id(1)
    s = scores_of(mask_ref, q_ref, k_ref, scale)
    m = jnp.max(s, axis=1, keepdims=True)
    e = jnp.exp(s - m)
    total = jnp.sum(e, axis=1, keepdims=True)
    w = e * (1.0 / total)
    p = w.astype(jnp.bfloat16)
    do = do_ref[...]
    row_dot = jnp.sum(
        do.astype(jnp.float32) * o_ref[...].astype(jnp.float32), axis=1, keepdims=True
    )
    k = k_ref[...].reshape(-1, HD)
    v = v_ref[...].reshape(-1, HD)
    dp = lax.dot_general(do, v, (((1,), (1,)), ((), ())), preferred_element_type=jnp.float32)
    ds = (w * (dp - row_dot)).astype(jnp.bfloat16)
    dq = jnp.dot(ds, k, preferred_element_type=jnp.float32) * scale
    dq_ref[...] = dq.astype(dq_ref.dtype)
    contract0 = (((0,), (0,)), ((), ()))
    dk = lax.dot_general(ds, q_ref[...], contract0, preferred_element_type=jnp.float32) * scale
    dv = lax.dot_general(p, do, contract0, preferred_element_type=jnp.float32)
    tiles, tokens = k_ref.shape[0], k_ref.shape[1]
    dk = dk.reshape(tiles, tokens, HD)
    dv = dv.reshape(tiles, tokens, HD)

    @pl.when(chunk == 0)
    def _():
        acc_ref[:, :tokens, :] = dk
        acc_ref[:, tokens:, :] = dv

    @pl.when(chunk > 0)
    def _():
        acc_ref[:, :tokens, :] += dk
        acc_ref[:, tokens:, :] += dv

    @pl.when(chunk == pl.num_programs(1) - 1)
    def _():
        side_ref[...] = acc_ref[...].astype(side_ref.dtype)
        third = tiles // 3
        mid_ref[...] = acc_ref[third : 2 * third]


def attention_forward(mask, queries, window):
    tokens, features = queries.shape
    tiles = window.shape[0]
    heads = features // HD
    chunk = FORWARD_CHUNK
    chunks = tokens // chunk
    scale = HD ** (-0.5)
    return pl.pallas_call(
        functools.partial(forward_kernel, scale),
        grid=(heads, chunks),
        in_specs=[
            pl.BlockSpec((1, tiles * tokens), lambda h, c: (0, 0)),
            pl.BlockSpec((chunk, HD), lambda h, c: (c, h)),
            pl.BlockSpec((tiles, tokens, HD), lambda h, c: (0, 0, h)),
            pl.BlockSpec((tiles, tokens, HD), lambda h, c: (0, 1, h)),
        ],
        out_specs=pl.BlockSpec((chunk, HD), lambda h, c: (c, h)),
        out_shape=jax.ShapeDtypeStruct((tokens, features), jnp.bfloat16),
        name="tile_attention_forward",
    )(mask, queries, window, window)


def attention_backward(mask, queries, window, attended, grad_attended):
    tokens, features = queries.shape
    tiles = window.shape[0]
    heads = features // HD
    chunk = BACKWARD_CHUNK
    chunks = tokens // chunk
    scale = HD ** (-0.5)
    return pl.pallas_call(
        functools.partial(backward_kernel, scale),
        grid=(heads, chunks),
        in_specs=[
            pl.BlockSpec((1, tiles * tokens), lambda h, c: (0, 0)),
            pl.BlockSpec((chunk, HD), lambda h, c: (c, h)),
            pl.BlockSpec((tiles, tokens, HD), lambda h, c: (0, 0, h)),
            pl.BlockSpec((tiles, tokens, HD), lambda h, c: (0, 1, h)),
            pl.BlockSpec((chunk, HD), lambda h, c: (c, h)),
            pl.BlockSpec((chunk, HD), lambda h, c: (c, h)),
        ],
        out_specs=[
            pl.BlockSpec((chunk, HD), lambda h, c: (c, h)),
            pl.BlockSpec((tiles, 2 * tokens, HD), lambda h, c: (0, 0, h)),
            pl.BlockSpec((tiles // 3, 2 * tokens, HD), lambda h, c: (0, 0, h)),
        ],
        out_shape=[
            jax.ShapeDtypeStruct((tokens, features), jnp.bfloat16),
            jax.ShapeDtypeStruct((tiles, 2 * tokens, features), jnp.bfloat16),
            jax.ShapeDtypeStruct((tiles // 3, 2 * tokens, features), jnp.float32),
        ],
        scratch_shapes=[pltpu.VMEM((tiles, 2 * tokens, HD), jnp.float32)],
        name="tile_attention_backward",
    )(mask, queries, window, window, attended, grad_attended)


def gather_over(piece, axis):
    count = lax.axis_size(axis)
    me = lax.axis_index(axis)
    received = [piece] + [cyclic(piece, axis, steps) for steps in range(1, count)]
    ordered = jnp.stack([received[(-k) % count] for k in range(count)])
    return jnp.roll(ordered, me, axis=0)


def scatter_sum(full, axis, dim):
    count = lax.axis_size(axis)
    me = lax.axis_index(axis)
    size = full.shape[dim] // count

    def part(index):
        return lax.dynamic_slice_in_dim(full, index * size, size, axis=dim)

    total = part(me).astype(jnp.float32)
    for steps in range(1, count):
        sent = part((me + steps) % count).astype(jnp.bfloat16)
        total = total + cyclic(sent, axis, steps).astype(jnp.float32)
    return total


def body(queries, key_states, value_states, valid_mask, out_weight, out_cotangent):
    tile_rows, tile_columns, tokens, features = queries.shape
    assert tile_rows == 1 and tile_columns == 1
    model_width = out_weight.shape[1]
    q = queries[0, 0]
    flag_rows = jnp.zeros((FLAG_ROWS, features), jnp.bfloat16)
    flag_rows = flag_rows.at[0, :tokens].set(valid_mask[0, 0].astype(jnp.bfloat16))
    packed = jnp.concatenate([key_states[0, 0], value_states[0, 0], flag_rows], axis=0)

    with jax.named_scope("halo_exchange"):
        column = jnp.stack([shifted(packed, "fh", 1), packed, shifted(packed, "fh", -1)])
        window = jnp.concatenate(
            [shifted(column, "wa", 1), column, shifted(column, "wa", -1)], axis=0
        )
    tiles = window.shape[0]
    flags = window[:, 2 * tokens, :tokens].reshape(1, tiles * tokens)
    mask = jnp.where(flags > 0, 0.0, MASKED).astype(jnp.float32)

    with jax.named_scope("cotangent_gather"):
        cot_all = lax.all_gather(out_cotangent[0, 0], "ha", axis=0, tiled=True)

    with jax.named_scope("attention_forward"):
        attended = attention_forward(mask, q, window)

    with jax.named_scope("output_projection"):
        projected = jnp.dot(attended, out_weight, preferred_element_type=jnp.float32)
        layer_out = lax.psum_scatter(
            projected.astype(jnp.bfloat16), "ha", scatter_dimension=0, tiled=True
        )

    with jax.named_scope("grad_attended"):
        grad_attended = lax.dot_general(
            cot_all, out_weight, (((1,), (1,)), ((), ())), preferred_element_type=jnp.float32
        ).astype(jnp.bfloat16)

    with jax.named_scope("attention_backward"):
        grad_q, sides, partials = attention_backward(mask, q, window, attended, grad_attended)

    with jax.named_scope("grad_weight"):
        weight_part = lax.dot_general(
            cot_all, attended, (((0,), (0,)), ((), ())), preferred_element_type=jnp.float32
        )
        grad_weight = scatter_sum(scatter_sum(weight_part, "fh", 0), "wa", 0)

    with jax.named_scope("halo_reduction"):
        middle = (
            partials
            + shifted(sides[0:3], "wa", -1).astype(jnp.float32)
            + shifted(sides[6:9], "wa", 1).astype(jnp.float32)
        )
        middle_sides = middle.astype(jnp.bfloat16)
        own = (
            middle[1]
            + shifted(middle_sides[0], "fh", -1).astype(jnp.float32)
            + shifted(middle_sides[2], "fh", 1).astype(jnp.float32)
        )
    grad_keys = own[:tokens].astype(jnp.bfloat16)
    grad_values = own[tokens:].astype(jnp.bfloat16)
    expand = lambda x: x[None, None]
    return (
        expand(layer_out),
        expand(grad_q),
        expand(grad_keys),
        expand(grad_values),
        grad_weight,
    )


def solution(mesh):
    return jax.shard_map(
        body,
        mesh=mesh,
        in_specs=(
            P("fh", "wa", None, "ha"),
            P("fh", "wa", None, "ha"),
            P("fh", "wa", None, "ha"),
            P("fh", "wa", None),
            P("ha", None),
            P("fh", "wa", "ha", None),
        ),
        out_specs=(
            P("fh", "wa", "ha", None),
            P("fh", "wa", None, "ha"),
            P("fh", "wa", None, "ha"),
            P("fh", "wa", None, "ha"),
            P(("fh", "wa"), "ha"),
        ),
        check_vma=False,
    )
```

```python
import functools

import jax
import jax.numpy as jnp
from jax import lax
from jax.experimental import pallas as pl
from jax.experimental.pallas import tpu as pltpu
from jax.sharding import PartitionSpec as P

HD = 128
MASKED = -1e30
FORWARD_CHUNK = 384
BACKWARD_CHUNK = 192
FLAG_ROWS = 16


def shift_pairs(count, steps):
    return [(source, source + steps) for source in range(count) if 0 <= source + steps < count]


def shifted(value, axis, steps):
    return lax.ppermute(value, axis, shift_pairs(lax.axis_size(axis), steps))


def cyclic(value, axis, steps):
    count = lax.axis_size(axis)
    return lax.ppermute(value, axis, [(i, (i + steps) % count) for i in range(count)])


def scores_of(mask_ref, q_ref, k_ref, scale):
    q = q_ref[...]
    k = k_ref[...].reshape(-1, HD)
    s = lax.dot_general(q, k, (((1,), (1,)), ((), ())), preferred_element_type=jnp.float32)
    return s * scale + mask_ref[...]


def forward_kernel(scale, mask_ref, q_ref, k_ref, v_ref, o_ref):
    s = scores_of(mask_ref, q_ref, k_ref, scale)
    m = jnp.max(s, axis=1, keepdims=True)
    e = jnp.exp(s - m)
    total = jnp.sum(e, axis=1, keepdims=True)
    p = (e * (1.0 / total)).astype(jnp.bfloat16)
    v = v_ref[...].reshape(-1, HD)
    o_ref[...] = jnp.dot(p, v, preferred_element_type=jnp.float32).astype(o_ref.dtype)


def backward_kernel(
    scale, mask_ref, q_ref, k_ref, v_ref, o_ref, do_ref, dq_ref, left_ref, mid_ref, right_ref, acc_ref
):
    chunk = pl.program_id(1)
    s = scores_of(mask_ref, q_ref, k_ref, scale)
    m = jnp.max(s, axis=1, keepdims=True)
    e = jnp.exp(s - m)
    total = jnp.sum(e, axis=1, keepdims=True)
    w = e * (1.0 / total)
    p = w.astype(jnp.bfloat16)
    do = do_ref[...]
    row_dot = jnp.sum(
        do.astype(jnp.float32) * o_ref[...].astype(jnp.float32), axis=1, keepdims=True
    )
    k = k_ref[...].reshape(-1, HD)
    v = v_ref[...].reshape(-1, HD)
    dp = lax.dot_general(do, v, (((1,), (1,)), ((), ())), preferred_element_type=jnp.float32)
    ds = (w * (dp - row_dot)).astype(jnp.bfloat16)
    dq = jnp.dot(ds, k, preferred_element_type=jnp.float32) * scale
    dq_ref[...] = dq.astype(dq_ref.dtype)
    contract0 = (((0,), (0,)), ((), ()))
    dk = lax.dot_general(ds, q_ref[...], contract0, preferred_element_type=jnp.float32) * scale
    dv = lax.dot_general(p, do, contract0, preferred_element_type=jnp.float32)
    tiles, tokens = k_ref.shape[0], k_ref.shape[1]
    dk = dk.reshape(tiles, tokens, HD)
    dv = dv.reshape(tiles, tokens, HD)

    @pl.when(chunk == 0)
    def _():
        acc_ref[:, :tokens, :] = dk
        acc_ref[:, tokens:, :] = dv

    @pl.when(chunk > 0)
    def _():
        acc_ref[:, :tokens, :] += dk
        acc_ref[:, tokens:, :] += dv

    @pl.when(chunk == pl.num_programs(1) - 1)
    def _():
        third = tiles // 3
        left_ref[...] = acc_ref[:third].astype(left_ref.dtype)
        mid_ref[...] = acc_ref[third : 2 * third]
        right_ref[...] = acc_ref[2 * third :].astype(right_ref.dtype)


def attention_forward(mask, queries, window):
    tokens, features = queries.shape
    tiles = window.shape[0]
    heads = features // HD
    chunk = FORWARD_CHUNK
    chunks = tokens // chunk
    scale = HD ** (-0.5)
    return pl.pallas_call(
        functools.partial(forward_kernel, scale),
        grid=(heads, chunks),
        in_specs=[
            pl.BlockSpec((1, tiles * tokens), lambda h, c: (0, 0)),
            pl.BlockSpec((chunk, HD), lambda h, c: (c, h)),
            pl.BlockSpec((tiles, tokens, HD), lambda h, c: (0, 0, h)),
            pl.BlockSpec((tiles, tokens, HD), lambda h, c: (0, 1, h)),
        ],
        out_specs=pl.BlockSpec((chunk, HD), lambda h, c: (c, h)),
        out_shape=jax.ShapeDtypeStruct((tokens, features), jnp.bfloat16),
        name="tile_attention_forward",
    )(mask, queries, window, window)


def attention_backward(mask, queries, window, attended, grad_attended):
    tokens, features = queries.shape
    tiles = window.shape[0]
    heads = features // HD
    chunk = BACKWARD_CHUNK
    chunks = tokens // chunk
    scale = HD ** (-0.5)
    return pl.pallas_call(
        functools.partial(backward_kernel, scale),
        grid=(heads, chunks),
        in_specs=[
            pl.BlockSpec((1, tiles * tokens), lambda h, c: (0, 0)),
            pl.BlockSpec((chunk, HD), lambda h, c: (c, h)),
            pl.BlockSpec((tiles, tokens, HD), lambda h, c: (0, 0, h)),
            pl.BlockSpec((tiles, tokens, HD), lambda h, c: (0, 1, h)),
            pl.BlockSpec((chunk, HD), lambda h, c: (c, h)),
            pl.BlockSpec((chunk, HD), lambda h, c: (c, h)),
        ],
        out_specs=[
            pl.BlockSpec((chunk, HD), lambda h, c: (c, h)),
            pl.BlockSpec((tiles // 3, 2 * tokens, HD), lambda h, c: (0, 0, h)),
            pl.BlockSpec((tiles // 3, 2 * tokens, HD), lambda h, c: (0, 0, h)),
            pl.BlockSpec((tiles // 3, 2 * tokens, HD), lambda h, c: (0, 0, h)),
        ],
        out_shape=[
            jax.ShapeDtypeStruct((tokens, features), jnp.bfloat16),
            jax.ShapeDtypeStruct((tiles // 3, 2 * tokens, features), jnp.bfloat16),
            jax.ShapeDtypeStruct((tiles // 3, 2 * tokens, features), jnp.float32),
            jax.ShapeDtypeStruct((tiles // 3, 2 * tokens, features), jnp.bfloat16),
        ],
        scratch_shapes=[pltpu.VMEM((tiles, 2 * tokens, HD), jnp.float32)],
        name="tile_attention_backward",
    )(mask, queries, window, window, attended, grad_attended)


def gather_over(piece, axis):
    count = lax.axis_size(axis)
    me = lax.axis_index(axis)
    received = [piece] + [cyclic(piece, axis, steps) for steps in range(1, count)]
    ordered = jnp.stack([received[(-k) % count] for k in range(count)])
    return jnp.roll(ordered, me, axis=0)


def scatter_parts(full, axis, dim):
    count = lax.axis_size(axis)
    me = lax.axis_index(axis)
    size = full.shape[dim] // count

    def part(index):
        return lax.dynamic_slice_in_dim(full, index * size, size, axis=dim)

    sent = [part((me + steps) % count).astype(jnp.bfloat16) for steps in range(1, count)]
    return part(me).astype(jnp.float32), sent


def scatter_finish(own, sent, axis):
    total = own
    for steps, piece in enumerate(sent, start=1):
        total = total + cyclic(piece, axis, steps).astype(jnp.float32)
    return total


def scatter_sum(full, axis, dim):
    count = lax.axis_size(axis)
    me = lax.axis_index(axis)
    size = full.shape[dim] // count

    def part(index):
        return lax.dynamic_slice_in_dim(full, index * size, size, axis=dim)

    total = part(me).astype(jnp.float32)
    for steps in range(1, count):
        sent = part((me + steps) % count).astype(jnp.bfloat16)
        total = total + cyclic(sent, axis, steps).astype(jnp.float32)
    return total


def body(queries, key_states, value_states, valid_mask, out_weight, out_cotangent):
    tile_rows, tile_columns, tokens, features = queries.shape
    assert tile_rows == 1 and tile_columns == 1
    model_width = out_weight.shape[1]
    q = queries[0, 0]
    flag_rows = jnp.zeros((FLAG_ROWS, features), jnp.bfloat16)
    flag_rows = flag_rows.at[0, :tokens].set(valid_mask[0, 0].astype(jnp.bfloat16))
    packed = jnp.concatenate([key_states[0, 0], value_states[0, 0], flag_rows], axis=0)

    with jax.named_scope("halo_exchange"):
        column = jnp.stack([shifted(packed, "fh", 1), packed, shifted(packed, "fh", -1)])
        window = jnp.concatenate(
            [shifted(column, "wa", 1), column, shifted(column, "wa", -1)], axis=0
        )
    tiles = window.shape[0]
    flags = window[:, 2 * tokens, :tokens].reshape(1, tiles * tokens)
    mask = jnp.where(flags > 0, 0.0, MASKED).astype(jnp.float32)

    with jax.named_scope("cotangent_gather"):
        cot_all = lax.all_gather(out_cotangent[0, 0], "ha", axis=0, tiled=True)

    with jax.named_scope("attention_forward"):
        attended = attention_forward(mask, q, window)

    with jax.named_scope("output_projection"):
        projected = jnp.dot(attended, out_weight, preferred_element_type=jnp.float32)
        layer_out = lax.psum_scatter(
            projected.astype(jnp.bfloat16), "ha", scatter_dimension=0, tiled=True
        )

    with jax.named_scope("grad_attended"):
        grad_attended = lax.dot_general(
            cot_all, out_weight, (((1,), (1,)), ((), ())), preferred_element_type=jnp.float32
        ).astype(jnp.bfloat16)

    with jax.named_scope("grad_weight"):
        weight_part = lax.dot_general(
            cot_all, attended, (((0,), (0,)), ((), ())), preferred_element_type=jnp.float32
        )
        weight_own, weight_sent = scatter_parts(weight_part, "fh", 0)
        weight_own, weight_sent, grad_attended = lax.optimization_barrier(
            (weight_own, weight_sent, grad_attended)
        )
        weight_rows = scatter_finish(weight_own, weight_sent, "fh")

    with jax.named_scope("attention_backward"):
        grad_q, left, partials, right = attention_backward(
            mask, q, window, attended, grad_attended
        )

    with jax.named_scope("grad_weight"):
        grad_weight = scatter_sum(weight_rows, "wa", 0)

    with jax.named_scope("halo_reduction"):
        middle = (
            partials
            + shifted(left, "wa", -1).astype(jnp.float32)
            + shifted(right, "wa", 1).astype(jnp.float32)
        )
        middle_sides = middle.astype(jnp.bfloat16)
        own = (
            middle[1]
            + shifted(middle_sides[0], "fh", -1).astype(jnp.float32)
            + shifted(middle_sides[2], "fh", 1).astype(jnp.float32)
        )
    grad_keys = own[:tokens].astype(jnp.bfloat16)
    grad_values = own[tokens:].astype(jnp.bfloat16)
    expand = lambda x: x[None, None]
    return (
        expand(layer_out),
        expand(grad_q),
        expand(grad_keys),
        expand(grad_values),
        grad_weight,
    )


def solution(mesh):
    return jax.shard_map(
        body,
        mesh=mesh,
        in_specs=(
            P("fh", "wa", None, "ha"),
            P("fh", "wa", None, "ha"),
            P("fh", "wa", None, "ha"),
            P("fh", "wa", None),
            P("ha", None),
            P("fh", "wa", "ha", None),
        ),
        out_specs=(
            P("fh", "wa", "ha", None),
            P("fh", "wa", None, "ha"),
            P("fh", "wa", None, "ha"),
            P("fh", "wa", None, "ha"),
            P(("fh", "wa"), "ha"),
        ),
        check_vma=False,
    )
```

```python
import functools

import jax
import jax.numpy as jnp
from jax import lax
from jax.experimental import pallas as pl
from jax.experimental.pallas import tpu as pltpu
from jax.sharding import PartitionSpec as P

HD = 128
MASKED = -1e30
FORWARD_CHUNK = 384
BACKWARD_CHUNK = 192
FLAG_ROWS = 16


def shift_pairs(count, steps):
    return [(source, source + steps) for source in range(count) if 0 <= source + steps < count]


def shifted(value, axis, steps):
    return lax.ppermute(value, axis, shift_pairs(lax.axis_size(axis), steps))


def cyclic(value, axis, steps):
    count = lax.axis_size(axis)
    return lax.ppermute(value, axis, [(i, (i + steps) % count) for i in range(count)])


def scores_of(mask_ref, q_ref, k_ref, scale):
    q = q_ref[...]
    k = k_ref[...].reshape(-1, HD)
    s = lax.dot_general(q, k, (((1,), (1,)), ((), ())), preferred_element_type=jnp.float32)
    return s * scale + mask_ref[...]


def forward_kernel(scale, mask_ref, q_ref, k_ref, v_ref, o_ref):
    s = scores_of(mask_ref, q_ref, k_ref, scale)
    m = jnp.max(s, axis=1, keepdims=True)
    e = jnp.exp(s - m)
    total = jnp.sum(e, axis=1, keepdims=True)
    p = (e * (1.0 / total)).astype(jnp.bfloat16)
    v = v_ref[...].reshape(-1, HD)
    o_ref[...] = jnp.dot(p, v, preferred_element_type=jnp.float32).astype(o_ref.dtype)


def backward_kernel(
    scale, mask_ref, q_ref, k_ref, v_ref, o_ref, do_ref, dq_ref, left_ref, mid_ref, right_ref, acc_ref
):
    chunk = pl.program_id(1)
    s = scores_of(mask_ref, q_ref, k_ref, scale)
    m = jnp.max(s, axis=1, keepdims=True)
    e = jnp.exp(s - m)
    total = jnp.sum(e, axis=1, keepdims=True)
    w = e * (1.0 / total)
    p = w.astype(jnp.bfloat16)
    do = do_ref[...]
    row_dot = jnp.sum(
        do.astype(jnp.float32) * o_ref[...].astype(jnp.float32), axis=1, keepdims=True
    )
    k = k_ref[...].reshape(-1, HD)
    v = v_ref[...].reshape(-1, HD)
    dp = lax.dot_general(do, v, (((1,), (1,)), ((), ())), preferred_element_type=jnp.float32)
    ds = (w * (dp - row_dot)).astype(jnp.bfloat16)
    dq = jnp.dot(ds, k, preferred_element_type=jnp.float32) * scale
    dq_ref[...] = dq.astype(dq_ref.dtype)
    contract0 = (((0,), (0,)), ((), ()))
    dk = lax.dot_general(ds, q_ref[...], contract0, preferred_element_type=jnp.float32) * scale
    dv = lax.dot_general(p, do, contract0, preferred_element_type=jnp.float32)
    tiles, tokens = k_ref.shape[0], k_ref.shape[1]
    dk = dk.reshape(tiles, tokens, HD)
    dv = dv.reshape(tiles, tokens, HD)

    @pl.when(chunk == 0)
    def _():
        acc_ref[:, :tokens, :] = dk
        acc_ref[:, tokens:, :] = dv

    @pl.when(chunk > 0)
    def _():
        acc_ref[:, :tokens, :] += dk
        acc_ref[:, tokens:, :] += dv

    @pl.when(chunk == pl.num_programs(1) - 1)
    def _():
        third = tiles // 3
        left_ref[...] = acc_ref[:third].astype(left_ref.dtype)
        mid_ref[...] = acc_ref[third : 2 * third]
        right_ref[...] = acc_ref[2 * third :].astype(right_ref.dtype)


def attention_forward(mask, queries, window):
    tokens, features = queries.shape
    tiles = window.shape[0]
    heads = features // HD
    chunk = FORWARD_CHUNK
    chunks = tokens // chunk
    scale = HD ** (-0.5)
    return pl.pallas_call(
        functools.partial(forward_kernel, scale),
        grid=(heads, chunks),
        in_specs=[
            pl.BlockSpec((1, tiles * tokens), lambda h, c: (0, 0)),
            pl.BlockSpec((chunk, HD), lambda h, c: (c, h)),
            pl.BlockSpec((tiles, tokens, HD), lambda h, c: (0, 0, h)),
            pl.BlockSpec((tiles, tokens, HD), lambda h, c: (0, 1, h)),
        ],
        out_specs=pl.BlockSpec((chunk, HD), lambda h, c: (c, h)),
        out_shape=jax.ShapeDtypeStruct((tokens, features), jnp.bfloat16),
        name="tile_attention_forward",
    )(mask, queries, window, window)


def attention_backward(mask, queries, window, attended, grad_attended):
    tokens, features = queries.shape
    tiles = window.shape[0]
    heads = features // HD
    chunk = BACKWARD_CHUNK
    chunks = tokens // chunk
    scale = HD ** (-0.5)
    return pl.pallas_call(
        functools.partial(backward_kernel, scale),
        grid=(heads, chunks),
        in_specs=[
            pl.BlockSpec((1, tiles * tokens), lambda h, c: (0, 0)),
            pl.BlockSpec((chunk, HD), lambda h, c: (c, h)),
            pl.BlockSpec((tiles, tokens, HD), lambda h, c: (0, 0, h)),
            pl.BlockSpec((tiles, tokens, HD), lambda h, c: (0, 1, h)),
            pl.BlockSpec((chunk, HD), lambda h, c: (c, h)),
            pl.BlockSpec((chunk, HD), lambda h, c: (c, h)),
        ],
        out_specs=[
            pl.BlockSpec((chunk, HD), lambda h, c: (c, h)),
            pl.BlockSpec((tiles // 3, 2 * tokens, HD), lambda h, c: (0, 0, h)),
            pl.BlockSpec((tiles // 3, 2 * tokens, HD), lambda h, c: (0, 0, h)),
            pl.BlockSpec((tiles // 3, 2 * tokens, HD), lambda h, c: (0, 0, h)),
        ],
        out_shape=[
            jax.ShapeDtypeStruct((tokens, features), jnp.bfloat16),
            jax.ShapeDtypeStruct((tiles // 3, 2 * tokens, features), jnp.bfloat16),
            jax.ShapeDtypeStruct((tiles // 3, 2 * tokens, features), jnp.float32),
            jax.ShapeDtypeStruct((tiles // 3, 2 * tokens, features), jnp.bfloat16),
        ],
        scratch_shapes=[pltpu.VMEM((tiles, 2 * tokens, HD), jnp.float32)],
        name="tile_attention_backward",
    )(mask, queries, window, window, attended, grad_attended)


def gather_over(piece, axis):
    count = lax.axis_size(axis)
    me = lax.axis_index(axis)
    received = [piece] + [cyclic(piece, axis, steps) for steps in range(1, count)]
    ordered = jnp.stack([received[(-k) % count] for k in range(count)])
    return jnp.roll(ordered, me, axis=0)


def scatter_parts(full, axis, dim):
    count = lax.axis_size(axis)
    me = lax.axis_index(axis)
    size = full.shape[dim] // count

    def part(index):
        return lax.dynamic_slice_in_dim(full, index * size, size, axis=dim)

    sent = [part((me + steps) % count).astype(jnp.bfloat16) for steps in range(1, count)]
    return part(me).astype(jnp.float32), sent


def scatter_finish(own, sent, axis):
    total = own
    for steps, piece in enumerate(sent, start=1):
        total = total + cyclic(piece, axis, steps).astype(jnp.float32)
    return total


def scatter_sum(full, axis, dim):
    count = lax.axis_size(axis)
    me = lax.axis_index(axis)
    size = full.shape[dim] // count

    def part(index):
        return lax.dynamic_slice_in_dim(full, index * size, size, axis=dim)

    total = part(me).astype(jnp.float32)
    for steps in range(1, count):
        sent = part((me + steps) % count).astype(jnp.bfloat16)
        total = total + cyclic(sent, axis, steps).astype(jnp.float32)
    return total


def body(queries, key_states, value_states, valid_mask, out_weight, out_cotangent):
    tile_rows, tile_columns, tokens, features = queries.shape
    assert tile_rows == 1 and tile_columns == 1
    model_width = out_weight.shape[1]
    q = queries[0, 0]
    flag_rows = jnp.zeros((FLAG_ROWS, features), jnp.bfloat16)
    flag_rows = flag_rows.at[0, :tokens].set(valid_mask[0, 0].astype(jnp.bfloat16))
    packed = jnp.concatenate([key_states[0, 0], value_states[0, 0], flag_rows], axis=0)

    with jax.named_scope("halo_exchange"):
        column = jnp.stack([shifted(packed, "fh", 1), packed, shifted(packed, "fh", -1)])
        window = jnp.concatenate(
            [shifted(column, "wa", 1), column, shifted(column, "wa", -1)], axis=0
        )
    tiles = window.shape[0]
    flags = window[:, 2 * tokens, :tokens].reshape(1, tiles * tokens)
    mask = jnp.where(flags > 0, 0.0, MASKED).astype(jnp.float32)

    with jax.named_scope("cotangent_gather"):
        cot_all = lax.all_gather(out_cotangent[0, 0], "ha", axis=0, tiled=True)

    with jax.named_scope("attention_forward"):
        attended = attention_forward(mask, q, window)

    with jax.named_scope("output_projection"):
        projected = jnp.dot(attended, out_weight, preferred_element_type=jnp.float32)
        layer_out = lax.psum_scatter(
            projected.astype(jnp.bfloat16), "ha", scatter_dimension=0, tiled=True
        )

    with jax.named_scope("grad_attended"):
        grad_attended = lax.dot_general(
            cot_all, out_weight, (((1,), (1,)), ((), ())), preferred_element_type=jnp.float32
        ).astype(jnp.bfloat16)

    with jax.named_scope("grad_weight"):
        weight_part = lax.dot_general(
            cot_all, attended, (((0,), (0,)), ((), ())), preferred_element_type=jnp.float32
        )
        row_blocks = weight_part.reshape(
            lax.axis_size("fh"), lax.axis_size("wa"), -1, weight_part.shape[1]
        )
        weight_own, weight_sent = scatter_parts(row_blocks, "wa", 1)
        weight_own, weight_sent, grad_attended = lax.optimization_barrier(
            (weight_own, weight_sent, grad_attended)
        )
        weight_rows = scatter_finish(weight_own, weight_sent, "wa")

    with jax.named_scope("attention_backward"):
        grad_q, left, partials, right = attention_backward(
            mask, q, window, attended, grad_attended
        )

    with jax.named_scope("grad_weight"):
        grad_weight = scatter_sum(weight_rows, "fh", 0).reshape(-1, weight_part.shape[1])

    with jax.named_scope("halo_reduction"):
        middle = (
            partials
            + shifted(left, "wa", -1).astype(jnp.float32)
            + shifted(right, "wa", 1).astype(jnp.float32)
        )
        middle_sides = middle.astype(jnp.bfloat16)
        own = (
            middle[1]
            + shifted(middle_sides[0], "fh", -1).astype(jnp.float32)
            + shifted(middle_sides[2], "fh", 1).astype(jnp.float32)
        )
    grad_keys = own[:tokens].astype(jnp.bfloat16)
    grad_values = own[tokens:].astype(jnp.bfloat16)
    expand = lambda x: x[None, None]
    return (
        expand(layer_out),
        expand(grad_q),
        expand(grad_keys),
        expand(grad_values),
        grad_weight,
    )


def solution(mesh):
    return jax.shard_map(
        body,
        mesh=mesh,
        in_specs=(
            P("fh", "wa", None, "ha"),
            P("fh", "wa", None, "ha"),
            P("fh", "wa", None, "ha"),
            P("fh", "wa", None),
            P("ha", None),
            P("fh", "wa", "ha", None),
        ),
        out_specs=(
            P("fh", "wa", "ha", None),
            P("fh", "wa", None, "ha"),
            P("fh", "wa", None, "ha"),
            P("fh", "wa", None, "ha"),
            P(("fh", "wa"), "ha"),
        ),
        check_vma=False,
    )
```

```python
import functools

import jax
import jax.numpy as jnp
from jax import lax
from jax.experimental import pallas as pl
from jax.experimental.pallas import tpu as pltpu
from jax.sharding import PartitionSpec as P

HD = 128
MASKED = -1e30
FORWARD_CHUNK = 384
BACKWARD_CHUNK = 192
FLAG_ROWS = 16


def shift_pairs(count, steps):
    return [(source, source + steps) for source in range(count) if 0 <= source + steps < count]


def shifted(value, axis, steps):
    return lax.ppermute(value, axis, shift_pairs(lax.axis_size(axis), steps))


def cyclic(value, axis, steps):
    count = lax.axis_size(axis)
    return lax.ppermute(value, axis, [(i, (i + steps) % count) for i in range(count)])


def scores_of(mask_ref, q_ref, k_ref, scale):
    q = q_ref[...]
    k = k_ref[...].reshape(-1, HD)
    s = lax.dot_general(q, k, (((1,), (1,)), ((), ())), preferred_element_type=jnp.float32)
    return s * scale + mask_ref[...]


def forward_kernel(scale, mask_ref, q_ref, k_ref, v_ref, o_ref):
    s = scores_of(mask_ref, q_ref, k_ref, scale)
    m = jnp.max(s, axis=1, keepdims=True)
    e = jnp.exp(s - m)
    total = jnp.sum(e, axis=1, keepdims=True)
    p = (e * (1.0 / total)).astype(jnp.bfloat16)
    v = v_ref[...].reshape(-1, HD)
    o_ref[...] = jnp.dot(p, v, preferred_element_type=jnp.float32).astype(o_ref.dtype)


def backward_kernel(
    scale, mask_ref, q_ref, k_ref, v_ref, o_ref, do_ref, dq_ref, left_ref, mid_ref, right_ref, acc_ref
):
    chunk = pl.program_id(1)
    s = scores_of(mask_ref, q_ref, k_ref, scale)
    m = jnp.max(s, axis=1, keepdims=True)
    e = jnp.exp(s - m)
    total = jnp.sum(e, axis=1, keepdims=True)
    w = e * (1.0 / total)
    p = w.astype(jnp.bfloat16)
    do = do_ref[...]
    row_dot = jnp.sum(
        do.astype(jnp.float32) * o_ref[...].astype(jnp.float32), axis=1, keepdims=True
    )
    k = k_ref[...].reshape(-1, HD)
    v = v_ref[...].reshape(-1, HD)
    dp = lax.dot_general(do, v, (((1,), (1,)), ((), ())), preferred_element_type=jnp.float32)
    ds = (w * (dp - row_dot)).astype(jnp.bfloat16)
    dq = jnp.dot(ds, k, preferred_element_type=jnp.float32) * scale
    dq_ref[...] = dq.astype(dq_ref.dtype)
    contract0 = (((0,), (0,)), ((), ()))
    dk = lax.dot_general(ds, q_ref[...], contract0, preferred_element_type=jnp.float32) * scale
    dv = lax.dot_general(p, do, contract0, preferred_element_type=jnp.float32)
    tiles, tokens = k_ref.shape[0], k_ref.shape[1]
    dk = dk.reshape(tiles, tokens, HD)
    dv = dv.reshape(tiles, tokens, HD)

    @pl.when(chunk == 0)
    def _():
        acc_ref[:, :tokens, :] = dk
        acc_ref[:, tokens:, :] = dv

    @pl.when(chunk > 0)
    def _():
        acc_ref[:, :tokens, :] += dk
        acc_ref[:, tokens:, :] += dv

    @pl.when(chunk == pl.num_programs(1) - 1)
    def _():
        third = tiles // 3
        left_ref[...] = acc_ref[:third].astype(left_ref.dtype)
        mid_ref[...] = acc_ref[third : 2 * third]
        right_ref[...] = acc_ref[2 * third :].astype(right_ref.dtype)


def attention_forward(mask, queries, window):
    tokens, features = queries.shape
    tiles = window.shape[0]
    heads = features // HD
    chunk = FORWARD_CHUNK
    chunks = tokens // chunk
    scale = HD ** (-0.5)
    return pl.pallas_call(
        functools.partial(forward_kernel, scale),
        grid=(heads, chunks),
        in_specs=[
            pl.BlockSpec((1, tiles * tokens), lambda h, c: (0, 0)),
            pl.BlockSpec((chunk, HD), lambda h, c: (c, h)),
            pl.BlockSpec((tiles, tokens, HD), lambda h, c: (0, 0, h)),
            pl.BlockSpec((tiles, tokens, HD), lambda h, c: (0, 1, h)),
        ],
        out_specs=pl.BlockSpec((chunk, HD), lambda h, c: (c, h)),
        out_shape=jax.ShapeDtypeStruct((tokens, features), jnp.bfloat16),
        name="tile_attention_forward",
    )(mask, queries, window, window)


def attention_backward(mask, queries, window, attended, grad_attended, head):
    tokens, features = queries.shape
    tiles = window.shape[0]
    chunk = BACKWARD_CHUNK
    chunks = tokens // chunk
    scale = HD ** (-0.5)
    third = tiles // 3
    return pl.pallas_call(
        functools.partial(backward_kernel, scale),
        grid=(1, chunks),
        in_specs=[
            pl.BlockSpec((1, tiles * tokens), lambda h, c: (0, 0)),
            pl.BlockSpec((chunk, HD), lambda h, c: (c, head)),
            pl.BlockSpec((tiles, tokens, HD), lambda h, c: (0, 0, head)),
            pl.BlockSpec((tiles, tokens, HD), lambda h, c: (0, 1, head)),
            pl.BlockSpec((chunk, HD), lambda h, c: (c, head)),
            pl.BlockSpec((chunk, HD), lambda h, c: (c, head)),
        ],
        out_specs=[
            pl.BlockSpec((chunk, HD), lambda h, c: (c, 0)),
            pl.BlockSpec((third, 2 * tokens, HD), lambda h, c: (0, 0, 0)),
            pl.BlockSpec((third, 2 * tokens, HD), lambda h, c: (0, 0, 0)),
            pl.BlockSpec((third, 2 * tokens, HD), lambda h, c: (0, 0, 0)),
        ],
        out_shape=[
            jax.ShapeDtypeStruct((tokens, HD), jnp.bfloat16),
            jax.ShapeDtypeStruct((third, 2 * tokens, HD), jnp.bfloat16),
            jax.ShapeDtypeStruct((third, 2 * tokens, HD), jnp.float32),
            jax.ShapeDtypeStruct((third, 2 * tokens, HD), jnp.bfloat16),
        ],
        scratch_shapes=[pltpu.VMEM((tiles, 2 * tokens, HD), jnp.float32)],
        name="tile_attention_backward",
    )(mask, queries, window, window, attended, grad_attended)


def return_halo(left, partials, right):
    middle = (
        partials
        + shifted(left, "wa", -1).astype(jnp.float32)
        + shifted(right, "wa", 1).astype(jnp.float32)
    )
    middle_sides = middle.astype(jnp.bfloat16)
    return (
        middle[1]
        + shifted(middle_sides[0], "fh", -1).astype(jnp.float32)
        + shifted(middle_sides[2], "fh", 1).astype(jnp.float32)
    )


def gather_over(piece, axis):
    count = lax.axis_size(axis)
    me = lax.axis_index(axis)
    received = [piece] + [cyclic(piece, axis, steps) for steps in range(1, count)]
    ordered = jnp.stack([received[(-k) % count] for k in range(count)])
    return jnp.roll(ordered, me, axis=0)


def scatter_parts(full, axis, dim):
    count = lax.axis_size(axis)
    me = lax.axis_index(axis)
    size = full.shape[dim] // count

    def part(index):
        return lax.dynamic_slice_in_dim(full, index * size, size, axis=dim)

    sent = [part((me + steps) % count).astype(jnp.bfloat16) for steps in range(1, count)]
    return part(me).astype(jnp.float32), sent


def scatter_finish(own, sent, axis):
    total = own
    for steps, piece in enumerate(sent, start=1):
        total = total + cyclic(piece, axis, steps).astype(jnp.float32)
    return total


def scatter_sum(full, axis, dim):
    count = lax.axis_size(axis)
    me = lax.axis_index(axis)
    size = full.shape[dim] // count

    def part(index):
        return lax.dynamic_slice_in_dim(full, index * size, size, axis=dim)

    total = part(me).astype(jnp.float32)
    for steps in range(1, count):
        sent = part((me + steps) % count).astype(jnp.bfloat16)
        total = total + cyclic(sent, axis, steps).astype(jnp.float32)
    return total


def body(queries, key_states, value_states, valid_mask, out_weight, out_cotangent):
    tile_rows, tile_columns, tokens, features = queries.shape
    assert tile_rows == 1 and tile_columns == 1
    model_width = out_weight.shape[1]
    q = queries[0, 0]
    flag_rows = jnp.zeros((FLAG_ROWS, features), jnp.bfloat16)
    flag_rows = flag_rows.at[0, :tokens].set(valid_mask[0, 0].astype(jnp.bfloat16))
    packed = jnp.concatenate([key_states[0, 0], value_states[0, 0], flag_rows], axis=0)

    with jax.named_scope("halo_exchange"):
        column = jnp.stack([shifted(packed, "fh", 1), packed, shifted(packed, "fh", -1)])
        window = jnp.concatenate(
            [shifted(column, "wa", 1), column, shifted(column, "wa", -1)], axis=0
        )
    tiles = window.shape[0]
    flags = window[:, 2 * tokens, :tokens].reshape(1, tiles * tokens)
    mask = jnp.where(flags > 0, 0.0, MASKED).astype(jnp.float32)

    with jax.named_scope("cotangent_gather"):
        cot_all = lax.all_gather(out_cotangent[0, 0], "ha", axis=0, tiled=True)

    with jax.named_scope("attention_forward"):
        attended = attention_forward(mask, q, window)

    with jax.named_scope("output_projection"):
        projected = jnp.dot(attended, out_weight, preferred_element_type=jnp.float32)
        layer_out = lax.psum_scatter(
            projected.astype(jnp.bfloat16), "ha", scatter_dimension=0, tiled=True
        )

    with jax.named_scope("grad_attended"):
        grad_attended = lax.dot_general(
            cot_all, out_weight, (((1,), (1,)), ((), ())), preferred_element_type=jnp.float32
        ).astype(jnp.bfloat16)

    with jax.named_scope("grad_weight"):
        weight_part = lax.dot_general(
            cot_all, attended, (((0,), (0,)), ((), ())), preferred_element_type=jnp.float32
        )
        weight_own, weight_sent = scatter_parts(weight_part, "fh", 0)
        weight_own, weight_sent, grad_attended = lax.optimization_barrier(
            (weight_own, weight_sent, grad_attended)
        )
        weight_rows = scatter_finish(weight_own, weight_sent, "fh")

    grad_q_heads, own_heads = [], []
    for head in range(features // HD):
        with jax.named_scope("attention_backward"):
            grad_q, left, partials, right = attention_backward(
                mask, q, window, attended, grad_attended, head
            )
        with jax.named_scope("halo_reduction"):
            own_heads.append(return_halo(left, partials, right))
        grad_q_heads.append(grad_q)
    grad_q = jnp.concatenate(grad_q_heads, axis=1)
    own = jnp.concatenate(own_heads, axis=1)

    with jax.named_scope("grad_weight"):
        grad_weight = scatter_sum(weight_rows, "wa", 0)

    grad_keys = own[:tokens].astype(jnp.bfloat16)
    grad_values = own[tokens:].astype(jnp.bfloat16)
    expand = lambda x: x[None, None]
    return (
        expand(layer_out),
        expand(grad_q),
        expand(grad_keys),
        expand(grad_values),
        grad_weight,
    )


def solution(mesh):
    return jax.shard_map(
        body,
        mesh=mesh,
        in_specs=(
            P("fh", "wa", None, "ha"),
            P("fh", "wa", None, "ha"),
            P("fh", "wa", None, "ha"),
            P("fh", "wa", None),
            P("ha", None),
            P("fh", "wa", "ha", None),
        ),
        out_specs=(
            P("fh", "wa", "ha", None),
            P("fh", "wa", None, "ha"),
            P("fh", "wa", None, "ha"),
            P("fh", "wa", None, "ha"),
            P(("fh", "wa"), "ha"),
        ),
        check_vma=False,
    )
```

```python
import functools

import jax
import jax.numpy as jnp
from jax import lax
from jax.experimental import pallas as pl
from jax.experimental.pallas import tpu as pltpu
from jax.sharding import PartitionSpec as P

HD = 128
MASKED = -1e30
FORWARD_CHUNK = 384
BACKWARD_CHUNK = 192
FLAG_ROWS = 16


def shift_pairs(count, steps):
    return [(source, source + steps) for source in range(count) if 0 <= source + steps < count]


def shifted(value, axis, steps):
    return lax.ppermute(value, axis, shift_pairs(lax.axis_size(axis), steps))


def cyclic(value, axis, steps):
    count = lax.axis_size(axis)
    return lax.ppermute(value, axis, [(i, (i + steps) % count) for i in range(count)])


def scores_of(mask_ref, q_ref, k_ref, scale):
    q = q_ref[...]
    k = k_ref[...].reshape(-1, HD)
    s = lax.dot_general(q, k, (((1,), (1,)), ((), ())), preferred_element_type=jnp.float32)
    return s * scale + mask_ref[...]


def forward_kernel(scale, mask_ref, q_ref, k_ref, v_ref, o_ref):
    s = scores_of(mask_ref, q_ref, k_ref, scale)
    m = jnp.max(s, axis=1, keepdims=True)
    e = jnp.exp(s - m)
    total = jnp.sum(e, axis=1, keepdims=True)
    p = (e * (1.0 / total)).astype(jnp.bfloat16)
    v = v_ref[...].reshape(-1, HD)
    o_ref[...] = jnp.dot(p, v, preferred_element_type=jnp.float32).astype(o_ref.dtype)


def backward_kernel(
    scale, mask_ref, q_ref, k_ref, v_ref, o_ref, do_ref, dq_ref, left_ref, mid_ref, right_ref, acc_ref
):
    chunk = pl.program_id(1)
    s = scores_of(mask_ref, q_ref, k_ref, scale)
    m = jnp.max(s, axis=1, keepdims=True)
    e = jnp.exp(s - m)
    total = jnp.sum(e, axis=1, keepdims=True)
    w = e * (1.0 / total)
    p = w.astype(jnp.bfloat16)
    do = do_ref[...]
    row_dot = jnp.sum(
        do.astype(jnp.float32) * o_ref[...].astype(jnp.float32), axis=1, keepdims=True
    )
    k = k_ref[...].reshape(-1, HD)
    v = v_ref[...].reshape(-1, HD)
    dp = lax.dot_general(do, v, (((1,), (1,)), ((), ())), preferred_element_type=jnp.float32)
    ds = (w * (dp - row_dot)).astype(jnp.bfloat16)
    dq = jnp.dot(ds, k, preferred_element_type=jnp.float32) * scale
    dq_ref[...] = dq.astype(dq_ref.dtype)
    contract0 = (((0,), (0,)), ((), ()))
    dk = lax.dot_general(ds, q_ref[...], contract0, preferred_element_type=jnp.float32) * scale
    dv = lax.dot_general(p, do, contract0, preferred_element_type=jnp.float32)
    tiles, tokens = k_ref.shape[0], k_ref.shape[1]
    dk = dk.reshape(tiles, tokens, HD)
    dv = dv.reshape(tiles, tokens, HD)

    @pl.when(chunk == 0)
    def _():
        acc_ref[:, :tokens, :] = dk
        acc_ref[:, tokens:, :] = dv

    @pl.when(chunk > 0)
    def _():
        acc_ref[:, :tokens, :] += dk
        acc_ref[:, tokens:, :] += dv

    @pl.when(chunk == pl.num_programs(1) - 1)
    def _():
        third = tiles // 3
        left_ref[...] = acc_ref[:third].astype(left_ref.dtype)
        mid_ref[...] = acc_ref[third : 2 * third]
        right_ref[...] = acc_ref[2 * third :].astype(right_ref.dtype)


def attention_forward(mask, queries, window):
    tokens, features = queries.shape
    tiles = window.shape[0]
    heads = features // HD
    chunk = FORWARD_CHUNK
    chunks = tokens // chunk
    scale = HD ** (-0.5)
    return pl.pallas_call(
        functools.partial(forward_kernel, scale),
        grid=(heads, chunks),
        in_specs=[
            pl.BlockSpec((1, tiles * tokens), lambda h, c: (0, 0)),
            pl.BlockSpec((chunk, HD), lambda h, c: (c, h)),
            pl.BlockSpec((tiles, tokens, HD), lambda h, c: (0, 0, h)),
            pl.BlockSpec((tiles, tokens, HD), lambda h, c: (0, 1, h)),
        ],
        out_specs=pl.BlockSpec((chunk, HD), lambda h, c: (c, h)),
        out_shape=jax.ShapeDtypeStruct((tokens, features), jnp.bfloat16),
        name="tile_attention_forward",
    )(mask, queries, window, window)


def attention_backward(mask, queries, window, attended, grad_attended):
    tokens, features = queries.shape
    tiles = window.shape[0]
    heads = features // HD
    chunk = BACKWARD_CHUNK
    chunks = tokens // chunk
    scale = HD ** (-0.5)
    return pl.pallas_call(
        functools.partial(backward_kernel, scale),
        grid=(heads, chunks),
        in_specs=[
            pl.BlockSpec((1, tiles * tokens), lambda h, c: (0, 0)),
            pl.BlockSpec((chunk, HD), lambda h, c: (c, h)),
            pl.BlockSpec((tiles, tokens, HD), lambda h, c: (0, 0, h)),
            pl.BlockSpec((tiles, tokens, HD), lambda h, c: (0, 1, h)),
            pl.BlockSpec((chunk, HD), lambda h, c: (c, h)),
            pl.BlockSpec((chunk, HD), lambda h, c: (c, h)),
        ],
        out_specs=[
            pl.BlockSpec((chunk, HD), lambda h, c: (c, h)),
            pl.BlockSpec((tiles // 3, 2 * tokens, HD), lambda h, c: (0, 0, h)),
            pl.BlockSpec((tiles // 3, 2 * tokens, HD), lambda h, c: (0, 0, h)),
            pl.BlockSpec((tiles // 3, 2 * tokens, HD), lambda h, c: (0, 0, h)),
        ],
        out_shape=[
            jax.ShapeDtypeStruct((tokens, features), jnp.bfloat16),
            jax.ShapeDtypeStruct((tiles // 3, 2 * tokens, features), jnp.bfloat16),
            jax.ShapeDtypeStruct((tiles // 3, 2 * tokens, features), jnp.float32),
            jax.ShapeDtypeStruct((tiles // 3, 2 * tokens, features), jnp.bfloat16),
        ],
        scratch_shapes=[pltpu.VMEM((tiles, 2 * tokens, HD), jnp.float32)],
        name="tile_attention_backward",
    )(mask, queries, window, window, attended, grad_attended)


def gather_over(piece, axis):
    count = lax.axis_size(axis)
    me = lax.axis_index(axis)
    received = [piece] + [cyclic(piece, axis, steps) for steps in range(1, count)]
    ordered = jnp.stack([received[(-k) % count] for k in range(count)])
    return jnp.roll(ordered, me, axis=0)


def scatter_parts(full, axis, dim):
    count = lax.axis_size(axis)
    me = lax.axis_index(axis)
    size = full.shape[dim] // count

    def part(index):
        return lax.dynamic_slice_in_dim(full, index * size, size, axis=dim)

    sent = [part((me + steps) % count).astype(jnp.bfloat16) for steps in range(1, count)]
    return part(me).astype(jnp.float32), sent


def scatter_finish(own, sent, axis):
    total = own
    for steps, piece in enumerate(sent, start=1):
        total = total + cyclic(piece, axis, steps).astype(jnp.float32)
    return total


def scatter_sum(full, axis, dim):
    count = lax.axis_size(axis)
    me = lax.axis_index(axis)
    size = full.shape[dim] // count

    def part(index):
        return lax.dynamic_slice_in_dim(full, index * size, size, axis=dim)

    total = part(me).astype(jnp.float32)
    for steps in range(1, count):
        sent = part((me + steps) % count).astype(jnp.bfloat16)
        total = total + cyclic(sent, axis, steps).astype(jnp.float32)
    return total


def body(queries, key_states, value_states, valid_mask, out_weight, out_cotangent):
    tile_rows, tile_columns, tokens, features = queries.shape
    assert tile_rows == 1 and tile_columns == 1
    model_width = out_weight.shape[1]
    q = queries[0, 0]
    flag_rows = jnp.zeros((FLAG_ROWS, features), jnp.bfloat16)
    flag_rows = flag_rows.at[0, :tokens].set(valid_mask[0, 0].astype(jnp.bfloat16))
    packed = jnp.concatenate([key_states[0, 0], value_states[0, 0], flag_rows], axis=0)

    with jax.named_scope("halo_exchange"):
        column = jnp.stack([shifted(packed, "fh", 1), packed, shifted(packed, "fh", -1)])
        window = jnp.concatenate(
            [shifted(column, "wa", 1), column, shifted(column, "wa", -1)], axis=0
        )
    tiles = window.shape[0]
    flags = window[:, 2 * tokens, :tokens].reshape(1, tiles * tokens)
    mask = jnp.where(flags > 0, 0.0, MASKED).astype(jnp.float32)

    with jax.named_scope("cotangent_gather"):
        cot_all = lax.all_gather(out_cotangent[0, 0], "ha", axis=0, tiled=True)

    with jax.named_scope("attention_forward"):
        attended = attention_forward(mask, q, window)

    with jax.named_scope("output_projection"):
        projected = jnp.dot(attended, out_weight, preferred_element_type=jnp.float32)
        out_own, out_sent = scatter_parts(projected, "ha", 0)

    with jax.named_scope("grad_attended"):
        grad_attended = lax.dot_general(
            cot_all, out_weight, (((1,), (1,)), ((), ())), preferred_element_type=jnp.float32
        ).astype(jnp.bfloat16)

    with jax.named_scope("grad_weight"):
        weight_part = lax.dot_general(
            cot_all, attended, (((0,), (0,)), ((), ())), preferred_element_type=jnp.float32
        )
        weight_bf16 = weight_part.astype(jnp.bfloat16)
        out_own, out_sent, weight_bf16, grad_attended = lax.optimization_barrier(
            (out_own, out_sent, weight_bf16, grad_attended)
        )
        layer_out = scatter_finish(out_own, out_sent, "ha").astype(jnp.bfloat16)
        weight_summed = lax.psum_scatter(
            weight_bf16, ("fh", "wa"), scatter_dimension=0, tiled=True
        )

    with jax.named_scope("attention_backward"):
        grad_q, left, partials, right = attention_backward(
            mask, q, window, attended, grad_attended
        )

    with jax.named_scope("grad_weight"):
        grad_weight = weight_summed.astype(jnp.float32)

    with jax.named_scope("halo_reduction"):
        middle = (
            partials
            + shifted(left, "wa", -1).astype(jnp.float32)
            + shifted(right, "wa", 1).astype(jnp.float32)
        )
        middle_sides = middle.astype(jnp.bfloat16)
        own = (
            middle[1]
            + shifted(middle_sides[0], "fh", -1).astype(jnp.float32)
            + shifted(middle_sides[2], "fh", 1).astype(jnp.float32)
        )
    grad_keys = own[:tokens].astype(jnp.bfloat16)
    grad_values = own[tokens:].astype(jnp.bfloat16)
    expand = lambda x: x[None, None]
    return (
        expand(layer_out),
        expand(grad_q),
        expand(grad_keys),
        expand(grad_values),
        grad_weight,
    )


def solution(mesh):
    return jax.shard_map(
        body,
        mesh=mesh,
        in_specs=(
            P("fh", "wa", None, "ha"),
            P("fh", "wa", None, "ha"),
            P("fh", "wa", None, "ha"),
            P("fh", "wa", None),
            P("ha", None),
            P("fh", "wa", "ha", None),
        ),
        out_specs=(
            P("fh", "wa", "ha", None),
            P("fh", "wa", None, "ha"),
            P("fh", "wa", None, "ha"),
            P("fh", "wa", None, "ha"),
            P(("fh", "wa"), "ha"),
        ),
        check_vma=False,
    )
```

```python
import functools

import jax
import jax.numpy as jnp
from jax import lax
from jax.experimental import pallas as pl
from jax.experimental.pallas import tpu as pltpu
from jax.sharding import PartitionSpec as P

HD = 128
MASKED = -1e30
FORWARD_CHUNK = 384
BACKWARD_CHUNK = 192
FLAG_ROWS = 16


def shift_pairs(count, steps):
    return [(source, source + steps) for source in range(count) if 0 <= source + steps < count]


def shifted(value, axis, steps):
    return lax.ppermute(value, axis, shift_pairs(lax.axis_size(axis), steps))


def cyclic(value, axis, steps):
    count = lax.axis_size(axis)
    return lax.ppermute(value, axis, [(i, (i + steps) % count) for i in range(count)])


def joined(refs):
    return jnp.concatenate([ref[...].reshape(-1, HD) for ref in refs], axis=0)


def scores_of(mask_ref, q_ref, k, scale):
    q = q_ref[...]
    s = lax.dot_general(q, k, (((1,), (1,)), ((), ())), preferred_element_type=jnp.float32)
    return s * scale + mask_ref[...]


def forward_kernel(scale, mask_ref, q_ref, kl, km, kr, vl, vm, vr, o_ref):
    s = scores_of(mask_ref, q_ref, joined((kl, km, kr)), scale)
    m = jnp.max(s, axis=1, keepdims=True)
    e = jnp.exp(s - m)
    total = jnp.sum(e, axis=1, keepdims=True)
    p = (e * (1.0 / total)).astype(jnp.bfloat16)
    v = joined((vl, vm, vr))
    o_ref[...] = jnp.dot(p, v, preferred_element_type=jnp.float32).astype(o_ref.dtype)


def backward_kernel(
    scale, mask_ref, q_ref, kl, km, kr, vl, vm, vr, o_ref, do_ref, dq_ref, left_ref, mid_ref,
    right_ref, acc_ref
):
    chunk = pl.program_id(1)
    k = joined((kl, km, kr))
    v = joined((vl, vm, vr))
    s = scores_of(mask_ref, q_ref, k, scale)
    m = jnp.max(s, axis=1, keepdims=True)
    e = jnp.exp(s - m)
    total = jnp.sum(e, axis=1, keepdims=True)
    w = e * (1.0 / total)
    p = w.astype(jnp.bfloat16)
    do = do_ref[...]
    row_dot = jnp.sum(
        do.astype(jnp.float32) * o_ref[...].astype(jnp.float32), axis=1, keepdims=True
    )
    dp = lax.dot_general(do, v, (((1,), (1,)), ((), ())), preferred_element_type=jnp.float32)
    ds = (w * (dp - row_dot)).astype(jnp.bfloat16)
    dq = jnp.dot(ds, k, preferred_element_type=jnp.float32) * scale
    dq_ref[...] = dq.astype(dq_ref.dtype)
    contract0 = (((0,), (0,)), ((), ()))
    dk = lax.dot_general(ds, q_ref[...], contract0, preferred_element_type=jnp.float32) * scale
    dv = lax.dot_general(p, do, contract0, preferred_element_type=jnp.float32)
    tiles, tokens = 3 * kl.shape[0], kl.shape[1]
    dk = dk.reshape(tiles, tokens, HD)
    dv = dv.reshape(tiles, tokens, HD)

    @pl.when(chunk == 0)
    def _():
        acc_ref[:, :tokens, :] = dk
        acc_ref[:, tokens:, :] = dv

    @pl.when(chunk > 0)
    def _():
        acc_ref[:, :tokens, :] += dk
        acc_ref[:, tokens:, :] += dv

    @pl.when(chunk == pl.num_programs(1) - 1)
    def _():
        third = tiles // 3
        left_ref[...] = acc_ref[:third].astype(left_ref.dtype)
        mid_ref[...] = acc_ref[third : 2 * third]
        right_ref[...] = acc_ref[2 * third :].astype(right_ref.dtype)


def attention_forward(mask, queries, columns):
    tokens, features = queries.shape
    tiles = 3 * columns[0].shape[0]
    heads = features // HD
    chunk = FORWARD_CHUNK
    chunks = tokens // chunk
    scale = HD ** (-0.5)
    return pl.pallas_call(
        functools.partial(forward_kernel, scale),
        grid=(heads, chunks),
        in_specs=[
            pl.BlockSpec((1, tiles * tokens), lambda h, c: (0, 0)),
            pl.BlockSpec((chunk, HD), lambda h, c: (c, h)),
            *[pl.BlockSpec((tiles // 3, tokens, HD), lambda h, c: (0, 0, h))] * 3,
            *[pl.BlockSpec((tiles // 3, tokens, HD), lambda h, c: (0, 1, h))] * 3,
        ],
        out_specs=pl.BlockSpec((chunk, HD), lambda h, c: (c, h)),
        out_shape=jax.ShapeDtypeStruct((tokens, features), jnp.bfloat16),
        name="tile_attention_forward",
    )(mask, queries, *columns, *columns)


def attention_backward(mask, queries, columns, attended, grad_attended):
    tokens, features = queries.shape
    tiles = 3 * columns[0].shape[0]
    heads = features // HD
    chunk = BACKWARD_CHUNK
    chunks = tokens // chunk
    scale = HD ** (-0.5)
    return pl.pallas_call(
        functools.partial(backward_kernel, scale),
        grid=(heads, chunks),
        in_specs=[
            pl.BlockSpec((1, tiles * tokens), lambda h, c: (0, 0)),
            pl.BlockSpec((chunk, HD), lambda h, c: (c, h)),
            *[pl.BlockSpec((tiles // 3, tokens, HD), lambda h, c: (0, 0, h))] * 3,
            *[pl.BlockSpec((tiles // 3, tokens, HD), lambda h, c: (0, 1, h))] * 3,
            pl.BlockSpec((chunk, HD), lambda h, c: (c, h)),
            pl.BlockSpec((chunk, HD), lambda h, c: (c, h)),
        ],
        out_specs=[
            pl.BlockSpec((chunk, HD), lambda h, c: (c, h)),
            pl.BlockSpec((tiles // 3, 2 * tokens, HD), lambda h, c: (0, 0, h)),
            pl.BlockSpec((tiles // 3, 2 * tokens, HD), lambda h, c: (0, 0, h)),
            pl.BlockSpec((tiles // 3, 2 * tokens, HD), lambda h, c: (0, 0, h)),
        ],
        out_shape=[
            jax.ShapeDtypeStruct((tokens, features), jnp.bfloat16),
            jax.ShapeDtypeStruct((tiles // 3, 2 * tokens, features), jnp.bfloat16),
            jax.ShapeDtypeStruct((tiles // 3, 2 * tokens, features), jnp.float32),
            jax.ShapeDtypeStruct((tiles // 3, 2 * tokens, features), jnp.bfloat16),
        ],
        scratch_shapes=[pltpu.VMEM((tiles, 2 * tokens, HD), jnp.float32)],
        name="tile_attention_backward",
    )(mask, queries, *columns, *columns, attended, grad_attended)


def gather_over(piece, axis):
    count = lax.axis_size(axis)
    me = lax.axis_index(axis)
    received = [piece] + [cyclic(piece, axis, steps) for steps in range(1, count)]
    ordered = jnp.stack([received[(-k) % count] for k in range(count)])
    return jnp.roll(ordered, me, axis=0)


def scatter_parts(full, axis, dim):
    count = lax.axis_size(axis)
    me = lax.axis_index(axis)
    size = full.shape[dim] // count

    def part(index):
        return lax.dynamic_slice_in_dim(full, index * size, size, axis=dim)

    sent = [part((me + steps) % count).astype(jnp.bfloat16) for steps in range(1, count)]
    return part(me).astype(jnp.float32), sent


def scatter_finish(own, sent, axis):
    total = own
    for steps, piece in enumerate(sent, start=1):
        total = total + cyclic(piece, axis, steps).astype(jnp.float32)
    return total


def scatter_sum(full, axis, dim):
    count = lax.axis_size(axis)
    me = lax.axis_index(axis)
    size = full.shape[dim] // count

    def part(index):
        return lax.dynamic_slice_in_dim(full, index * size, size, axis=dim)

    total = part(me).astype(jnp.float32)
    for steps in range(1, count):
        sent = part((me + steps) % count).astype(jnp.bfloat16)
        total = total + cyclic(sent, axis, steps).astype(jnp.float32)
    return total


def body(queries, key_states, value_states, valid_mask, out_weight, out_cotangent):
    tile_rows, tile_columns, tokens, features = queries.shape
    assert tile_rows == 1 and tile_columns == 1
    model_width = out_weight.shape[1]
    q = queries[0, 0]
    flag_rows = jnp.zeros((FLAG_ROWS, features), jnp.bfloat16)
    flag_rows = flag_rows.at[0, :tokens].set(valid_mask[0, 0].astype(jnp.bfloat16))
    packed = jnp.concatenate([key_states[0, 0], value_states[0, 0], flag_rows], axis=0)

    with jax.named_scope("halo_exchange"):
        column = jnp.stack([shifted(packed, "fh", 1), packed, shifted(packed, "fh", -1)])
        columns = (shifted(column, "wa", 1), column, shifted(column, "wa", -1))
    flags = jnp.concatenate([side[:, 2 * tokens, :tokens] for side in columns], axis=0)
    flags = flags.reshape(1, -1)
    mask = jnp.where(flags > 0, 0.0, MASKED).astype(jnp.float32)

    with jax.named_scope("cotangent_gather"):
        cot_all = lax.all_gather(out_cotangent[0, 0], "ha", axis=0, tiled=True)

    with jax.named_scope("attention_forward"):
        attended = attention_forward(mask, q, columns)

    with jax.named_scope("output_projection"):
        projected = jnp.dot(attended, out_weight, preferred_element_type=jnp.float32)
        layer_out = lax.psum_scatter(
            projected.astype(jnp.bfloat16), "ha", scatter_dimension=0, tiled=True
        )

    with jax.named_scope("grad_attended"):
        grad_attended = lax.dot_general(
            cot_all, out_weight, (((1,), (1,)), ((), ())), preferred_element_type=jnp.float32
        ).astype(jnp.bfloat16)

    with jax.named_scope("grad_weight"):
        weight_part = lax.dot_general(
            cot_all, attended, (((0,), (0,)), ((), ())), preferred_element_type=jnp.float32
        )
        weight_own, weight_sent = scatter_parts(weight_part, "fh", 0)
        weight_own, weight_sent, grad_attended = lax.optimization_barrier(
            (weight_own, weight_sent, grad_attended)
        )
        weight_rows = scatter_finish(weight_own, weight_sent, "fh")

    with jax.named_scope("attention_backward"):
        grad_q, left, partials, right = attention_backward(
            mask, q, columns, attended, grad_attended
        )

    with jax.named_scope("grad_weight"):
        grad_weight = scatter_sum(weight_rows, "wa", 0)

    with jax.named_scope("halo_reduction"):
        middle = (
            partials
            + shifted(left, "wa", -1).astype(jnp.float32)
            + shifted(right, "wa", 1).astype(jnp.float32)
        )
        middle_sides = middle.astype(jnp.bfloat16)
        own = (
            middle[1]
            + shifted(middle_sides[0], "fh", -1).astype(jnp.float32)
            + shifted(middle_sides[2], "fh", 1).astype(jnp.float32)
        )
    grad_keys = own[:tokens].astype(jnp.bfloat16)
    grad_values = own[tokens:].astype(jnp.bfloat16)
    expand = lambda x: x[None, None]
    return (
        expand(layer_out),
        expand(grad_q),
        expand(grad_keys),
        expand(grad_values),
        grad_weight,
    )


def solution(mesh):
    return jax.shard_map(
        body,
        mesh=mesh,
        in_specs=(
            P("fh", "wa", None, "ha"),
            P("fh", "wa", None, "ha"),
            P("fh", "wa", None, "ha"),
            P("fh", "wa", None),
            P("ha", None),
            P("fh", "wa", "ha", None),
        ),
        out_specs=(
            P("fh", "wa", "ha", None),
            P("fh", "wa", None, "ha"),
            P("fh", "wa", None, "ha"),
            P("fh", "wa", None, "ha"),
            P(("fh", "wa"), "ha"),
        ),
        check_vma=False,
    )
```

```python
import functools

import jax
import jax.numpy as jnp
from jax import lax
from jax.experimental import pallas as pl
from jax.experimental.pallas import tpu as pltpu
from jax.sharding import PartitionSpec as P

HD = 128
MASKED = -1e30
FORWARD_CHUNK = 384
BACKWARD_CHUNK = 192
FLAG_ROWS = 16


def shift_pairs(count, steps):
    return [(source, source + steps) for source in range(count) if 0 <= source + steps < count]


def shifted(value, axis, steps):
    return lax.ppermute(value, axis, shift_pairs(lax.axis_size(axis), steps))


def cyclic(value, axis, steps):
    count = lax.axis_size(axis)
    return lax.ppermute(value, axis, [(i, (i + steps) % count) for i in range(count)])


def softmax_rows(scale, present_ref, mask_ref, q, k_cols, s_scr, m_scr, l_scr):
    tiles = s_scr.shape[0]
    rows = tiles // len(k_cols)
    m_scr[...] = jnp.full(m_scr.shape, -jnp.inf, jnp.float32)
    l_scr[...] = jnp.zeros(l_scr.shape, jnp.float32)
    for t in range(tiles):

        @pl.when(present_ref[t] > 0)
        def _():
            k = k_cols[t // rows][t % rows]
            s = lax.dot_general(q, k, (((1,), (1,)), ((), ())), preferred_element_type=jnp.float32)
            s = s * scale + mask_ref[t]
            s_scr[t] = s
            m_scr[...] = jnp.maximum(m_scr[...], jnp.max(s, axis=1, keepdims=True))

    for t in range(tiles):

        @pl.when(present_ref[t] > 0)
        def _():
            e = jnp.exp(s_scr[t] - m_scr[...])
            s_scr[t] = e
            l_scr[...] += jnp.sum(e, axis=1, keepdims=True)


def forward_kernel(
    scale, present_ref, mask_ref, q_ref, kl, km, kr, vl, vm, vr, o_ref, s_scr, m_scr, l_scr, acc_scr
):
    q = q_ref[...]
    softmax_rows(scale, present_ref, mask_ref, q, (kl, km, kr), s_scr, m_scr, l_scr)
    inverse = 1.0 / l_scr[...]
    v_cols = (vl, vm, vr)
    tiles = s_scr.shape[0]
    rows = tiles // 3
    acc_scr[...] = jnp.zeros(acc_scr.shape, jnp.float32)
    for t in range(tiles):

        @pl.when(present_ref[t] > 0)
        def _():
            p = (s_scr[t] * inverse).astype(jnp.bfloat16)
            v = v_cols[t // rows][t % rows]
            acc_scr[...] += jnp.dot(p, v, preferred_element_type=jnp.float32)

    o_ref[...] = acc_scr[...].astype(o_ref.dtype)


def backward_kernel(
    scale, present_ref, mask_ref, q_ref, kl, km, kr, vl, vm, vr, o_ref, do_ref,
    dq_ref, left_ref, mid_ref, right_ref, s_scr, m_scr, l_scr, dq_scr, acc_ref
):
    chunk = pl.program_id(1)
    tiles = s_scr.shape[0]
    rows = tiles // 3
    tokens = kl.shape[1]

    @pl.when(chunk == 0)
    def _():
        acc_ref[...] = jnp.zeros(acc_ref.shape, jnp.float32)

    q = q_ref[...]
    k_cols = (kl, km, kr)
    v_cols = (vl, vm, vr)
    softmax_rows(scale, present_ref, mask_ref, q, k_cols, s_scr, m_scr, l_scr)
    inverse = 1.0 / l_scr[...]
    do = do_ref[...]
    row_dot = jnp.sum(
        do.astype(jnp.float32) * o_ref[...].astype(jnp.float32), axis=1, keepdims=True
    )
    dq_scr[...] = jnp.zeros(dq_scr.shape, jnp.float32)
    contract0 = (((0,), (0,)), ((), ()))
    for t in range(tiles):

        @pl.when(present_ref[t] > 0)
        def _():
            k = k_cols[t // rows][t % rows]
            v = v_cols[t // rows][t % rows]
            w = s_scr[t] * inverse
            p = w.astype(jnp.bfloat16)
            dp = lax.dot_general(
                do, v, (((1,), (1,)), ((), ())), preferred_element_type=jnp.float32
            )
            ds = (w * (dp - row_dot)).astype(jnp.bfloat16)
            dq_scr[...] += jnp.dot(ds, k, preferred_element_type=jnp.float32)
            dk = lax.dot_general(ds, q, contract0, preferred_element_type=jnp.float32) * scale
            dv = lax.dot_general(p, do, contract0, preferred_element_type=jnp.float32)
            acc_ref[t, :tokens, :] += dk
            acc_ref[t, tokens:, :] += dv

    dq_ref[...] = (dq_scr[...] * scale).astype(dq_ref.dtype)

    @pl.when(chunk == pl.num_programs(1) - 1)
    def _():
        left_ref[...] = acc_ref[:rows].astype(left_ref.dtype)
        mid_ref[...] = acc_ref[rows : 2 * rows]
        right_ref[...] = acc_ref[2 * rows :].astype(right_ref.dtype)


def attention_forward(present, mask, queries, columns):
    tokens, features = queries.shape
    rows = columns[0].shape[0]
    tiles = 3 * rows
    heads = features // HD
    chunk = FORWARD_CHUNK
    chunks = tokens // chunk
    scale = HD ** (-0.5)
    return pl.pallas_call(
        functools.partial(forward_kernel, scale),
        grid_spec=pltpu.PrefetchScalarGridSpec(
            num_scalar_prefetch=1,
            grid=(heads, chunks),
            in_specs=[
                pl.BlockSpec((tiles, 1, tokens), lambda h, c, flags: (0, 0, 0)),
                pl.BlockSpec((chunk, HD), lambda h, c, flags: (c, h)),
                *[pl.BlockSpec((rows, tokens, HD), lambda h, c, flags: (0, 0, h))] * 3,
                *[pl.BlockSpec((rows, tokens, HD), lambda h, c, flags: (0, 1, h))] * 3,
            ],
            out_specs=pl.BlockSpec((chunk, HD), lambda h, c, flags: (c, h)),
            scratch_shapes=[
                pltpu.VMEM((tiles, chunk, tokens), jnp.float32),
                pltpu.VMEM((chunk, 1), jnp.float32),
                pltpu.VMEM((chunk, 1), jnp.float32),
                pltpu.VMEM((chunk, HD), jnp.float32),
            ],
        ),
        out_shape=jax.ShapeDtypeStruct((tokens, features), jnp.bfloat16),
        name="tile_attention_forward",
    )(present, mask, queries, *columns, *columns)


def attention_backward(present, mask, queries, columns, attended, grad_attended):
    tokens, features = queries.shape
    rows = columns[0].shape[0]
    tiles = 3 * rows
    heads = features // HD
    chunk = BACKWARD_CHUNK
    chunks = tokens // chunk
    scale = HD ** (-0.5)
    return pl.pallas_call(
        functools.partial(backward_kernel, scale),
        grid_spec=pltpu.PrefetchScalarGridSpec(
            num_scalar_prefetch=1,
            grid=(heads, chunks),
            in_specs=[
                pl.BlockSpec((tiles, 1, tokens), lambda h, c, flags: (0, 0, 0)),
                pl.BlockSpec((chunk, HD), lambda h, c, flags: (c, h)),
                *[pl.BlockSpec((rows, tokens, HD), lambda h, c, flags: (0, 0, h))] * 3,
                *[pl.BlockSpec((rows, tokens, HD), lambda h, c, flags: (0, 1, h))] * 3,
                pl.BlockSpec((chunk, HD), lambda h, c, flags: (c, h)),
                pl.BlockSpec((chunk, HD), lambda h, c, flags: (c, h)),
            ],
            out_specs=[
                pl.BlockSpec((chunk, HD), lambda h, c, flags: (c, h)),
                *[pl.BlockSpec((rows, 2 * tokens, HD), lambda h, c, flags: (0, 0, h))] * 3,
            ],
            scratch_shapes=[
                pltpu.VMEM((tiles, chunk, tokens), jnp.float32),
                pltpu.VMEM((chunk, 1), jnp.float32),
                pltpu.VMEM((chunk, 1), jnp.float32),
                pltpu.VMEM((chunk, HD), jnp.float32),
                pltpu.VMEM((tiles, 2 * tokens, HD), jnp.float32),
            ],
        ),
        out_shape=[
            jax.ShapeDtypeStruct((tokens, features), jnp.bfloat16),
            jax.ShapeDtypeStruct((rows, 2 * tokens, features), jnp.bfloat16),
            jax.ShapeDtypeStruct((rows, 2 * tokens, features), jnp.float32),
            jax.ShapeDtypeStruct((rows, 2 * tokens, features), jnp.bfloat16),
        ],
        name="tile_attention_backward",
    )(present, mask, queries, *columns, *columns, attended, grad_attended)


def gather_over(piece, axis):
    count = lax.axis_size(axis)
    me = lax.axis_index(axis)
    received = [piece] + [cyclic(piece, axis, steps) for steps in range(1, count)]
    ordered = jnp.stack([received[(-k) % count] for k in range(count)])
    return jnp.roll(ordered, me, axis=0)


def scatter_parts(full, axis, dim):
    count = lax.axis_size(axis)
    me = lax.axis_index(axis)
    size = full.shape[dim] // count

    def part(index):
        return lax.dynamic_slice_in_dim(full, index * size, size, axis=dim)

    sent = [part((me + steps) % count).astype(jnp.bfloat16) for steps in range(1, count)]
    return part(me).astype(jnp.float32), sent


def scatter_finish(own, sent, axis):
    total = own
    for steps, piece in enumerate(sent, start=1):
        total = total + cyclic(piece, axis, steps).astype(jnp.float32)
    return total


def scatter_sum(full, axis, dim):
    count = lax.axis_size(axis)
    me = lax.axis_index(axis)
    size = full.shape[dim] // count

    def part(index):
        return lax.dynamic_slice_in_dim(full, index * size, size, axis=dim)

    total = part(me).astype(jnp.float32)
    for steps in range(1, count):
        sent = part((me + steps) % count).astype(jnp.bfloat16)
        total = total + cyclic(sent, axis, steps).astype(jnp.float32)
    return total


def body(queries, key_states, value_states, valid_mask, out_weight, out_cotangent):
    tile_rows, tile_columns, tokens, features = queries.shape
    assert tile_rows == 1 and tile_columns == 1
    model_width = out_weight.shape[1]
    q = queries[0, 0]
    flag_rows = jnp.zeros((FLAG_ROWS, features), jnp.bfloat16)
    flag_rows = flag_rows.at[0, :tokens].set(valid_mask[0, 0].astype(jnp.bfloat16))
    packed = jnp.concatenate([key_states[0, 0], value_states[0, 0], flag_rows], axis=0)

    with jax.named_scope("halo_exchange"):
        column = jnp.stack([shifted(packed, "fh", 1), packed, shifted(packed, "fh", -1)])
        columns = (shifted(column, "wa", 1), column, shifted(column, "wa", -1))
    mask = jnp.concatenate(
        [jnp.where(side[:, 2 * tokens : 2 * tokens + 1, :tokens] > 0, 0.0, MASKED) for side in columns]
    ).astype(jnp.float32)
    row_at = lax.axis_index("fh") + jnp.arange(3) - 1
    column_at = lax.axis_index("wa") + jnp.arange(3) - 1
    present = (
        ((column_at >= 0) & (column_at < lax.axis_size("wa")))[:, None]
        & ((row_at >= 0) & (row_at < lax.axis_size("fh")))[None, :]
    ).reshape(-1).astype(jnp.int32)

    with jax.named_scope("cotangent_gather"):
        cot_all = lax.all_gather(out_cotangent[0, 0], "ha", axis=0, tiled=True)

    with jax.named_scope("attention_forward"):
        attended = attention_forward(present, mask, q, columns)

    with jax.named_scope("output_projection"):
        projected = jnp.dot(attended, out_weight, preferred_element_type=jnp.float32)
        layer_out = lax.psum_scatter(
            projected.astype(jnp.bfloat16), "ha", scatter_dimension=0, tiled=True
        )

    with jax.named_scope("grad_attended"):
        grad_attended = lax.dot_general(
            cot_all, out_weight, (((1,), (1,)), ((), ())), preferred_element_type=jnp.float32
        ).astype(jnp.bfloat16)

    with jax.named_scope("grad_weight"):
        weight_part = lax.dot_general(
            cot_all, attended, (((0,), (0,)), ((), ())), preferred_element_type=jnp.float32
        )
        weight_own, weight_sent = scatter_parts(weight_part, "fh", 0)
        weight_own, weight_sent, grad_attended = lax.optimization_barrier(
            (weight_own, weight_sent, grad_attended)
        )
        weight_rows = scatter_finish(weight_own, weight_sent, "fh")

    with jax.named_scope("attention_backward"):
        grad_q, left, partials, right = attention_backward(
            present, mask, q, columns, attended, grad_attended
        )

    with jax.named_scope("grad_weight"):
        grad_weight = scatter_sum(weight_rows, "wa", 0)

    with jax.named_scope("halo_reduction"):
        middle = (
            partials
            + shifted(left, "wa", -1).astype(jnp.float32)
            + shifted(right, "wa", 1).astype(jnp.float32)
        )
        middle_sides = middle.astype(jnp.bfloat16)
        own = (
            middle[1]
            + shifted(middle_sides[0], "fh", -1).astype(jnp.float32)
            + shifted(middle_sides[2], "fh", 1).astype(jnp.float32)
        )
    grad_keys = own[:tokens].astype(jnp.bfloat16)
    grad_values = own[tokens:].astype(jnp.bfloat16)
    expand = lambda x: x[None, None]
    return (
        expand(layer_out),
        expand(grad_q),
        expand(grad_keys),
        expand(grad_values),
        grad_weight,
    )


def solution(mesh):
    return jax.shard_map(
        body,
        mesh=mesh,
        in_specs=(
            P("fh", "wa", None, "ha"),
            P("fh", "wa", None, "ha"),
            P("fh", "wa", None, "ha"),
            P("fh", "wa", None),
            P("ha", None),
            P("fh", "wa", "ha", None),
        ),
        out_specs=(
            P("fh", "wa", "ha", None),
            P("fh", "wa", None, "ha"),
            P("fh", "wa", None, "ha"),
            P("fh", "wa", None, "ha"),
            P(("fh", "wa"), "ha"),
        ),
        check_vma=False,
    )
```

```python
import functools

import jax
import jax.numpy as jnp
from jax import lax
from jax.experimental import pallas as pl
from jax.experimental.pallas import tpu as pltpu
from jax.sharding import PartitionSpec as P

HD = 128
MASKED = -1e30
FORWARD_CHUNK = 384
BACKWARD_CHUNK = 192
FLAG_ROWS = 16
LOG2E = 1.4426950408889634


def shift_pairs(count, steps):
    return [(source, source + steps) for source in range(count) if 0 <= source + steps < count]


def shifted(value, axis, steps):
    return lax.ppermute(value, axis, shift_pairs(lax.axis_size(axis), steps))


def cyclic(value, axis, steps):
    count = lax.axis_size(axis)
    return lax.ppermute(value, axis, [(i, (i + steps) % count) for i in range(count)])


def joined(refs):
    return jnp.concatenate([ref[...].reshape(-1, HD) for ref in refs], axis=0)


def raw_scores(mask_ref, q_ref, k):
    s = lax.dot_general(q_ref[...], k, (((1,), (1,)), ((), ())), preferred_element_type=jnp.float32)
    return s + mask_ref[...]


def forward_kernel(exp_scale, mask_ref, q_ref, kl, km, kr, vl, vm, vr, o_ref, m_ref, r_ref):
    s = raw_scores(mask_ref, q_ref, joined((kl, km, kr)))
    m = jnp.max(s, axis=1, keepdims=True)
    e = jnp.exp2((s - m) * exp_scale)
    inverse = 1.0 / jnp.sum(e, axis=1, keepdims=True)
    p = (e * inverse).astype(jnp.bfloat16)
    v = joined((vl, vm, vr))
    o_ref[...] = jnp.dot(p, v, preferred_element_type=jnp.float32).astype(o_ref.dtype)
    m_ref[...] = jnp.broadcast_to(m, m_ref.shape)
    r_ref[...] = jnp.broadcast_to(inverse, r_ref.shape)


def backward_kernel(
    scale, exp_scale, mask_ref, q_ref, kl, km, kr, vl, vm, vr, o_ref, m_ref, r_ref, do_ref,
    dq_ref, left_ref, mid_ref, right_ref, acc_ref
):
    chunk = pl.program_id(1)
    k = joined((kl, km, kr))
    v = joined((vl, vm, vr))
    s = raw_scores(mask_ref, q_ref, k)
    w = jnp.exp2((s - m_ref[:, :1]) * exp_scale) * r_ref[:, :1]
    p = w.astype(jnp.bfloat16)
    do = do_ref[...]
    row_dot = jnp.sum(
        do.astype(jnp.float32) * o_ref[...].astype(jnp.float32), axis=1, keepdims=True
    )
    dp = lax.dot_general(do, v, (((1,), (1,)), ((), ())), preferred_element_type=jnp.float32)
    ds = (w * (dp - row_dot)).astype(jnp.bfloat16)
    dq = jnp.dot(ds, k, preferred_element_type=jnp.float32) * scale
    dq_ref[...] = dq.astype(dq_ref.dtype)
    contract0 = (((0,), (0,)), ((), ()))
    dk = lax.dot_general(ds, q_ref[...], contract0, preferred_element_type=jnp.float32) * scale
    dv = lax.dot_general(p, do, contract0, preferred_element_type=jnp.float32)
    tiles, tokens = 3 * kl.shape[0], kl.shape[1]
    dk = dk.reshape(tiles, tokens, HD)
    dv = dv.reshape(tiles, tokens, HD)

    @pl.when(chunk == 0)
    def _():
        acc_ref[:, :tokens, :] = dk
        acc_ref[:, tokens:, :] = dv

    @pl.when(chunk > 0)
    def _():
        acc_ref[:, :tokens, :] += dk
        acc_ref[:, tokens:, :] += dv

    @pl.when(chunk == pl.num_programs(1) - 1)
    def _():
        third = tiles // 3
        left_ref[...] = acc_ref[:third].astype(left_ref.dtype)
        mid_ref[...] = acc_ref[third : 2 * third]
        right_ref[...] = acc_ref[2 * third :].astype(right_ref.dtype)


def attention_forward(mask, queries, columns):
    tokens, features = queries.shape
    tiles = 3 * columns[0].shape[0]
    heads = features // HD
    chunk = FORWARD_CHUNK
    chunks = tokens // chunk
    scale = HD ** (-0.5)
    return pl.pallas_call(
        functools.partial(forward_kernel, scale * LOG2E),
        grid=(heads, chunks),
        in_specs=[
            pl.BlockSpec((1, tiles * tokens), lambda h, c: (0, 0)),
            pl.BlockSpec((chunk, HD), lambda h, c: (c, h)),
            *[pl.BlockSpec((tiles // 3, tokens, HD), lambda h, c: (0, 0, h))] * 3,
            *[pl.BlockSpec((tiles // 3, tokens, HD), lambda h, c: (0, 1, h))] * 3,
        ],
        out_specs=[pl.BlockSpec((chunk, HD), lambda h, c: (c, h))] * 3,
        out_shape=[
            jax.ShapeDtypeStruct((tokens, features), jnp.bfloat16),
            jax.ShapeDtypeStruct((tokens, features), jnp.float32),
            jax.ShapeDtypeStruct((tokens, features), jnp.float32),
        ],
        name="tile_attention_forward",
    )(mask, queries, *columns, *columns)


def attention_backward(mask, queries, columns, attended, row_max, row_inverse, grad_attended):
    tokens, features = queries.shape
    tiles = 3 * columns[0].shape[0]
    heads = features // HD
    chunk = BACKWARD_CHUNK
    chunks = tokens // chunk
    scale = HD ** (-0.5)
    return pl.pallas_call(
        functools.partial(backward_kernel, scale, scale * LOG2E),
        grid=(heads, chunks),
        in_specs=[
            pl.BlockSpec((1, tiles * tokens), lambda h, c: (0, 0)),
            pl.BlockSpec((chunk, HD), lambda h, c: (c, h)),
            *[pl.BlockSpec((tiles // 3, tokens, HD), lambda h, c: (0, 0, h))] * 3,
            *[pl.BlockSpec((tiles // 3, tokens, HD), lambda h, c: (0, 1, h))] * 3,
            pl.BlockSpec((chunk, HD), lambda h, c: (c, h)),
            pl.BlockSpec((chunk, HD), lambda h, c: (c, h)),
            pl.BlockSpec((chunk, HD), lambda h, c: (c, h)),
            pl.BlockSpec((chunk, HD), lambda h, c: (c, h)),
        ],
        out_specs=[
            pl.BlockSpec((chunk, HD), lambda h, c: (c, h)),
            pl.BlockSpec((tiles // 3, 2 * tokens, HD), lambda h, c: (0, 0, h)),
            pl.BlockSpec((tiles // 3, 2 * tokens, HD), lambda h, c: (0, 0, h)),
            pl.BlockSpec((tiles // 3, 2 * tokens, HD), lambda h, c: (0, 0, h)),
        ],
        out_shape=[
            jax.ShapeDtypeStruct((tokens, features), jnp.bfloat16),
            jax.ShapeDtypeStruct((tiles // 3, 2 * tokens, features), jnp.bfloat16),
            jax.ShapeDtypeStruct((tiles // 3, 2 * tokens, features), jnp.float32),
            jax.ShapeDtypeStruct((tiles // 3, 2 * tokens, features), jnp.bfloat16),
        ],
        scratch_shapes=[pltpu.VMEM((tiles, 2 * tokens, HD), jnp.float32)],
        name="tile_attention_backward",
    )(mask, queries, *columns, *columns, attended, row_max, row_inverse, grad_attended)


def gather_over(piece, axis):
    count = lax.axis_size(axis)
    me = lax.axis_index(axis)
    received = [piece] + [cyclic(piece, axis, steps) for steps in range(1, count)]
    ordered = jnp.stack([received[(-k) % count] for k in range(count)])
    return jnp.roll(ordered, me, axis=0)


def scatter_parts(full, axis, dim):
    count = lax.axis_size(axis)
    me = lax.axis_index(axis)
    size = full.shape[dim] // count

    def part(index):
        return lax.dynamic_slice_in_dim(full, index * size, size, axis=dim)

    sent = [part((me + steps) % count).astype(jnp.bfloat16) for steps in range(1, count)]
    return part(me).astype(jnp.float32), sent


def scatter_finish(own, sent, axis):
    total = own
    for steps, piece in enumerate(sent, start=1):
        total = total + cyclic(piece, axis, steps).astype(jnp.float32)
    return total


def scatter_sum(full, axis, dim):
    count = lax.axis_size(axis)
    me = lax.axis_index(axis)
    size = full.shape[dim] // count

    def part(index):
        return lax.dynamic_slice_in_dim(full, index * size, size, axis=dim)

    total = part(me).astype(jnp.float32)
    for steps in range(1, count):
        sent = part((me + steps) % count).astype(jnp.bfloat16)
        total = total + cyclic(sent, axis, steps).astype(jnp.float32)
    return total


def body(queries, key_states, value_states, valid_mask, out_weight, out_cotangent):
    tile_rows, tile_columns, tokens, features = queries.shape
    assert tile_rows == 1 and tile_columns == 1
    model_width = out_weight.shape[1]
    q = queries[0, 0]
    flag_rows = jnp.zeros((FLAG_ROWS, features), jnp.bfloat16)
    flag_rows = flag_rows.at[0, :tokens].set(valid_mask[0, 0].astype(jnp.bfloat16))
    packed = jnp.concatenate([key_states[0, 0], value_states[0, 0], flag_rows], axis=0)

    with jax.named_scope("halo_exchange"):
        column = jnp.stack([shifted(packed, "fh", 1), packed, shifted(packed, "fh", -1)])
        columns = (shifted(column, "wa", 1), column, shifted(column, "wa", -1))
    flags = jnp.concatenate([side[:, 2 * tokens, :tokens] for side in columns], axis=0)
    flags = flags.reshape(1, -1)
    mask = jnp.where(flags > 0, 0.0, MASKED / HD ** (-0.5)).astype(jnp.float32)

    with jax.named_scope("cotangent_gather"):
        cot_all = lax.all_gather(out_cotangent[0, 0], "ha", axis=0, tiled=True)

    with jax.named_scope("attention_forward"):
        attended, row_max, row_inverse = attention_forward(mask, q, columns)

    with jax.named_scope("output_projection"):
        projected = jnp.dot(attended, out_weight, preferred_element_type=jnp.float32)
        layer_out = lax.psum_scatter(
            projected.astype(jnp.bfloat16), "ha", scatter_dimension=0, tiled=True
        )

    with jax.named_scope("grad_attended"):
        grad_attended = lax.dot_general(
            cot_all, out_weight, (((1,), (1,)), ((), ())), preferred_element_type=jnp.float32
        ).astype(jnp.bfloat16)

    with jax.named_scope("grad_weight"):
        weight_part = lax.dot_general(
            cot_all, attended, (((0,), (0,)), ((), ())), preferred_element_type=jnp.float32
        )
        weight_own, weight_sent = scatter_parts(weight_part, "fh", 0)
        weight_own, weight_sent, grad_attended = lax.optimization_barrier(
            (weight_own, weight_sent, grad_attended)
        )
        weight_rows = scatter_finish(weight_own, weight_sent, "fh")

    with jax.named_scope("attention_backward"):
        grad_q, left, partials, right = attention_backward(
            mask, q, columns, attended, row_max, row_inverse, grad_attended
        )

    with jax.named_scope("grad_weight"):
        grad_weight = scatter_sum(weight_rows, "wa", 0)

    with jax.named_scope("halo_reduction"):
        middle = (
            partials
            + shifted(left, "wa", -1).astype(jnp.float32)
            + shifted(right, "wa", 1).astype(jnp.float32)
        )
        middle_sides = middle.astype(jnp.bfloat16)
        own = (
            middle[1]
            + shifted(middle_sides[0], "fh", -1).astype(jnp.float32)
            + shifted(middle_sides[2], "fh", 1).astype(jnp.float32)
        )
    grad_keys = own[:tokens].astype(jnp.bfloat16)
    grad_values = own[tokens:].astype(jnp.bfloat16)
    expand = lambda x: x[None, None]
    return (
        expand(layer_out),
        expand(grad_q),
        expand(grad_keys),
        expand(grad_values),
        grad_weight,
    )


def solution(mesh):
    return jax.shard_map(
        body,
        mesh=mesh,
        in_specs=(
            P("fh", "wa", None, "ha"),
            P("fh", "wa", None, "ha"),
            P("fh", "wa", None, "ha"),
            P("fh", "wa", None),
            P("ha", None),
            P("fh", "wa", "ha", None),
        ),
        out_specs=(
            P("fh", "wa", "ha", None),
            P("fh", "wa", None, "ha"),
            P("fh", "wa", None, "ha"),
            P("fh", "wa", None, "ha"),
            P(("fh", "wa"), "ha"),
        ),
        check_vma=False,
    )
```

```python
import functools

import jax
import jax.numpy as jnp
from jax import lax
from jax.experimental import pallas as pl
from jax.experimental.pallas import tpu as pltpu
from jax.sharding import PartitionSpec as P

HD = 128
MASKED = -1e30
FORWARD_CHUNK = 384
BACKWARD_CHUNK = 192
FLAG_ROWS = 16
LOG2E = 1.4426950408889634


def shift_pairs(count, steps):
    return [(source, source + steps) for source in range(count) if 0 <= source + steps < count]


def shifted(value, axis, steps):
    return lax.ppermute(value, axis, shift_pairs(lax.axis_size(axis), steps))


def cyclic(value, axis, steps):
    count = lax.axis_size(axis)
    return lax.ppermute(value, axis, [(i, (i + steps) % count) for i in range(count)])


def joined(refs):
    return jnp.concatenate([ref[...].reshape(-1, HD) for ref in refs], axis=0)


def raw_scores(mask_ref, q_ref, k):
    s = lax.dot_general(q_ref[...], k, (((1,), (1,)), ((), ())), preferred_element_type=jnp.float32)
    return s + mask_ref[...]


def forward_kernel(exp_scale, mask_ref, q_ref, kl, km, kr, vl, vm, vr, o_ref, m_ref, r_ref):
    s = raw_scores(mask_ref, q_ref, joined((kl, km, kr)))
    m = jnp.max(s, axis=1, keepdims=True)
    e = jnp.exp2((s - m) * exp_scale)
    inverse = 1.0 / jnp.sum(e, axis=1, keepdims=True)
    p = (e * inverse).astype(jnp.bfloat16)
    v = joined((vl, vm, vr))
    o_ref[...] = jnp.dot(p, v, preferred_element_type=jnp.float32).astype(o_ref.dtype)
    m_ref[...] = jnp.broadcast_to(m, m_ref.shape)
    r_ref[...] = jnp.broadcast_to(inverse, r_ref.shape)


def backward_kernel(
    scale, exp_scale, mask_ref, q_ref, kl, km, kr, vl, vm, vr, o_ref, m_ref, r_ref, do_ref,
    dq_ref, left_ref, mid_ref, right_ref, acc_ref
):
    chunk = pl.program_id(1)
    k = joined((kl, km, kr))
    v = joined((vl, vm, vr))
    s = raw_scores(mask_ref, q_ref, k)
    w = jnp.exp2((s - m_ref[:, :1]) * exp_scale) * r_ref[:, :1]
    p = w.astype(jnp.bfloat16)
    do = do_ref[...]
    row_dot = jnp.sum(
        do.astype(jnp.float32) * o_ref[...].astype(jnp.float32), axis=1, keepdims=True
    )
    dp = lax.dot_general(do, v, (((1,), (1,)), ((), ())), preferred_element_type=jnp.float32)
    ds = (w * (dp - row_dot)).astype(jnp.bfloat16)
    dq = jnp.dot(ds, k, preferred_element_type=jnp.float32) * scale
    dq_ref[...] = dq.astype(dq_ref.dtype)
    contract0 = (((0,), (0,)), ((), ()))
    dk = lax.dot_general(ds, q_ref[...], contract0, preferred_element_type=jnp.float32) * scale
    dv = lax.dot_general(p, do, contract0, preferred_element_type=jnp.float32)
    tiles, tokens = 3 * kl.shape[0], kl.shape[1]
    dk = dk.reshape(tiles, tokens, HD)
    dv = dv.reshape(tiles, tokens, HD)

    @pl.when(chunk == 0)
    def _():
        acc_ref[:, :tokens, :] = dk
        acc_ref[:, tokens:, :] = dv

    @pl.when(chunk > 0)
    def _():
        acc_ref[:, :tokens, :] += dk
        acc_ref[:, tokens:, :] += dv

    @pl.when(chunk == pl.num_programs(1) - 1)
    def _():
        third = tiles // 3
        left_ref[...] = acc_ref[:third].astype(left_ref.dtype)
        mid_ref[...] = acc_ref[third : 2 * third]
        right_ref[...] = acc_ref[2 * third :].astype(right_ref.dtype)


def attention_forward(mask, queries, columns):
    tokens, features = queries.shape
    tiles = 3 * columns[0].shape[0]
    heads = features // HD
    chunk = FORWARD_CHUNK
    chunks = tokens // chunk
    scale = HD ** (-0.5)
    return pl.pallas_call(
        functools.partial(forward_kernel, scale * LOG2E),
        grid=(heads, chunks),
        in_specs=[
            pl.BlockSpec((1, tiles * tokens), lambda h, c: (0, 0)),
            pl.BlockSpec((chunk, HD), lambda h, c: (c, h)),
            *[pl.BlockSpec((tiles // 3, tokens, HD), lambda h, c: (0, 0, h))] * 3,
            *[pl.BlockSpec((tiles // 3, tokens, HD), lambda h, c: (0, 1, h))] * 3,
        ],
        out_specs=[pl.BlockSpec((chunk, HD), lambda h, c: (c, h))] * 3,
        out_shape=[
            jax.ShapeDtypeStruct((tokens, features), jnp.bfloat16),
            jax.ShapeDtypeStruct((tokens, features), jnp.float32),
            jax.ShapeDtypeStruct((tokens, features), jnp.float32),
        ],
        name="tile_attention_forward",
    )(mask, queries, *columns, *columns)


def attention_backward(mask, queries, columns, attended, row_max, row_inverse, grad_attended):
    tokens, features = queries.shape
    tiles = 3 * columns[0].shape[0]
    heads = features // HD
    chunk = BACKWARD_CHUNK
    chunks = tokens // chunk
    scale = HD ** (-0.5)
    return pl.pallas_call(
        functools.partial(backward_kernel, scale, scale * LOG2E),
        grid=(heads, chunks),
        in_specs=[
            pl.BlockSpec((1, tiles * tokens), lambda h, c: (0, 0)),
            pl.BlockSpec((chunk, HD), lambda h, c: (c, h)),
            *[pl.BlockSpec((tiles // 3, tokens, HD), lambda h, c: (0, 0, h))] * 3,
            *[pl.BlockSpec((tiles // 3, tokens, HD), lambda h, c: (0, 1, h))] * 3,
            pl.BlockSpec((chunk, HD), lambda h, c: (c, h)),
            pl.BlockSpec((chunk, HD), lambda h, c: (c, h)),
            pl.BlockSpec((chunk, HD), lambda h, c: (c, h)),
            pl.BlockSpec((chunk, HD), lambda h, c: (c, h)),
        ],
        out_specs=[
            pl.BlockSpec((chunk, HD), lambda h, c: (c, h)),
            pl.BlockSpec((tiles // 3, 2 * tokens, HD), lambda h, c: (0, 0, h)),
            pl.BlockSpec((tiles // 3, 2 * tokens, HD), lambda h, c: (0, 0, h)),
            pl.BlockSpec((tiles // 3, 2 * tokens, HD), lambda h, c: (0, 0, h)),
        ],
        out_shape=[
            jax.ShapeDtypeStruct((tokens, features), jnp.bfloat16),
            jax.ShapeDtypeStruct((tiles // 3, 2 * tokens, features), jnp.bfloat16),
            jax.ShapeDtypeStruct((tiles // 3, 2 * tokens, features), jnp.float32),
            jax.ShapeDtypeStruct((tiles // 3, 2 * tokens, features), jnp.bfloat16),
        ],
        scratch_shapes=[pltpu.VMEM((tiles, 2 * tokens, HD), jnp.float32)],
        name="tile_attention_backward",
    )(mask, queries, *columns, *columns, attended, row_max, row_inverse, grad_attended)


def gather_over(piece, axis):
    count = lax.axis_size(axis)
    me = lax.axis_index(axis)
    received = [piece] + [cyclic(piece, axis, steps) for steps in range(1, count)]
    ordered = jnp.stack([received[(-k) % count] for k in range(count)])
    return jnp.roll(ordered, me, axis=0)


def scatter_parts(full, axis, dim):
    count = lax.axis_size(axis)
    me = lax.axis_index(axis)
    size = full.shape[dim] // count

    def part(index):
        return lax.dynamic_slice_in_dim(full, index * size, size, axis=dim)

    sent = [part((me + steps) % count).astype(jnp.bfloat16) for steps in range(1, count)]
    return part(me).astype(jnp.float32), sent


def scatter_finish(own, sent, axis):
    total = own
    for steps, piece in enumerate(sent, start=1):
        total = total + cyclic(piece, axis, steps).astype(jnp.float32)
    return total


def scatter_sum(full, axis, dim):
    count = lax.axis_size(axis)
    me = lax.axis_index(axis)
    size = full.shape[dim] // count

    def part(index):
        return lax.dynamic_slice_in_dim(full, index * size, size, axis=dim)

    total = part(me).astype(jnp.float32)
    for steps in range(1, count):
        sent = part((me + steps) % count).astype(jnp.bfloat16)
        total = total + cyclic(sent, axis, steps).astype(jnp.float32)
    return total


def body(queries, key_states, value_states, valid_mask, out_weight, out_cotangent):
    tile_rows, tile_columns, tokens, features = queries.shape
    assert tile_rows == 1 and tile_columns == 1
    model_width = out_weight.shape[1]
    q = queries[0, 0]
    flag_rows = jnp.zeros((FLAG_ROWS, features), jnp.bfloat16)
    flag_rows = flag_rows.at[0, :tokens].set(valid_mask[0, 0].astype(jnp.bfloat16))
    packed = jnp.concatenate([key_states[0, 0], value_states[0, 0], flag_rows], axis=0)

    with jax.named_scope("halo_exchange"):
        if lax.axis_size("fh") == 2:
            column = jnp.stack([cyclic(packed, "fh", 1), packed])
        else:
            column = jnp.stack([shifted(packed, "fh", 1), packed, shifted(packed, "fh", -1)])
        columns = (shifted(column, "wa", 1), column, shifted(column, "wa", -1))
    flags = jnp.concatenate([side[:, 2 * tokens, :tokens] for side in columns], axis=0)
    flags = flags.reshape(1, -1)
    mask = jnp.where(flags > 0, 0.0, MASKED / HD ** (-0.5)).astype(jnp.float32)

    with jax.named_scope("cotangent_gather"):
        cot_all = lax.all_gather(out_cotangent[0, 0], "ha", axis=0, tiled=True)

    with jax.named_scope("attention_forward"):
        attended, row_max, row_inverse = attention_forward(mask, q, columns)

    with jax.named_scope("output_projection"):
        projected = jnp.dot(attended, out_weight, preferred_element_type=jnp.float32)
        layer_out = lax.psum_scatter(
            projected.astype(jnp.bfloat16), "ha", scatter_dimension=0, tiled=True
        )

    with jax.named_scope("grad_attended"):
        grad_attended = lax.dot_general(
            cot_all, out_weight, (((1,), (1,)), ((), ())), preferred_element_type=jnp.float32
        ).astype(jnp.bfloat16)

    with jax.named_scope("grad_weight"):
        weight_part = lax.dot_general(
            cot_all, attended, (((0,), (0,)), ((), ())), preferred_element_type=jnp.float32
        )
        weight_own, weight_sent = scatter_parts(weight_part, "fh", 0)
        weight_own, weight_sent, grad_attended = lax.optimization_barrier(
            (weight_own, weight_sent, grad_attended)
        )
        weight_rows = scatter_finish(weight_own, weight_sent, "fh")

    with jax.named_scope("attention_backward"):
        grad_q, left, partials, right = attention_backward(
            mask, q, columns, attended, row_max, row_inverse, grad_attended
        )

    with jax.named_scope("grad_weight"):
        grad_weight = scatter_sum(weight_rows, "wa", 0)

    with jax.named_scope("halo_reduction"):
        middle = (
            partials
            + shifted(left, "wa", -1).astype(jnp.float32)
            + shifted(right, "wa", 1).astype(jnp.float32)
        )
        middle_sides = middle.astype(jnp.bfloat16)
        if lax.axis_size("fh") == 2:
            own = middle[1] + cyclic(middle_sides[0], "fh", 1).astype(jnp.float32)
        else:
            own = (
                middle[1]
                + shifted(middle_sides[0], "fh", -1).astype(jnp.float32)
                + shifted(middle_sides[2], "fh", 1).astype(jnp.float32)
            )
    grad_keys = own[:tokens].astype(jnp.bfloat16)
    grad_values = own[tokens:].astype(jnp.bfloat16)
    expand = lambda x: x[None, None]
    return (
        expand(layer_out),
        expand(grad_q),
        expand(grad_keys),
        expand(grad_values),
        grad_weight,
    )


def solution(mesh):
    return jax.shard_map(
        body,
        mesh=mesh,
        in_specs=(
            P("fh", "wa", None, "ha"),
            P("fh", "wa", None, "ha"),
            P("fh", "wa", None, "ha"),
            P("fh", "wa", None),
            P("ha", None),
            P("fh", "wa", "ha", None),
        ),
        out_specs=(
            P("fh", "wa", "ha", None),
            P("fh", "wa", None, "ha"),
            P("fh", "wa", None, "ha"),
            P("fh", "wa", None, "ha"),
            P(("fh", "wa"), "ha"),
        ),
        check_vma=False,
    )
```

```python
import functools

import jax
import jax.numpy as jnp
from jax import lax
from jax.experimental import pallas as pl
from jax.experimental.pallas import tpu as pltpu
from jax.sharding import PartitionSpec as P

HD = 128
MASKED = -1e30
FORWARD_CHUNK = 384
BACKWARD_CHUNK = 192
FLAG_ROWS = 16
LOG2E = 1.4426950408889634


def shift_pairs(count, steps):
    return [(source, source + steps) for source in range(count) if 0 <= source + steps < count]


def shifted(value, axis, steps):
    return lax.ppermute(value, axis, shift_pairs(lax.axis_size(axis), steps))


def partner(value, axis, bit):
    count = lax.axis_size(axis)
    return lax.ppermute(value, axis, [(i, i ^ bit) for i in range(count)])


def cyclic(value, axis, steps):
    count = lax.axis_size(axis)
    return lax.ppermute(value, axis, [(i, (i + steps) % count) for i in range(count)])


def joined(refs):
    return jnp.concatenate([ref[...].reshape(-1, HD) for ref in refs], axis=0)


def raw_scores(mask_ref, q_ref, k):
    s = lax.dot_general(q_ref[...], k, (((1,), (1,)), ((), ())), preferred_element_type=jnp.float32)
    return s + mask_ref[...]


def forward_kernel(exp_scale, mask_ref, q_ref, kl, km, kr, vl, vm, vr, o_ref, m_ref, r_ref):
    s = raw_scores(mask_ref, q_ref, joined((kl, km, kr)))
    m = jnp.max(s, axis=1, keepdims=True)
    e = jnp.exp2((s - m) * exp_scale)
    inverse = 1.0 / jnp.sum(e, axis=1, keepdims=True)
    p = (e * inverse).astype(jnp.bfloat16)
    v = joined((vl, vm, vr))
    o_ref[...] = jnp.dot(p, v, preferred_element_type=jnp.float32).astype(o_ref.dtype)
    m_ref[...] = jnp.broadcast_to(m, m_ref.shape)
    r_ref[...] = jnp.broadcast_to(inverse, r_ref.shape)


def backward_kernel(
    scale, exp_scale, mask_ref, q_ref, kl, km, kr, vl, vm, vr, o_ref, m_ref, r_ref, do_ref,
    dq_ref, left_ref, mid_ref, right_ref, acc_ref
):
    chunk = pl.program_id(1)
    k = joined((kl, km, kr))
    v = joined((vl, vm, vr))
    s = raw_scores(mask_ref, q_ref, k)
    w = jnp.exp2((s - m_ref[:, :1]) * exp_scale) * r_ref[:, :1]
    p = w.astype(jnp.bfloat16)
    do = do_ref[...]
    row_dot = jnp.sum(
        do.astype(jnp.float32) * o_ref[...].astype(jnp.float32), axis=1, keepdims=True
    )
    dp = lax.dot_general(do, v, (((1,), (1,)), ((), ())), preferred_element_type=jnp.float32)
    ds = (w * (dp - row_dot)).astype(jnp.bfloat16)
    dq = jnp.dot(ds, k, preferred_element_type=jnp.float32) * scale
    dq_ref[...] = dq.astype(dq_ref.dtype)
    contract0 = (((0,), (0,)), ((), ()))
    dk = lax.dot_general(ds, q_ref[...], contract0, preferred_element_type=jnp.float32) * scale
    dv = lax.dot_general(p, do, contract0, preferred_element_type=jnp.float32)
    tiles, tokens = 3 * kl.shape[0], kl.shape[1]
    dk = dk.reshape(tiles, tokens, HD)
    dv = dv.reshape(tiles, tokens, HD)

    @pl.when(chunk == 0)
    def _():
        acc_ref[:, :tokens, :] = dk
        acc_ref[:, tokens:, :] = dv

    @pl.when(chunk > 0)
    def _():
        acc_ref[:, :tokens, :] += dk
        acc_ref[:, tokens:, :] += dv

    @pl.when(chunk == pl.num_programs(1) - 1)
    def _():
        third = tiles // 3
        left_ref[...] = acc_ref[:third].astype(left_ref.dtype)
        mid_ref[...] = acc_ref[third : 2 * third]
        right_ref[...] = acc_ref[2 * third :].astype(right_ref.dtype)


def attention_forward(mask, queries, columns):
    tokens, features = queries.shape
    tiles = 3 * columns[0].shape[0]
    heads = features // HD
    chunk = FORWARD_CHUNK
    chunks = tokens // chunk
    scale = HD ** (-0.5)
    return pl.pallas_call(
        functools.partial(forward_kernel, scale * LOG2E),
        grid=(heads, chunks),
        in_specs=[
            pl.BlockSpec((1, tiles * tokens), lambda h, c: (0, 0)),
            pl.BlockSpec((chunk, HD), lambda h, c: (c, h)),
            *[pl.BlockSpec((tiles // 3, tokens, HD), lambda h, c: (0, 0, h))] * 3,
            *[pl.BlockSpec((tiles // 3, tokens, HD), lambda h, c: (0, 1, h))] * 3,
        ],
        out_specs=[pl.BlockSpec((chunk, HD), lambda h, c: (c, h))] * 3,
        out_shape=[
            jax.ShapeDtypeStruct((tokens, features), jnp.bfloat16),
            jax.ShapeDtypeStruct((tokens, features), jnp.float32),
            jax.ShapeDtypeStruct((tokens, features), jnp.float32),
        ],
        name="tile_attention_forward",
    )(mask, queries, *columns, *columns)


def attention_backward(mask, queries, columns, attended, row_max, row_inverse, grad_attended):
    tokens, features = queries.shape
    tiles = 3 * columns[0].shape[0]
    heads = features // HD
    chunk = BACKWARD_CHUNK
    chunks = tokens // chunk
    scale = HD ** (-0.5)
    return pl.pallas_call(
        functools.partial(backward_kernel, scale, scale * LOG2E),
        grid=(heads, chunks),
        in_specs=[
            pl.BlockSpec((1, tiles * tokens), lambda h, c: (0, 0)),
            pl.BlockSpec((chunk, HD), lambda h, c: (c, h)),
            *[pl.BlockSpec((tiles // 3, tokens, HD), lambda h, c: (0, 0, h))] * 3,
            *[pl.BlockSpec((tiles // 3, tokens, HD), lambda h, c: (0, 1, h))] * 3,
            pl.BlockSpec((chunk, HD), lambda h, c: (c, h)),
            pl.BlockSpec((chunk, HD), lambda h, c: (c, h)),
            pl.BlockSpec((chunk, HD), lambda h, c: (c, h)),
            pl.BlockSpec((chunk, HD), lambda h, c: (c, h)),
        ],
        out_specs=[
            pl.BlockSpec((chunk, HD), lambda h, c: (c, h)),
            pl.BlockSpec((tiles // 3, 2 * tokens, HD), lambda h, c: (0, 0, h)),
            pl.BlockSpec((tiles // 3, 2 * tokens, HD), lambda h, c: (0, 0, h)),
            pl.BlockSpec((tiles // 3, 2 * tokens, HD), lambda h, c: (0, 0, h)),
        ],
        out_shape=[
            jax.ShapeDtypeStruct((tokens, features), jnp.bfloat16),
            jax.ShapeDtypeStruct((tiles // 3, 2 * tokens, features), jnp.bfloat16),
            jax.ShapeDtypeStruct((tiles // 3, 2 * tokens, features), jnp.float32),
            jax.ShapeDtypeStruct((tiles // 3, 2 * tokens, features), jnp.bfloat16),
        ],
        scratch_shapes=[pltpu.VMEM((tiles, 2 * tokens, HD), jnp.float32)],
        name="tile_attention_backward",
    )(mask, queries, *columns, *columns, attended, row_max, row_inverse, grad_attended)


def gather_over(piece, axis):
    count = lax.axis_size(axis)
    me = lax.axis_index(axis)
    received = [piece] + [cyclic(piece, axis, steps) for steps in range(1, count)]
    ordered = jnp.stack([received[(-k) % count] for k in range(count)])
    return jnp.roll(ordered, me, axis=0)


def scatter_parts(full, axis, dim):
    count = lax.axis_size(axis)
    me = lax.axis_index(axis)
    size = full.shape[dim] // count

    def part(index):
        return lax.dynamic_slice_in_dim(full, index * size, size, axis=dim)

    sent = [part((me + steps) % count).astype(jnp.bfloat16) for steps in range(1, count)]
    return part(me).astype(jnp.float32), sent


def scatter_finish(own, sent, axis):
    total = own
    for steps, piece in enumerate(sent, start=1):
        total = total + cyclic(piece, axis, steps).astype(jnp.float32)
    return total


def scatter_sum(full, axis, dim):
    count = lax.axis_size(axis)
    me = lax.axis_index(axis)
    size = full.shape[dim] // count

    def part(index):
        return lax.dynamic_slice_in_dim(full, index * size, size, axis=dim)

    total = part(me).astype(jnp.float32)
    for steps in range(1, count):
        sent = part((me + steps) % count).astype(jnp.bfloat16)
        total = total + cyclic(sent, axis, steps).astype(jnp.float32)
    return total


def body(queries, key_states, value_states, valid_mask, out_weight, out_cotangent):
    tile_rows, tile_columns, tokens, features = queries.shape
    assert tile_rows == 1 and tile_columns == 1
    model_width = out_weight.shape[1]
    q = queries[0, 0]
    flag_rows = jnp.zeros((FLAG_ROWS, features), jnp.bfloat16)
    flag_rows = flag_rows.at[0, :tokens].set(valid_mask[0, 0].astype(jnp.bfloat16))
    packed = jnp.concatenate([key_states[0, 0], value_states[0, 0], flag_rows], axis=0)

    with jax.named_scope("halo_exchange"):
        if lax.axis_size("fh") == 2:
            column = jnp.stack([cyclic(packed, "fh", 1), packed])
        else:
            column = jnp.stack([shifted(packed, "fh", 1), packed, shifted(packed, "fh", -1)])
        columns = (shifted(column, "wa", 1), column, shifted(column, "wa", -1))
    flags = jnp.concatenate([side[:, 2 * tokens, :tokens] for side in columns], axis=0)
    flags = flags.reshape(1, -1)
    mask = jnp.where(flags > 0, 0.0, MASKED / HD ** (-0.5)).astype(jnp.float32)

    with jax.named_scope("cotangent_gather"):
        cot_all = lax.all_gather(out_cotangent[0, 0], "ha", axis=0, tiled=True)

    with jax.named_scope("attention_forward"):
        attended, row_max, row_inverse = attention_forward(mask, q, columns)

    with jax.named_scope("output_projection"):
        projected = jnp.dot(attended, out_weight, preferred_element_type=jnp.float32)
        layer_out = lax.psum_scatter(
            projected.astype(jnp.bfloat16), "ha", scatter_dimension=0, tiled=True
        )

    with jax.named_scope("grad_attended"):
        grad_attended = lax.dot_general(
            cot_all, out_weight, (((1,), (1,)), ((), ())), preferred_element_type=jnp.float32
        ).astype(jnp.bfloat16)

    halving = lax.axis_size("fh") == 2 and lax.axis_size("wa") == 4
    with jax.named_scope("grad_weight"):
        if halving:
            rows = model_width // 8
            cot_blocks = cot_all.reshape(-1, 2, 2, 2, rows)
            weight_blocks = lax.dot_general(
                cot_blocks, attended, (((0,), (0,)), ((), ())), preferred_element_type=jnp.float32
            )
            weight_blocks = jnp.transpose(weight_blocks, (2, 1, 0, 3, 4))
            core = lax.axis_index("wa") % 2
            weight_own = lax.dynamic_index_in_dim(weight_blocks, core, 0, keepdims=False)
            weight_sent = lax.dynamic_index_in_dim(weight_blocks, 1 - core, 0, keepdims=False)
            weight_sent = weight_sent.astype(jnp.bfloat16)
            weight_own, weight_sent, grad_attended = lax.optimization_barrier(
                (weight_own, weight_sent, grad_attended)
            )
            weight_x = weight_own + partner(weight_sent, "wa", 1).astype(jnp.float32)
        else:
            weight_part = lax.dot_general(
                cot_all, attended, (((0,), (0,)), ((), ())), preferred_element_type=jnp.float32
            )
            weight_own, weight_sent = scatter_parts(weight_part, "fh", 0)
            weight_own, weight_sent, grad_attended = lax.optimization_barrier(
                (weight_own, weight_sent, grad_attended)
            )
            weight_rows = scatter_finish(weight_own, weight_sent, "fh")

    with jax.named_scope("attention_backward"):
        grad_q, left, partials, right = attention_backward(
            mask, q, columns, attended, row_max, row_inverse, grad_attended
        )

    with jax.named_scope("grad_weight"):
        if halving:
            column = lax.axis_index("wa") // 2
            kept = lax.dynamic_index_in_dim(weight_x, column, 0, keepdims=False)
            sent = lax.dynamic_index_in_dim(weight_x, 1 - column, 0, keepdims=False)
            weight_f = kept + partner(sent.astype(jnp.bfloat16), "wa", 2).astype(jnp.float32)
            row = lax.axis_index("fh")
            kept = lax.dynamic_index_in_dim(weight_f, row, 0, keepdims=False)
            sent = lax.dynamic_index_in_dim(weight_f, 1 - row, 0, keepdims=False)
            grad_weight = kept + partner(sent.astype(jnp.bfloat16), "fh", 1).astype(jnp.float32)
        else:
            grad_weight = scatter_sum(weight_rows, "wa", 0)

    with jax.named_scope("halo_reduction"):
        middle = (
            partials
            + shifted(left, "wa", -1).astype(jnp.float32)
            + shifted(right, "wa", 1).astype(jnp.float32)
        )
        middle_sides = middle.astype(jnp.bfloat16)
        if lax.axis_size("fh") == 2:
            own = middle[1] + cyclic(middle_sides[0], "fh", 1).astype(jnp.float32)
        else:
            own = (
                middle[1]
                + shifted(middle_sides[0], "fh", -1).astype(jnp.float32)
                + shifted(middle_sides[2], "fh", 1).astype(jnp.float32)
            )
    grad_keys = own[:tokens].astype(jnp.bfloat16)
    grad_values = own[tokens:].astype(jnp.bfloat16)
    expand = lambda x: x[None, None]
    return (
        expand(layer_out),
        expand(grad_q),
        expand(grad_keys),
        expand(grad_values),
        grad_weight,
    )


def solution(mesh):
    return jax.shard_map(
        body,
        mesh=mesh,
        in_specs=(
            P("fh", "wa", None, "ha"),
            P("fh", "wa", None, "ha"),
            P("fh", "wa", None, "ha"),
            P("fh", "wa", None),
            P("ha", None),
            P("fh", "wa", "ha", None),
        ),
        out_specs=(
            P("fh", "wa", "ha", None),
            P("fh", "wa", None, "ha"),
            P("fh", "wa", None, "ha"),
            P("fh", "wa", None, "ha"),
            P(("fh", "wa"), "ha"),
        ),
        check_vma=False,
    )
```

```python
import functools

import jax
import jax.numpy as jnp
from jax import lax
from jax.experimental import pallas as pl
from jax.experimental.pallas import tpu as pltpu
from jax.sharding import PartitionSpec as P

HD = 128
MASKED = -1e30
FORWARD_CHUNK = 384
BACKWARD_CHUNK = 192
FLAG_ROWS = 16
LOG2E = 1.4426950408889634


def shift_pairs(count, steps):
    return [(source, source + steps) for source in range(count) if 0 <= source + steps < count]


def shifted(value, axis, steps):
    return lax.ppermute(value, axis, shift_pairs(lax.axis_size(axis), steps))


def partner(value, axis, bit):
    count = lax.axis_size(axis)
    return lax.ppermute(value, axis, [(i, i ^ bit) for i in range(count)])


def cyclic(value, axis, steps):
    count = lax.axis_size(axis)
    return lax.ppermute(value, axis, [(i, (i + steps) % count) for i in range(count)])


def joined(refs):
    return jnp.concatenate([ref[...].reshape(-1, HD) for ref in refs], axis=0)


def raw_scores(mask_ref, q_ref, k):
    s = lax.dot_general(q_ref[...], k, (((1,), (1,)), ((), ())), preferred_element_type=jnp.float32)
    return s + mask_ref[...]


def forward_kernel(exp_scale, mask_ref, q_ref, kl, km, kr, vl, vm, vr, o_ref, m_ref, r_ref):
    s = raw_scores(mask_ref, q_ref, joined((kl, km, kr)))
    m = jnp.max(s, axis=1, keepdims=True)
    e = jnp.exp2((s - m) * exp_scale)
    inverse = 1.0 / jnp.sum(e, axis=1, keepdims=True)
    p = (e * inverse).astype(jnp.bfloat16)
    v = joined((vl, vm, vr))
    o_ref[...] = jnp.dot(p, v, preferred_element_type=jnp.float32).astype(o_ref.dtype)
    m_ref[...] = jnp.broadcast_to(m, m_ref.shape)
    r_ref[...] = jnp.broadcast_to(inverse, r_ref.shape)


def backward_kernel(
    scale, exp_scale, mask_ref, q_ref, kl, km, kr, vl, vm, vr, o_ref, m_ref, r_ref, do_ref,
    dq_ref, left_ref, mid_ref, right_ref, acc_ref
):
    chunk = pl.program_id(1)
    k = joined((kl, km, kr))
    v = joined((vl, vm, vr))
    s = raw_scores(mask_ref, q_ref, k)
    w = jnp.exp2((s - m_ref[:, :1]) * exp_scale) * r_ref[:, :1]
    p = w.astype(jnp.bfloat16)
    do = do_ref[...]
    row_dot = jnp.sum(
        do.astype(jnp.float32) * o_ref[...].astype(jnp.float32), axis=1, keepdims=True
    )
    dp = lax.dot_general(do, v, (((1,), (1,)), ((), ())), preferred_element_type=jnp.float32)
    ds = (w * (dp - row_dot)).astype(jnp.bfloat16)
    dq = jnp.dot(ds, k, preferred_element_type=jnp.float32) * scale
    dq_ref[...] = dq.astype(dq_ref.dtype)
    contract0 = (((0,), (0,)), ((), ()))
    dk = lax.dot_general(ds, q_ref[...], contract0, preferred_element_type=jnp.float32) * scale
    dv = lax.dot_general(p, do, contract0, preferred_element_type=jnp.float32)
    tiles, tokens = 3 * kl.shape[0], kl.shape[1]
    dk = dk.reshape(tiles, tokens, HD)
    dv = dv.reshape(tiles, tokens, HD)

    @pl.when(chunk == 0)
    def _():
        acc_ref[:, :tokens, :] = dk
        acc_ref[:, tokens:, :] = dv

    @pl.when(chunk > 0)
    def _():
        acc_ref[:, :tokens, :] += dk
        acc_ref[:, tokens:, :] += dv

    @pl.when(chunk == pl.num_programs(1) - 1)
    def _():
        third = tiles // 3
        left_ref[...] = acc_ref[:third].astype(left_ref.dtype)
        mid_ref[...] = acc_ref[third : 2 * third]
        right_ref[...] = acc_ref[2 * third :].astype(right_ref.dtype)


def attention_forward(mask, queries, columns):
    tokens, features = queries.shape
    tiles = 3 * columns[0].shape[0]
    heads = features // HD
    chunk = FORWARD_CHUNK
    chunks = tokens // chunk
    scale = HD ** (-0.5)
    return pl.pallas_call(
        functools.partial(forward_kernel, scale * LOG2E),
        grid=(heads, chunks),
        in_specs=[
            pl.BlockSpec((1, tiles * tokens), lambda h, c: (0, 0)),
            pl.BlockSpec((chunk, HD), lambda h, c: (c, h)),
            *[pl.BlockSpec((tiles // 3, tokens, HD), lambda h, c: (0, 0, h))] * 3,
            *[pl.BlockSpec((tiles // 3, tokens, HD), lambda h, c: (0, 1, h))] * 3,
        ],
        out_specs=[pl.BlockSpec((chunk, HD), lambda h, c: (c, h))] * 3,
        out_shape=[
            jax.ShapeDtypeStruct((tokens, features), jnp.bfloat16),
            jax.ShapeDtypeStruct((tokens, features), jnp.float32),
            jax.ShapeDtypeStruct((tokens, features), jnp.float32),
        ],
        name="tile_attention_forward",
    )(mask, queries, *columns, *columns)


def attention_backward(mask, queries, columns, attended, row_max, row_inverse, grad_attended):
    tokens, features = queries.shape
    tiles = 3 * columns[0].shape[0]
    heads = features // HD
    chunk = BACKWARD_CHUNK
    chunks = tokens // chunk
    scale = HD ** (-0.5)
    return pl.pallas_call(
        functools.partial(backward_kernel, scale, scale * LOG2E),
        grid=(heads, chunks),
        in_specs=[
            pl.BlockSpec((1, tiles * tokens), lambda h, c: (0, 0)),
            pl.BlockSpec((chunk, HD), lambda h, c: (c, h)),
            *[pl.BlockSpec((tiles // 3, tokens, HD), lambda h, c: (0, 0, h))] * 3,
            *[pl.BlockSpec((tiles // 3, tokens, HD), lambda h, c: (0, 1, h))] * 3,
            pl.BlockSpec((chunk, HD), lambda h, c: (c, h)),
            pl.BlockSpec((chunk, HD), lambda h, c: (c, h)),
            pl.BlockSpec((chunk, HD), lambda h, c: (c, h)),
            pl.BlockSpec((chunk, HD), lambda h, c: (c, h)),
        ],
        out_specs=[
            pl.BlockSpec((chunk, HD), lambda h, c: (c, h)),
            pl.BlockSpec((tiles // 3, 2 * tokens, HD), lambda h, c: (0, 0, h)),
            pl.BlockSpec((tiles // 3, 2 * tokens, HD), lambda h, c: (0, 0, h)),
            pl.BlockSpec((tiles // 3, 2 * tokens, HD), lambda h, c: (0, 0, h)),
        ],
        out_shape=[
            jax.ShapeDtypeStruct((tokens, features), jnp.bfloat16),
            jax.ShapeDtypeStruct((tiles // 3, 2 * tokens, features), jnp.bfloat16),
            jax.ShapeDtypeStruct((tiles // 3, 2 * tokens, features), jnp.float32),
            jax.ShapeDtypeStruct((tiles // 3, 2 * tokens, features), jnp.bfloat16),
        ],
        scratch_shapes=[pltpu.VMEM((tiles, 2 * tokens, HD), jnp.float32)],
        name="tile_attention_backward",
    )(mask, queries, *columns, *columns, attended, row_max, row_inverse, grad_attended)


def gather_over(piece, axis):
    count = lax.axis_size(axis)
    me = lax.axis_index(axis)
    received = [piece] + [cyclic(piece, axis, steps) for steps in range(1, count)]
    ordered = jnp.stack([received[(-k) % count] for k in range(count)])
    return jnp.roll(ordered, me, axis=0)


def scatter_parts(full, axis, dim):
    count = lax.axis_size(axis)
    me = lax.axis_index(axis)
    size = full.shape[dim] // count

    def part(index):
        return lax.dynamic_slice_in_dim(full, index * size, size, axis=dim)

    sent = [part((me + steps) % count).astype(jnp.bfloat16) for steps in range(1, count)]
    return part(me).astype(jnp.float32), sent


def scatter_finish(own, sent, axis):
    total = own
    for steps, piece in enumerate(sent, start=1):
        total = total + cyclic(piece, axis, steps).astype(jnp.float32)
    return total


def scatter_sum(full, axis, dim):
    count = lax.axis_size(axis)
    me = lax.axis_index(axis)
    size = full.shape[dim] // count

    def part(index):
        return lax.dynamic_slice_in_dim(full, index * size, size, axis=dim)

    total = part(me).astype(jnp.float32)
    for steps in range(1, count):
        sent = part((me + steps) % count).astype(jnp.bfloat16)
        total = total + cyclic(sent, axis, steps).astype(jnp.float32)
    return total


def body(queries, key_states, value_states, valid_mask, out_weight, out_cotangent):
    tile_rows, tile_columns, tokens, features = queries.shape
    assert tile_rows == 1 and tile_columns == 1
    model_width = out_weight.shape[1]
    q = queries[0, 0]
    flag_rows = jnp.zeros((FLAG_ROWS, features), jnp.bfloat16)
    flag_rows = flag_rows.at[0, :tokens].set(valid_mask[0, 0].astype(jnp.bfloat16))
    packed = jnp.concatenate([key_states[0, 0], value_states[0, 0], flag_rows], axis=0)

    with jax.named_scope("halo_exchange"):
        if lax.axis_size("fh") == 2:
            column = jnp.stack([cyclic(packed, "fh", 1), packed])
        else:
            column = jnp.stack([shifted(packed, "fh", 1), packed, shifted(packed, "fh", -1)])
        columns = (shifted(column, "wa", 1), column, shifted(column, "wa", -1))
    flags = jnp.concatenate([side[:, 2 * tokens, :tokens] for side in columns], axis=0)
    flags = flags.reshape(1, -1)
    mask = jnp.where(flags > 0, 0.0, MASKED / HD ** (-0.5)).astype(jnp.float32)

    with jax.named_scope("cotangent_gather"):
        cot_all = lax.all_gather(out_cotangent[0, 0], "ha", axis=0, tiled=True)

    with jax.named_scope("attention_forward"):
        attended, row_max, row_inverse = attention_forward(mask, q, columns)

    with jax.named_scope("output_projection"):
        projected = jnp.dot(attended, out_weight, preferred_element_type=jnp.float32)
        layer_out = lax.psum_scatter(
            projected.astype(jnp.bfloat16), "ha", scatter_dimension=0, tiled=True
        )

    with jax.named_scope("grad_attended"):
        grad_attended = lax.dot_general(
            cot_all, out_weight, (((1,), (1,)), ((), ())), preferred_element_type=jnp.float32
        ).astype(jnp.bfloat16)

    halving = lax.axis_size("fh") == 2 and lax.axis_size("wa") == 4
    with jax.named_scope("grad_weight"):
        if halving:
            rows = model_width // 8
            cot_blocks = jnp.transpose(cot_all.reshape(-1, 2, 2, 2, rows), (0, 3, 2, 1, 4))
            weight_blocks = lax.dot_general(
                cot_blocks, attended, (((0,), (0,)), ((), ())), preferred_element_type=jnp.float32
            )
            core = lax.axis_index("wa") % 2
            weight_own = lax.dynamic_index_in_dim(weight_blocks, core, 0, keepdims=False)
            weight_sent = lax.dynamic_index_in_dim(weight_blocks, 1 - core, 0, keepdims=False)
            weight_sent = weight_sent.astype(jnp.bfloat16)
            weight_x = weight_own + partner(weight_sent, "wa", 1).astype(jnp.float32)
            column = lax.axis_index("wa") // 2
            kept = lax.dynamic_index_in_dim(weight_x, column, 0, keepdims=False)
            sent = lax.dynamic_index_in_dim(weight_x, 1 - column, 0, keepdims=False)
            kept, sent, grad_attended = lax.optimization_barrier(
                (kept, sent.astype(jnp.bfloat16), grad_attended)
            )
            weight_f = kept + partner(sent, "wa", 2).astype(jnp.float32)
        else:
            weight_part = lax.dot_general(
                cot_all, attended, (((0,), (0,)), ((), ())), preferred_element_type=jnp.float32
            )
            weight_own, weight_sent = scatter_parts(weight_part, "fh", 0)
            weight_own, weight_sent, grad_attended = lax.optimization_barrier(
                (weight_own, weight_sent, grad_attended)
            )
            weight_rows = scatter_finish(weight_own, weight_sent, "fh")

    with jax.named_scope("attention_backward"):
        grad_q, left, partials, right = attention_backward(
            mask, q, columns, attended, row_max, row_inverse, grad_attended
        )

    with jax.named_scope("grad_weight"):
        if halving:
            row = lax.axis_index("fh")
            kept = lax.dynamic_index_in_dim(weight_f, row, 0, keepdims=False)
            sent = lax.dynamic_index_in_dim(weight_f, 1 - row, 0, keepdims=False)
            grad_weight = kept + partner(sent.astype(jnp.bfloat16), "fh", 1).astype(jnp.float32)
        else:
            grad_weight = scatter_sum(weight_rows, "wa", 0)

    with jax.named_scope("halo_reduction"):
        middle = (
            partials
            + shifted(left, "wa", -1).astype(jnp.float32)
            + shifted(right, "wa", 1).astype(jnp.float32)
        )
        middle_sides = middle.astype(jnp.bfloat16)
        if lax.axis_size("fh") == 2:
            own = middle[1] + cyclic(middle_sides[0], "fh", 1).astype(jnp.float32)
        else:
            own = (
                middle[1]
                + shifted(middle_sides[0], "fh", -1).astype(jnp.float32)
                + shifted(middle_sides[2], "fh", 1).astype(jnp.float32)
            )
    grad_keys = own[:tokens].astype(jnp.bfloat16)
    grad_values = own[tokens:].astype(jnp.bfloat16)
    expand = lambda x: x[None, None]
    return (
        expand(layer_out),
        expand(grad_q),
        expand(grad_keys),
        expand(grad_values),
        grad_weight,
    )


def solution(mesh):
    return jax.shard_map(
        body,
        mesh=mesh,
        in_specs=(
            P("fh", "wa", None, "ha"),
            P("fh", "wa", None, "ha"),
            P("fh", "wa", None, "ha"),
            P("fh", "wa", None),
            P("ha", None),
            P("fh", "wa", "ha", None),
        ),
        out_specs=(
            P("fh", "wa", "ha", None),
            P("fh", "wa", None, "ha"),
            P("fh", "wa", None, "ha"),
            P("fh", "wa", None, "ha"),
            P(("fh", "wa"), "ha"),
        ),
        check_vma=False,
    )
```

```python
import functools

import jax
import jax.numpy as jnp
from jax import lax
from jax.experimental import pallas as pl
from jax.experimental.pallas import tpu as pltpu
from jax.sharding import PartitionSpec as P

HD = 128
MASKED = -1e30
FORWARD_CHUNK = 384
BACKWARD_CHUNK = 192
FLAG_ROWS = 16
LOG2E = 1.4426950408889634


def shift_pairs(count, steps):
    return [(source, source + steps) for source in range(count) if 0 <= source + steps < count]


def shifted(value, axis, steps):
    return lax.ppermute(value, axis, shift_pairs(lax.axis_size(axis), steps))


def partner(value, axis, bit):
    count = lax.axis_size(axis)
    return lax.ppermute(value, axis, [(i, i ^ bit) for i in range(count)])


def cyclic(value, axis, steps):
    count = lax.axis_size(axis)
    return lax.ppermute(value, axis, [(i, (i + steps) % count) for i in range(count)])


def joined(refs):
    return jnp.concatenate([ref[...].reshape(-1, HD) for ref in refs], axis=0)


def raw_scores(mask_ref, q_ref, k):
    s = lax.dot_general(q_ref[...], k, (((1,), (1,)), ((), ())), preferred_element_type=jnp.float32)
    return s + mask_ref[...]


def forward_kernel(exp_scale, mask_ref, q_ref, kl, km, kr, vl, vm, vr, o_ref, m_ref, r_ref):
    s = raw_scores(mask_ref, q_ref, joined((kl, km, kr)))
    m = jnp.max(s, axis=1, keepdims=True)
    e = jnp.exp2((s - m) * exp_scale)
    inverse = 1.0 / jnp.sum(e, axis=1, keepdims=True)
    p = (e * inverse).astype(jnp.bfloat16)
    v = joined((vl, vm, vr))
    o_ref[...] = jnp.dot(p, v, preferred_element_type=jnp.float32).astype(o_ref.dtype)
    m_ref[...] = jnp.broadcast_to(m, m_ref.shape)
    r_ref[...] = jnp.broadcast_to(inverse, r_ref.shape)


def backward_kernel(
    scale, exp_scale, mask_ref, q_ref, kl, km, kr, vl, vm, vr, o_ref, m_ref, r_ref, do_ref,
    dq_ref, left_ref, mid_ref, right_ref, acc_ref
):
    chunk = pl.program_id(1)
    k = joined((kl, km, kr))
    v = joined((vl, vm, vr))
    s = raw_scores(mask_ref, q_ref, k)
    w = jnp.exp2((s - m_ref[:, :1]) * exp_scale) * r_ref[:, :1]
    p = w.astype(jnp.bfloat16)
    do = do_ref[...]
    row_dot = jnp.sum(
        do.astype(jnp.float32) * o_ref[...].astype(jnp.float32), axis=1, keepdims=True
    )
    dp = lax.dot_general(do, v, (((1,), (1,)), ((), ())), preferred_element_type=jnp.float32)
    ds = (w * (dp - row_dot)).astype(jnp.bfloat16)
    dq = jnp.dot(ds, k, preferred_element_type=jnp.float32) * scale
    dq_ref[...] = dq.astype(dq_ref.dtype)
    contract0 = (((0,), (0,)), ((), ()))
    dk = lax.dot_general(ds, q_ref[...], contract0, preferred_element_type=jnp.float32) * scale
    dv = lax.dot_general(p, do, contract0, preferred_element_type=jnp.float32)
    tiles, tokens = 3 * kl.shape[0], kl.shape[1]
    dk = dk.reshape(tiles, tokens, HD)
    dv = dv.reshape(tiles, tokens, HD)

    @pl.when(chunk == 0)
    def _():
        acc_ref[:, :tokens, :] = dk
        acc_ref[:, tokens:, :] = dv

    @pl.when(chunk > 0)
    def _():
        acc_ref[:, :tokens, :] += dk
        acc_ref[:, tokens:, :] += dv

    @pl.when(chunk == pl.num_programs(1) - 1)
    def _():
        third = tiles // 3
        left_ref[...] = acc_ref[:third].astype(left_ref.dtype)
        mid_ref[...] = acc_ref[third : 2 * third]
        right_ref[...] = acc_ref[2 * third :].astype(right_ref.dtype)


def attention_forward(mask, queries, columns):
    tokens, features = queries.shape
    tiles = 3 * columns[0].shape[0]
    heads = features // HD
    chunk = FORWARD_CHUNK
    chunks = tokens // chunk
    scale = HD ** (-0.5)
    return pl.pallas_call(
        functools.partial(forward_kernel, scale * LOG2E),
        grid=(heads, chunks),
        in_specs=[
            pl.BlockSpec((1, tiles * tokens), lambda h, c: (0, 0)),
            pl.BlockSpec((chunk, HD), lambda h, c: (c, h)),
            *[pl.BlockSpec((tiles // 3, tokens, HD), lambda h, c: (0, 0, h))] * 3,
            *[pl.BlockSpec((tiles // 3, tokens, HD), lambda h, c: (0, 1, h))] * 3,
        ],
        out_specs=[pl.BlockSpec((chunk, HD), lambda h, c: (c, h))] * 3,
        out_shape=[
            jax.ShapeDtypeStruct((tokens, features), jnp.bfloat16),
            jax.ShapeDtypeStruct((tokens, features), jnp.float32),
            jax.ShapeDtypeStruct((tokens, features), jnp.float32),
        ],
        name="tile_attention_forward",
    )(mask, queries, *columns, *columns)


def attention_backward(mask, queries, columns, attended, row_max, row_inverse, grad_attended):
    tokens, features = queries.shape
    tiles = 3 * columns[0].shape[0]
    heads = features // HD
    chunk = BACKWARD_CHUNK
    chunks = tokens // chunk
    scale = HD ** (-0.5)
    return pl.pallas_call(
        functools.partial(backward_kernel, scale, scale * LOG2E),
        grid=(heads, chunks),
        in_specs=[
            pl.BlockSpec((1, tiles * tokens), lambda h, c: (0, 0)),
            pl.BlockSpec((chunk, HD), lambda h, c: (c, h)),
            *[pl.BlockSpec((tiles // 3, tokens, HD), lambda h, c: (0, 0, h))] * 3,
            *[pl.BlockSpec((tiles // 3, tokens, HD), lambda h, c: (0, 1, h))] * 3,
            pl.BlockSpec((chunk, HD), lambda h, c: (c, h)),
            pl.BlockSpec((chunk, HD), lambda h, c: (c, h)),
            pl.BlockSpec((chunk, HD), lambda h, c: (c, h)),
            pl.BlockSpec((chunk, HD), lambda h, c: (c, h)),
        ],
        out_specs=[
            pl.BlockSpec((chunk, HD), lambda h, c: (c, h)),
            pl.BlockSpec((tiles // 3, 2 * tokens, HD), lambda h, c: (0, 0, h)),
            pl.BlockSpec((tiles // 3, 2 * tokens, HD), lambda h, c: (0, 0, h)),
            pl.BlockSpec((tiles // 3, 2 * tokens, HD), lambda h, c: (0, 0, h)),
        ],
        out_shape=[
            jax.ShapeDtypeStruct((tokens, features), jnp.bfloat16),
            jax.ShapeDtypeStruct((tiles // 3, 2 * tokens, features), jnp.bfloat16),
            jax.ShapeDtypeStruct((tiles // 3, 2 * tokens, features), jnp.float32),
            jax.ShapeDtypeStruct((tiles // 3, 2 * tokens, features), jnp.bfloat16),
        ],
        scratch_shapes=[pltpu.VMEM((tiles, 2 * tokens, HD), jnp.float32)],
        name="tile_attention_backward",
    )(mask, queries, *columns, *columns, attended, row_max, row_inverse, grad_attended)


def gather_over(piece, axis):
    count = lax.axis_size(axis)
    me = lax.axis_index(axis)
    received = [piece] + [cyclic(piece, axis, steps) for steps in range(1, count)]
    ordered = jnp.stack([received[(-k) % count] for k in range(count)])
    return jnp.roll(ordered, me, axis=0)


def scatter_parts(full, axis, dim):
    count = lax.axis_size(axis)
    me = lax.axis_index(axis)
    size = full.shape[dim] // count

    def part(index):
        return lax.dynamic_slice_in_dim(full, index * size, size, axis=dim)

    sent = [part((me + steps) % count).astype(jnp.bfloat16) for steps in range(1, count)]
    return part(me).astype(jnp.float32), sent


def scatter_finish(own, sent, axis):
    total = own
    for steps, piece in enumerate(sent, start=1):
        total = total + cyclic(piece, axis, steps).astype(jnp.float32)
    return total


def scatter_sum(full, axis, dim):
    count = lax.axis_size(axis)
    me = lax.axis_index(axis)
    size = full.shape[dim] // count

    def part(index):
        return lax.dynamic_slice_in_dim(full, index * size, size, axis=dim)

    total = part(me).astype(jnp.float32)
    for steps in range(1, count):
        sent = part((me + steps) % count).astype(jnp.bfloat16)
        total = total + cyclic(sent, axis, steps).astype(jnp.float32)
    return total


def body(queries, key_states, value_states, valid_mask, out_weight, out_cotangent):
    tile_rows, tile_columns, tokens, features = queries.shape
    assert tile_rows == 1 and tile_columns == 1
    model_width = out_weight.shape[1]
    q = queries[0, 0]
    flag_rows = jnp.zeros((FLAG_ROWS, features), jnp.bfloat16)
    flag_rows = flag_rows.at[0, :tokens].set(valid_mask[0, 0].astype(jnp.bfloat16))
    packed = jnp.concatenate([key_states[0, 0], value_states[0, 0], flag_rows], axis=0)

    with jax.named_scope("halo_exchange"):
        if lax.axis_size("fh") == 2:
            column = jnp.stack([cyclic(packed, "fh", 1), packed])
        else:
            column = jnp.stack([shifted(packed, "fh", 1), packed, shifted(packed, "fh", -1)])
        columns = (shifted(column, "wa", 1), column, shifted(column, "wa", -1))
    flags = jnp.concatenate([side[:, 2 * tokens, :tokens] for side in columns], axis=0)
    flags = flags.reshape(1, -1)
    mask = jnp.where(flags > 0, 0.0, MASKED / HD ** (-0.5)).astype(jnp.float32)

    with jax.named_scope("cotangent_gather"):
        cot_all = lax.all_gather(out_cotangent[0, 0], "ha", axis=0, tiled=True)

    with jax.named_scope("attention_forward"):
        attended, row_max, row_inverse = attention_forward(mask, q, columns)

    with jax.named_scope("output_projection"):
        projected = jnp.dot(attended, out_weight, preferred_element_type=jnp.float32)
        layer_out = lax.psum_scatter(
            projected.astype(jnp.bfloat16), "ha", scatter_dimension=0, tiled=True
        )

    with jax.named_scope("grad_attended"):
        grad_attended = lax.dot_general(
            cot_all, out_weight, (((1,), (1,)), ((), ())), preferred_element_type=jnp.float32
        ).astype(jnp.bfloat16)

    halving = lax.axis_size("fh") == 2 and lax.axis_size("wa") == 4
    with jax.named_scope("grad_weight"):
        if halving:
            rows = model_width // 8
            weight_part = lax.dot_general(
                cot_all, attended, (((0,), (0,)), ((), ())), preferred_element_type=jnp.float32
            )
            weight_blocks = weight_part.reshape(2, 2, 2, rows, weight_part.shape[1])
            core = lax.axis_index("wa") % 2
            weight_own = lax.dynamic_index_in_dim(weight_blocks, core, 2, keepdims=False)
            weight_sent = lax.dynamic_index_in_dim(weight_blocks, 1 - core, 2, keepdims=False)
            weight_sent = weight_sent.astype(jnp.bfloat16)
            weight_own, weight_sent, grad_attended = lax.optimization_barrier(
                (weight_own, weight_sent, grad_attended)
            )
            weight_x = weight_own + partner(weight_sent, "wa", 1).astype(jnp.float32)
        else:
            weight_part = lax.dot_general(
                cot_all, attended, (((0,), (0,)), ((), ())), preferred_element_type=jnp.float32
            )
            weight_own, weight_sent = scatter_parts(weight_part, "fh", 0)
            weight_own, weight_sent, grad_attended = lax.optimization_barrier(
                (weight_own, weight_sent, grad_attended)
            )
            weight_rows = scatter_finish(weight_own, weight_sent, "fh")

    with jax.named_scope("attention_backward"):
        grad_q, left, partials, right = attention_backward(
            mask, q, columns, attended, row_max, row_inverse, grad_attended
        )

    with jax.named_scope("grad_weight"):
        if halving:
            column = lax.axis_index("wa") // 2
            kept = lax.dynamic_index_in_dim(weight_x, column, 1, keepdims=False)
            sent = lax.dynamic_index_in_dim(weight_x, 1 - column, 1, keepdims=False)
            weight_f = kept + partner(sent.astype(jnp.bfloat16), "wa", 2).astype(jnp.float32)
            row = lax.axis_index("fh")
            kept = lax.dynamic_index_in_dim(weight_f, row, 0, keepdims=False)
            sent = lax.dynamic_index_in_dim(weight_f, 1 - row, 0, keepdims=False)
            grad_weight = kept + partner(sent.astype(jnp.bfloat16), "fh", 1).astype(jnp.float32)
        else:
            grad_weight = scatter_sum(weight_rows, "wa", 0)

    with jax.named_scope("halo_reduction"):
        middle = (
            partials
            + shifted(left, "wa", -1).astype(jnp.float32)
            + shifted(right, "wa", 1).astype(jnp.float32)
        )
        middle_sides = middle.astype(jnp.bfloat16)
        if lax.axis_size("fh") == 2:
            own = middle[1] + cyclic(middle_sides[0], "fh", 1).astype(jnp.float32)
        else:
            own = (
                middle[1]
                + shifted(middle_sides[0], "fh", -1).astype(jnp.float32)
                + shifted(middle_sides[2], "fh", 1).astype(jnp.float32)
            )
    grad_keys = own[:tokens].astype(jnp.bfloat16)
    grad_values = own[tokens:].astype(jnp.bfloat16)
    expand = lambda x: x[None, None]
    return (
        expand(layer_out),
        expand(grad_q),
        expand(grad_keys),
        expand(grad_values),
        grad_weight,
    )


def solution(mesh):
    return jax.shard_map(
        body,
        mesh=mesh,
        in_specs=(
            P("fh", "wa", None, "ha"),
            P("fh", "wa", None, "ha"),
            P("fh", "wa", None, "ha"),
            P("fh", "wa", None),
            P("ha", None),
            P("fh", "wa", "ha", None),
        ),
        out_specs=(
            P("fh", "wa", "ha", None),
            P("fh", "wa", None, "ha"),
            P("fh", "wa", None, "ha"),
            P("fh", "wa", None, "ha"),
            P(("fh", "wa"), "ha"),
        ),
        check_vma=False,
    )
```

```python
import functools

import jax
import jax.numpy as jnp
from jax import lax
from jax.experimental import pallas as pl
from jax.experimental.pallas import tpu as pltpu
from jax.sharding import PartitionSpec as P

HD = 128
MASKED = -1e30
FORWARD_CHUNK = 384
BACKWARD_CHUNK = 384
FLAG_ROWS = 16
LOG2E = 1.4426950408889634


def shift_pairs(count, steps):
    return [(source, source + steps) for source in range(count) if 0 <= source + steps < count]


def shifted(value, axis, steps):
    return lax.ppermute(value, axis, shift_pairs(lax.axis_size(axis), steps))


def partner(value, axis, bit):
    count = lax.axis_size(axis)
    return lax.ppermute(value, axis, [(i, i ^ bit) for i in range(count)])


def cyclic(value, axis, steps):
    count = lax.axis_size(axis)
    return lax.ppermute(value, axis, [(i, (i + steps) % count) for i in range(count)])


def joined(refs):
    return jnp.concatenate([ref[...].reshape(-1, HD) for ref in refs], axis=0)


def raw_scores(mask_ref, q_ref, k):
    s = lax.dot_general(q_ref[...], k, (((1,), (1,)), ((), ())), preferred_element_type=jnp.float32)
    return s + mask_ref[...]


def forward_kernel(exp_scale, mask_ref, q_ref, kl, km, kr, vl, vm, vr, o_ref, m_ref, r_ref):
    s = raw_scores(mask_ref, q_ref, joined((kl, km, kr)))
    m = jnp.max(s, axis=1, keepdims=True)
    e = jnp.exp2((s - m) * exp_scale)
    inverse = 1.0 / jnp.sum(e, axis=1, keepdims=True)
    p = (e * inverse).astype(jnp.bfloat16)
    v = joined((vl, vm, vr))
    o_ref[...] = jnp.dot(p, v, preferred_element_type=jnp.float32).astype(o_ref.dtype)
    m_ref[...] = jnp.broadcast_to(m, m_ref.shape)
    r_ref[...] = jnp.broadcast_to(inverse, r_ref.shape)


def backward_kernel(
    scale, exp_scale, mask_ref, q_ref, kl, km, kr, vl, vm, vr, o_ref, m_ref, r_ref, do_ref,
    dq_ref, left_ref, mid_ref, right_ref, acc_ref
):
    chunk = pl.program_id(1)
    k = joined((kl, km, kr))
    v = joined((vl, vm, vr))
    s = raw_scores(mask_ref, q_ref, k)
    w = jnp.exp2((s - m_ref[:, :1]) * exp_scale) * r_ref[:, :1]
    p = w.astype(jnp.bfloat16)
    do = do_ref[...]
    row_dot = jnp.sum(
        do.astype(jnp.float32) * o_ref[...].astype(jnp.float32), axis=1, keepdims=True
    )
    dp = lax.dot_general(do, v, (((1,), (1,)), ((), ())), preferred_element_type=jnp.float32)
    ds = (w * (dp - row_dot)).astype(jnp.bfloat16)
    dq = jnp.dot(ds, k, preferred_element_type=jnp.float32) * scale
    dq_ref[...] = dq.astype(dq_ref.dtype)
    contract0 = (((0,), (0,)), ((), ()))
    dk = lax.dot_general(ds, q_ref[...], contract0, preferred_element_type=jnp.float32) * scale
    dv = lax.dot_general(p, do, contract0, preferred_element_type=jnp.float32)
    tiles, tokens = 3 * kl.shape[0], kl.shape[1]
    dk = dk.reshape(tiles, tokens, HD)
    dv = dv.reshape(tiles, tokens, HD)

    @pl.when(chunk == 0)
    def _():
        acc_ref[:, :tokens, :] = dk
        acc_ref[:, tokens:, :] = dv

    @pl.when(chunk > 0)
    def _():
        acc_ref[:, :tokens, :] += dk
        acc_ref[:, tokens:, :] += dv

    @pl.when(chunk == pl.num_programs(1) - 1)
    def _():
        third = tiles // 3
        left_ref[...] = acc_ref[:third].astype(left_ref.dtype)
        mid_ref[...] = acc_ref[third : 2 * third]
        right_ref[...] = acc_ref[2 * third :].astype(right_ref.dtype)


def attention_forward(mask, queries, columns):
    tokens, features = queries.shape
    tiles = 3 * columns[0].shape[0]
    heads = features // HD
    chunk = FORWARD_CHUNK
    chunks = tokens // chunk
    scale = HD ** (-0.5)
    return pl.pallas_call(
        functools.partial(forward_kernel, scale * LOG2E),
        grid=(heads, chunks),
        in_specs=[
            pl.BlockSpec((1, tiles * tokens), lambda h, c: (0, 0)),
            pl.BlockSpec((chunk, HD), lambda h, c: (c, h)),
            *[pl.BlockSpec((tiles // 3, tokens, HD), lambda h, c: (0, 0, h))] * 3,
            *[pl.BlockSpec((tiles // 3, tokens, HD), lambda h, c: (0, 1, h))] * 3,
        ],
        out_specs=[pl.BlockSpec((chunk, HD), lambda h, c: (c, h))] * 3,
        out_shape=[
            jax.ShapeDtypeStruct((tokens, features), jnp.bfloat16),
            jax.ShapeDtypeStruct((tokens, features), jnp.float32),
            jax.ShapeDtypeStruct((tokens, features), jnp.float32),
        ],
        name="tile_attention_forward",
    )(mask, queries, *columns, *columns)


def attention_backward(mask, queries, columns, attended, row_max, row_inverse, grad_attended):
    tokens, features = queries.shape
    tiles = 3 * columns[0].shape[0]
    heads = features // HD
    chunk = BACKWARD_CHUNK
    chunks = tokens // chunk
    scale = HD ** (-0.5)
    return pl.pallas_call(
        functools.partial(backward_kernel, scale, scale * LOG2E),
        grid=(heads, chunks),
        in_specs=[
            pl.BlockSpec((1, tiles * tokens), lambda h, c: (0, 0)),
            pl.BlockSpec((chunk, HD), lambda h, c: (c, h)),
            *[pl.BlockSpec((tiles // 3, tokens, HD), lambda h, c: (0, 0, h))] * 3,
            *[pl.BlockSpec((tiles // 3, tokens, HD), lambda h, c: (0, 1, h))] * 3,
            pl.BlockSpec((chunk, HD), lambda h, c: (c, h)),
            pl.BlockSpec((chunk, HD), lambda h, c: (c, h)),
            pl.BlockSpec((chunk, HD), lambda h, c: (c, h)),
            pl.BlockSpec((chunk, HD), lambda h, c: (c, h)),
        ],
        out_specs=[
            pl.BlockSpec((chunk, HD), lambda h, c: (c, h)),
            pl.BlockSpec((tiles // 3, 2 * tokens, HD), lambda h, c: (0, 0, h)),
            pl.BlockSpec((tiles // 3, 2 * tokens, HD), lambda h, c: (0, 0, h)),
            pl.BlockSpec((tiles // 3, 2 * tokens, HD), lambda h, c: (0, 0, h)),
        ],
        out_shape=[
            jax.ShapeDtypeStruct((tokens, features), jnp.bfloat16),
            jax.ShapeDtypeStruct((tiles // 3, 2 * tokens, features), jnp.bfloat16),
            jax.ShapeDtypeStruct((tiles // 3, 2 * tokens, features), jnp.float32),
            jax.ShapeDtypeStruct((tiles // 3, 2 * tokens, features), jnp.bfloat16),
        ],
        scratch_shapes=[pltpu.VMEM((tiles, 2 * tokens, HD), jnp.float32)],
        name="tile_attention_backward",
    )(mask, queries, *columns, *columns, attended, row_max, row_inverse, grad_attended)


def gather_over(piece, axis):
    count = lax.axis_size(axis)
    me = lax.axis_index(axis)
    received = [piece] + [cyclic(piece, axis, steps) for steps in range(1, count)]
    ordered = jnp.stack([received[(-k) % count] for k in range(count)])
    return jnp.roll(ordered, me, axis=0)


def scatter_parts(full, axis, dim):
    count = lax.axis_size(axis)
    me = lax.axis_index(axis)
    size = full.shape[dim] // count

    def part(index):
        return lax.dynamic_slice_in_dim(full, index * size, size, axis=dim)

    sent = [part((me + steps) % count).astype(jnp.bfloat16) for steps in range(1, count)]
    return part(me).astype(jnp.float32), sent


def scatter_finish(own, sent, axis):
    total = own
    for steps, piece in enumerate(sent, start=1):
        total = total + cyclic(piece, axis, steps).astype(jnp.float32)
    return total


def scatter_sum(full, axis, dim):
    count = lax.axis_size(axis)
    me = lax.axis_index(axis)
    size = full.shape[dim] // count

    def part(index):
        return lax.dynamic_slice_in_dim(full, index * size, size, axis=dim)

    total = part(me).astype(jnp.float32)
    for steps in range(1, count):
        sent = part((me + steps) % count).astype(jnp.bfloat16)
        total = total + cyclic(sent, axis, steps).astype(jnp.float32)
    return total


def body(queries, key_states, value_states, valid_mask, out_weight, out_cotangent):
    tile_rows, tile_columns, tokens, features = queries.shape
    assert tile_rows == 1 and tile_columns == 1
    model_width = out_weight.shape[1]
    q = queries[0, 0]
    flag_rows = jnp.zeros((FLAG_ROWS, features), jnp.bfloat16)
    flag_rows = flag_rows.at[0, :tokens].set(valid_mask[0, 0].astype(jnp.bfloat16))
    packed = jnp.concatenate([key_states[0, 0], value_states[0, 0], flag_rows], axis=0)

    with jax.named_scope("halo_exchange"):
        if lax.axis_size("fh") == 2:
            column = jnp.stack([cyclic(packed, "fh", 1), packed])
        else:
            column = jnp.stack([shifted(packed, "fh", 1), packed, shifted(packed, "fh", -1)])
        columns = (shifted(column, "wa", 1), column, shifted(column, "wa", -1))
    flags = jnp.concatenate([side[:, 2 * tokens, :tokens] for side in columns], axis=0)
    flags = flags.reshape(1, -1)
    mask = jnp.where(flags > 0, 0.0, MASKED / HD ** (-0.5)).astype(jnp.float32)

    with jax.named_scope("cotangent_gather"):
        cot_all = lax.all_gather(out_cotangent[0, 0], "ha", axis=0, tiled=True)

    with jax.named_scope("attention_forward"):
        attended, row_max, row_inverse = attention_forward(mask, q, columns)

    with jax.named_scope("output_projection"):
        projected = jnp.dot(attended, out_weight, preferred_element_type=jnp.float32)
        layer_out = lax.psum_scatter(
            projected.astype(jnp.bfloat16), "ha", scatter_dimension=0, tiled=True
        )

    with jax.named_scope("grad_attended"):
        grad_attended = lax.dot_general(
            cot_all, out_weight, (((1,), (1,)), ((), ())), preferred_element_type=jnp.float32
        ).astype(jnp.bfloat16)

    halving = lax.axis_size("fh") == 2 and lax.axis_size("wa") == 4
    with jax.named_scope("grad_weight"):
        if halving:
            rows = model_width // 8
            cot_blocks = cot_all.reshape(-1, 2, 2, 2, rows)
            weight_blocks = lax.dot_general(
                cot_blocks, attended, (((0,), (0,)), ((), ())), preferred_element_type=jnp.float32
            )
            weight_blocks = jnp.transpose(weight_blocks, (2, 1, 0, 3, 4))
            core = lax.axis_index("wa") % 2
            weight_own = lax.dynamic_index_in_dim(weight_blocks, core, 0, keepdims=False)
            weight_sent = lax.dynamic_index_in_dim(weight_blocks, 1 - core, 0, keepdims=False)
            weight_sent = weight_sent.astype(jnp.bfloat16)
            weight_own, weight_sent, grad_attended = lax.optimization_barrier(
                (weight_own, weight_sent, grad_attended)
            )
            weight_x = weight_own + partner(weight_sent, "wa", 1).astype(jnp.float32)
        else:
            weight_part = lax.dot_general(
                cot_all, attended, (((0,), (0,)), ((), ())), preferred_element_type=jnp.float32
            )
            weight_own, weight_sent = scatter_parts(weight_part, "fh", 0)
            weight_own, weight_sent, grad_attended = lax.optimization_barrier(
                (weight_own, weight_sent, grad_attended)
            )
            weight_rows = scatter_finish(weight_own, weight_sent, "fh")

    with jax.named_scope("attention_backward"):
        grad_q, left, partials, right = attention_backward(
            mask, q, columns, attended, row_max, row_inverse, grad_attended
        )

    with jax.named_scope("grad_weight"):
        if halving:
            column = lax.axis_index("wa") // 2
            kept = lax.dynamic_index_in_dim(weight_x, column, 0, keepdims=False)
            sent = lax.dynamic_index_in_dim(weight_x, 1 - column, 0, keepdims=False)
            weight_f = kept + partner(sent.astype(jnp.bfloat16), "wa", 2).astype(jnp.float32)
            row = lax.axis_index("fh")
            kept = lax.dynamic_index_in_dim(weight_f, row, 0, keepdims=False)
            sent = lax.dynamic_index_in_dim(weight_f, 1 - row, 0, keepdims=False)
            grad_weight = kept + partner(sent.astype(jnp.bfloat16), "fh", 1).astype(jnp.float32)
        else:
            grad_weight = scatter_sum(weight_rows, "wa", 0)

    with jax.named_scope("halo_reduction"):
        middle = (
            partials
            + shifted(left, "wa", -1).astype(jnp.float32)
            + shifted(right, "wa", 1).astype(jnp.float32)
        )
        middle_sides = middle.astype(jnp.bfloat16)
        if lax.axis_size("fh") == 2:
            own = middle[1] + cyclic(middle_sides[0], "fh", 1).astype(jnp.float32)
        else:
            own = (
                middle[1]
                + shifted(middle_sides[0], "fh", -1).astype(jnp.float32)
                + shifted(middle_sides[2], "fh", 1).astype(jnp.float32)
            )
    grad_keys = own[:tokens].astype(jnp.bfloat16)
    grad_values = own[tokens:].astype(jnp.bfloat16)
    expand = lambda x: x[None, None]
    return (
        expand(layer_out),
        expand(grad_q),
        expand(grad_keys),
        expand(grad_values),
        grad_weight,
    )


def solution(mesh):
    return jax.shard_map(
        body,
        mesh=mesh,
        in_specs=(
            P("fh", "wa", None, "ha"),
            P("fh", "wa", None, "ha"),
            P("fh", "wa", None, "ha"),
            P("fh", "wa", None),
            P("ha", None),
            P("fh", "wa", "ha", None),
        ),
        out_specs=(
            P("fh", "wa", "ha", None),
            P("fh", "wa", None, "ha"),
            P("fh", "wa", None, "ha"),
            P("fh", "wa", None, "ha"),
            P(("fh", "wa"), "ha"),
        ),
        check_vma=False,
    )
```

```python
import functools

import jax
import jax.numpy as jnp
from jax import lax
from jax.experimental import pallas as pl
from jax.experimental.pallas import tpu as pltpu
from jax.sharding import PartitionSpec as P

HD = 128
MASKED = -1e30
FORWARD_CHUNK = 384
BACKWARD_CHUNK = 384
FLAG_ROWS = 16
LOG2E = 1.4426950408889634


def shift_pairs(count, steps):
    return [(source, source + steps) for source in range(count) if 0 <= source + steps < count]


def shifted(value, axis, steps):
    return lax.ppermute(value, axis, shift_pairs(lax.axis_size(axis), steps))


def halving_order(matrix):
    rows = matrix.shape[1] // 8
    blocks = matrix.reshape(matrix.shape[0], 2, 2, 2, rows)
    return jnp.transpose(blocks, (0, 3, 2, 1, 4)).reshape(matrix.shape)


def partner(value, axis, bit):
    count = lax.axis_size(axis)
    return lax.ppermute(value, axis, [(i, i ^ bit) for i in range(count)])


def cyclic(value, axis, steps):
    count = lax.axis_size(axis)
    return lax.ppermute(value, axis, [(i, (i + steps) % count) for i in range(count)])


def joined(refs):
    return jnp.concatenate([ref[...].reshape(-1, HD) for ref in refs], axis=0)


def raw_scores(mask_ref, q_ref, k):
    s = lax.dot_general(q_ref[...], k, (((1,), (1,)), ((), ())), preferred_element_type=jnp.float32)
    return s + mask_ref[...]


def forward_kernel(exp_scale, mask_ref, q_ref, kl, km, kr, vl, vm, vr, o_ref, m_ref, r_ref):
    s = raw_scores(mask_ref, q_ref, joined((kl, km, kr)))
    m = jnp.max(s, axis=1, keepdims=True)
    e = jnp.exp2((s - m) * exp_scale)
    inverse = 1.0 / jnp.sum(e, axis=1, keepdims=True)
    p = (e * inverse).astype(jnp.bfloat16)
    v = joined((vl, vm, vr))
    o_ref[...] = jnp.dot(p, v, preferred_element_type=jnp.float32).astype(o_ref.dtype)
    m_ref[...] = jnp.broadcast_to(m, m_ref.shape)
    r_ref[...] = jnp.broadcast_to(inverse, r_ref.shape)


def backward_kernel(
    scale, exp_scale, mask_ref, q_ref, kl, km, kr, vl, vm, vr, o_ref, m_ref, r_ref, do_ref,
    dq_ref, left_ref, mid_ref, right_ref, acc_ref
):
    chunk = pl.program_id(1)
    k = joined((kl, km, kr))
    v = joined((vl, vm, vr))
    s = raw_scores(mask_ref, q_ref, k)
    w = jnp.exp2((s - m_ref[:, :1]) * exp_scale) * r_ref[:, :1]
    p = w.astype(jnp.bfloat16)
    do = do_ref[...]
    row_dot = jnp.sum(
        do.astype(jnp.float32) * o_ref[...].astype(jnp.float32), axis=1, keepdims=True
    )
    dp = lax.dot_general(do, v, (((1,), (1,)), ((), ())), preferred_element_type=jnp.float32)
    ds = (w * (dp - row_dot)).astype(jnp.bfloat16)
    dq = jnp.dot(ds, k, preferred_element_type=jnp.float32) * scale
    dq_ref[...] = dq.astype(dq_ref.dtype)
    contract0 = (((0,), (0,)), ((), ()))
    dk = lax.dot_general(ds, q_ref[...], contract0, preferred_element_type=jnp.float32) * scale
    dv = lax.dot_general(p, do, contract0, preferred_element_type=jnp.float32)
    tiles, tokens = 3 * kl.shape[0], kl.shape[1]
    dk = dk.reshape(tiles, tokens, HD)
    dv = dv.reshape(tiles, tokens, HD)

    @pl.when(chunk == 0)
    def _():
        acc_ref[:, :tokens, :] = dk
        acc_ref[:, tokens:, :] = dv

    @pl.when(chunk > 0)
    def _():
        acc_ref[:, :tokens, :] += dk
        acc_ref[:, tokens:, :] += dv

    @pl.when(chunk == pl.num_programs(1) - 1)
    def _():
        third = tiles // 3
        left_ref[...] = acc_ref[:third].astype(left_ref.dtype)
        mid_ref[...] = acc_ref[third : 2 * third]
        right_ref[...] = acc_ref[2 * third :].astype(right_ref.dtype)


def attention_forward(mask, queries, columns):
    tokens, features = queries.shape
    tiles = 3 * columns[0].shape[0]
    heads = features // HD
    chunk = FORWARD_CHUNK
    chunks = tokens // chunk
    scale = HD ** (-0.5)
    return pl.pallas_call(
        functools.partial(forward_kernel, scale * LOG2E),
        grid=(heads, chunks),
        in_specs=[
            pl.BlockSpec((1, tiles * tokens), lambda h, c: (0, 0)),
            pl.BlockSpec((chunk, HD), lambda h, c: (c, h)),
            *[pl.BlockSpec((tiles // 3, tokens, HD), lambda h, c: (0, 0, h))] * 3,
            *[pl.BlockSpec((tiles // 3, tokens, HD), lambda h, c: (0, 1, h))] * 3,
        ],
        out_specs=[pl.BlockSpec((chunk, HD), lambda h, c: (c, h))] * 3,
        out_shape=[
            jax.ShapeDtypeStruct((tokens, features), jnp.bfloat16),
            jax.ShapeDtypeStruct((tokens, features), jnp.float32),
            jax.ShapeDtypeStruct((tokens, features), jnp.float32),
        ],
        name="tile_attention_forward",
    )(mask, queries, *columns, *columns)


def attention_backward(mask, queries, columns, attended, row_max, row_inverse, grad_attended):
    tokens, features = queries.shape
    tiles = 3 * columns[0].shape[0]
    heads = features // HD
    chunk = BACKWARD_CHUNK
    chunks = tokens // chunk
    scale = HD ** (-0.5)
    return pl.pallas_call(
        functools.partial(backward_kernel, scale, scale * LOG2E),
        grid=(heads, chunks),
        in_specs=[
            pl.BlockSpec((1, tiles * tokens), lambda h, c: (0, 0)),
            pl.BlockSpec((chunk, HD), lambda h, c: (c, h)),
            *[pl.BlockSpec((tiles // 3, tokens, HD), lambda h, c: (0, 0, h))] * 3,
            *[pl.BlockSpec((tiles // 3, tokens, HD), lambda h, c: (0, 1, h))] * 3,
            pl.BlockSpec((chunk, HD), lambda h, c: (c, h)),
            pl.BlockSpec((chunk, HD), lambda h, c: (c, h)),
            pl.BlockSpec((chunk, HD), lambda h, c: (c, h)),
            pl.BlockSpec((chunk, HD), lambda h, c: (c, h)),
        ],
        out_specs=[
            pl.BlockSpec((chunk, HD), lambda h, c: (c, h)),
            pl.BlockSpec((tiles // 3, 2 * tokens, HD), lambda h, c: (0, 0, h)),
            pl.BlockSpec((tiles // 3, 2 * tokens, HD), lambda h, c: (0, 0, h)),
            pl.BlockSpec((tiles // 3, 2 * tokens, HD), lambda h, c: (0, 0, h)),
        ],
        out_shape=[
            jax.ShapeDtypeStruct((tokens, features), jnp.bfloat16),
            jax.ShapeDtypeStruct((tiles // 3, 2 * tokens, features), jnp.bfloat16),
            jax.ShapeDtypeStruct((tiles // 3, 2 * tokens, features), jnp.float32),
            jax.ShapeDtypeStruct((tiles // 3, 2 * tokens, features), jnp.bfloat16),
        ],
        scratch_shapes=[pltpu.VMEM((tiles, 2 * tokens, HD), jnp.float32)],
        name="tile_attention_backward",
    )(mask, queries, *columns, *columns, attended, row_max, row_inverse, grad_attended)


def gather_over(piece, axis):
    count = lax.axis_size(axis)
    me = lax.axis_index(axis)
    received = [piece] + [cyclic(piece, axis, steps) for steps in range(1, count)]
    ordered = jnp.stack([received[(-k) % count] for k in range(count)])
    return jnp.roll(ordered, me, axis=0)


def scatter_parts(full, axis, dim):
    count = lax.axis_size(axis)
    me = lax.axis_index(axis)
    size = full.shape[dim] // count

    def part(index):
        return lax.dynamic_slice_in_dim(full, index * size, size, axis=dim)

    sent = [part((me + steps) % count).astype(jnp.bfloat16) for steps in range(1, count)]
    return part(me).astype(jnp.float32), sent


def scatter_finish(own, sent, axis):
    total = own
    for steps, piece in enumerate(sent, start=1):
        total = total + cyclic(piece, axis, steps).astype(jnp.float32)
    return total


def scatter_sum(full, axis, dim):
    count = lax.axis_size(axis)
    me = lax.axis_index(axis)
    size = full.shape[dim] // count

    def part(index):
        return lax.dynamic_slice_in_dim(full, index * size, size, axis=dim)

    total = part(me).astype(jnp.float32)
    for steps in range(1, count):
        sent = part((me + steps) % count).astype(jnp.bfloat16)
        total = total + cyclic(sent, axis, steps).astype(jnp.float32)
    return total


def body(queries, key_states, value_states, valid_mask, out_weight, out_cotangent):
    tile_rows, tile_columns, tokens, features = queries.shape
    assert tile_rows == 1 and tile_columns == 1
    model_width = out_weight.shape[1]
    q = queries[0, 0]
    flag_rows = jnp.zeros((FLAG_ROWS, features), jnp.bfloat16)
    flag_rows = flag_rows.at[0, :tokens].set(valid_mask[0, 0].astype(jnp.bfloat16))
    packed = jnp.concatenate([key_states[0, 0], value_states[0, 0], flag_rows], axis=0)

    with jax.named_scope("halo_exchange"):
        if lax.axis_size("fh") == 2:
            column = jnp.stack([cyclic(packed, "fh", 1), packed])
        else:
            column = jnp.stack([shifted(packed, "fh", 1), packed, shifted(packed, "fh", -1)])
        columns = (shifted(column, "wa", 1), column, shifted(column, "wa", -1))
    flags = jnp.concatenate([side[:, 2 * tokens, :tokens] for side in columns], axis=0)
    flags = flags.reshape(1, -1)
    mask = jnp.where(flags > 0, 0.0, MASKED / HD ** (-0.5)).astype(jnp.float32)

    with jax.named_scope("cotangent_gather"):
        cot_local = out_cotangent[0, 0]
        weight_columns = out_weight
        if lax.axis_size("fh") == 2 and lax.axis_size("wa") == 4:
            cot_local = halving_order(cot_local)
            weight_columns = halving_order(out_weight)
        cot_all = lax.all_gather(cot_local, "ha", axis=0, tiled=True)

    with jax.named_scope("attention_forward"):
        attended, row_max, row_inverse = attention_forward(mask, q, columns)

    with jax.named_scope("output_projection"):
        projected = jnp.dot(attended, out_weight, preferred_element_type=jnp.float32)
        layer_out = lax.psum_scatter(
            projected.astype(jnp.bfloat16), "ha", scatter_dimension=0, tiled=True
        )

    with jax.named_scope("grad_attended"):
        grad_attended = lax.dot_general(
            cot_all, weight_columns, (((1,), (1,)), ((), ())), preferred_element_type=jnp.float32
        ).astype(jnp.bfloat16)

    halving = lax.axis_size("fh") == 2 and lax.axis_size("wa") == 4
    with jax.named_scope("grad_weight"):
        if halving:
            rows = model_width // 8
            weight_blocks = lax.dot_general(
                cot_all, attended, (((0,), (0,)), ((), ())), preferred_element_type=jnp.float32
            ).reshape(2, 2, 2, rows, attended.shape[1])
            core = lax.axis_index("wa") % 2
            weight_own = lax.dynamic_index_in_dim(weight_blocks, core, 0, keepdims=False)
            weight_sent = lax.dynamic_index_in_dim(weight_blocks, 1 - core, 0, keepdims=False)
            weight_sent = weight_sent.astype(jnp.bfloat16)
            weight_own, weight_sent, grad_attended = lax.optimization_barrier(
                (weight_own, weight_sent, grad_attended)
            )
            weight_x = weight_own + partner(weight_sent, "wa", 1).astype(jnp.float32)
        else:
            weight_part = lax.dot_general(
                cot_all, attended, (((0,), (0,)), ((), ())), preferred_element_type=jnp.float32
            )
            weight_own, weight_sent = scatter_parts(weight_part, "fh", 0)
            weight_own, weight_sent, grad_attended = lax.optimization_barrier(
                (weight_own, weight_sent, grad_attended)
            )
            weight_rows = scatter_finish(weight_own, weight_sent, "fh")

    with jax.named_scope("attention_backward"):
        grad_q, left, partials, right = attention_backward(
            mask, q, columns, attended, row_max, row_inverse, grad_attended
        )

    with jax.named_scope("grad_weight"):
        if halving:
            column = lax.axis_index("wa") // 2
            kept = lax.dynamic_index_in_dim(weight_x, column, 0, keepdims=False)
            sent = lax.dynamic_index_in_dim(weight_x, 1 - column, 0, keepdims=False)
            weight_f = kept + partner(sent.astype(jnp.bfloat16), "wa", 2).astype(jnp.float32)
            row = lax.axis_index("fh")
            kept = lax.dynamic_index_in_dim(weight_f, row, 0, keepdims=False)
            sent = lax.dynamic_index_in_dim(weight_f, 1 - row, 0, keepdims=False)
            grad_weight = kept + partner(sent.astype(jnp.bfloat16), "fh", 1).astype(jnp.float32)
        else:
            grad_weight = scatter_sum(weight_rows, "wa", 0)

    with jax.named_scope("halo_reduction"):
        middle = (
            partials
            + shifted(left, "wa", -1).astype(jnp.float32)
            + shifted(right, "wa", 1).astype(jnp.float32)
        )
        middle_sides = middle.astype(jnp.bfloat16)
        if lax.axis_size("fh") == 2:
            own = middle[1] + cyclic(middle_sides[0], "fh", 1).astype(jnp.float32)
        else:
            own = (
                middle[1]
                + shifted(middle_sides[0], "fh", -1).astype(jnp.float32)
                + shifted(middle_sides[2], "fh", 1).astype(jnp.float32)
            )
    grad_keys = own[:tokens].astype(jnp.bfloat16)
    grad_values = own[tokens:].astype(jnp.bfloat16)
    expand = lambda x: x[None, None]
    return (
        expand(layer_out),
        expand(grad_q),
        expand(grad_keys),
        expand(grad_values),
        grad_weight,
    )


def solution(mesh):
    return jax.shard_map(
        body,
        mesh=mesh,
        in_specs=(
            P("fh", "wa", None, "ha"),
            P("fh", "wa", None, "ha"),
            P("fh", "wa", None, "ha"),
            P("fh", "wa", None),
            P("ha", None),
            P("fh", "wa", "ha", None),
        ),
        out_specs=(
            P("fh", "wa", "ha", None),
            P("fh", "wa", None, "ha"),
            P("fh", "wa", None, "ha"),
            P("fh", "wa", None, "ha"),
            P(("fh", "wa"), "ha"),
        ),
        check_vma=False,
    )
```

```python
import functools

import jax
import jax.numpy as jnp
from jax import lax
from jax.experimental import pallas as pl
from jax.experimental.pallas import tpu as pltpu
from jax.sharding import PartitionSpec as P

HD = 128
MASKED = -1e30
FORWARD_CHUNK = 384
BACKWARD_CHUNK = 384
FLAG_ROWS = 16
LOG2E = 1.4426950408889634


def shift_pairs(count, steps):
    return [(source, source + steps) for source in range(count) if 0 <= source + steps < count]


def shifted(value, axis, steps):
    return lax.ppermute(value, axis, shift_pairs(lax.axis_size(axis), steps))


def partner(value, axis, bit):
    count = lax.axis_size(axis)
    return lax.ppermute(value, axis, [(i, i ^ bit) for i in range(count)])


def cyclic(value, axis, steps):
    count = lax.axis_size(axis)
    return lax.ppermute(value, axis, [(i, (i + steps) % count) for i in range(count)])


def joined(refs):
    return jnp.concatenate([ref[...].reshape(-1, HD) for ref in refs], axis=0)


def raw_scores(mask_ref, q_ref, k):
    s = lax.dot_general(q_ref[...], k, (((1,), (1,)), ((), ())), preferred_element_type=jnp.float32)
    return s + mask_ref[...]


def forward_kernel(exp_scale, mask_ref, q_ref, kl, km, kr, vl, vm, vr, o_ref, m_ref, r_ref):
    s = raw_scores(mask_ref, q_ref, joined((kl, km, kr)))
    m = jnp.max(s, axis=1, keepdims=True)
    e = jnp.exp2((s - m) * exp_scale)
    inverse = 1.0 / jnp.sum(e, axis=1, keepdims=True)
    p = (e * inverse).astype(jnp.bfloat16)
    v = joined((vl, vm, vr))
    o_ref[...] = jnp.dot(p, v, preferred_element_type=jnp.float32).astype(o_ref.dtype)
    m_ref[...] = jnp.broadcast_to(m, m_ref.shape)
    r_ref[...] = jnp.broadcast_to(inverse, r_ref.shape)


def backward_kernel(
    scale, exp_scale, mask_ref, q_ref, kl, km, kr, vl, vm, vr, o_ref, m_ref, r_ref, do_ref,
    dq_ref, left_ref, mid_ref, right_ref, acc_ref
):
    chunk = pl.program_id(1)
    k = joined((kl, km, kr))
    v = joined((vl, vm, vr))
    s = raw_scores(mask_ref, q_ref, k)
    w = jnp.exp2((s - m_ref[:, :1]) * exp_scale) * r_ref[:, :1]
    p = w.astype(jnp.bfloat16)
    do = do_ref[...]
    row_dot = jnp.sum(
        do.astype(jnp.float32) * o_ref[...].astype(jnp.float32), axis=1, keepdims=True
    )
    dp = lax.dot_general(do, v, (((1,), (1,)), ((), ())), preferred_element_type=jnp.float32)
    ds = (w * (dp - row_dot)).astype(jnp.bfloat16)
    dq = jnp.dot(ds, k, preferred_element_type=jnp.float32) * scale
    dq_ref[...] = dq.astype(dq_ref.dtype)
    contract0 = (((0,), (0,)), ((), ()))
    dk = lax.dot_general(ds, q_ref[...], contract0, preferred_element_type=jnp.float32) * scale
    dv = lax.dot_general(p, do, contract0, preferred_element_type=jnp.float32)
    tiles, tokens = 3 * kl.shape[0], kl.shape[1]
    dk = dk.reshape(tiles, tokens, HD)
    dv = dv.reshape(tiles, tokens, HD)

    @pl.when(chunk == 0)
    def _():
        acc_ref[:, :tokens, :] = dk
        acc_ref[:, tokens:, :] = dv

    @pl.when(chunk > 0)
    def _():
        acc_ref[:, :tokens, :] += dk
        acc_ref[:, tokens:, :] += dv

    @pl.when(chunk == pl.num_programs(1) - 1)
    def _():
        third = tiles // 3
        left_ref[...] = acc_ref[:third].astype(left_ref.dtype)
        mid_ref[...] = acc_ref[third : 2 * third]
        right_ref[...] = acc_ref[2 * third :].astype(right_ref.dtype)


def attention_forward(mask, queries, columns):
    tokens, features = queries.shape
    tiles = 3 * columns[0].shape[0]
    heads = features // HD
    chunk = FORWARD_CHUNK
    chunks = tokens // chunk
    scale = HD ** (-0.5)
    return pl.pallas_call(
        functools.partial(forward_kernel, scale * LOG2E),
        grid=(heads, chunks),
        in_specs=[
            pl.BlockSpec((1, tiles * tokens), lambda h, c: (0, 0)),
            pl.BlockSpec((chunk, HD), lambda h, c: (c, h)),
            *[pl.BlockSpec((tiles // 3, tokens, HD), lambda h, c: (0, 0, h))] * 3,
            *[pl.BlockSpec((tiles // 3, tokens, HD), lambda h, c: (0, 1, h))] * 3,
        ],
        out_specs=[pl.BlockSpec((chunk, HD), lambda h, c: (c, h))] * 3,
        out_shape=[
            jax.ShapeDtypeStruct((tokens, features), jnp.bfloat16),
            jax.ShapeDtypeStruct((tokens, features), jnp.float32),
            jax.ShapeDtypeStruct((tokens, features), jnp.float32),
        ],
        name="tile_attention_forward",
    )(mask, queries, *columns, *columns)


def attention_backward(mask, queries, columns, attended, row_max, row_inverse, grad_attended):
    tokens, features = queries.shape
    tiles = 3 * columns[0].shape[0]
    heads = features // HD
    chunk = BACKWARD_CHUNK
    chunks = tokens // chunk
    scale = HD ** (-0.5)
    return pl.pallas_call(
        functools.partial(backward_kernel, scale, scale * LOG2E),
        grid=(heads, chunks),
        in_specs=[
            pl.BlockSpec((1, tiles * tokens), lambda h, c: (0, 0)),
            pl.BlockSpec((chunk, HD), lambda h, c: (c, h)),
            *[pl.BlockSpec((tiles // 3, tokens, HD), lambda h, c: (0, 0, h))] * 3,
            *[pl.BlockSpec((tiles // 3, tokens, HD), lambda h, c: (0, 1, h))] * 3,
            pl.BlockSpec((chunk, HD), lambda h, c: (c, h)),
            pl.BlockSpec((chunk, HD), lambda h, c: (c, h)),
            pl.BlockSpec((chunk, HD), lambda h, c: (c, h)),
            pl.BlockSpec((chunk, HD), lambda h, c: (c, h)),
        ],
        out_specs=[
            pl.BlockSpec((chunk, HD), lambda h, c: (c, h)),
            pl.BlockSpec((tiles // 3, 2 * tokens, HD), lambda h, c: (0, 0, h)),
            pl.BlockSpec((tiles // 3, 2 * tokens, HD), lambda h, c: (0, 0, h)),
            pl.BlockSpec((tiles // 3, 2 * tokens, HD), lambda h, c: (0, 0, h)),
        ],
        out_shape=[
            jax.ShapeDtypeStruct((tokens, features), jnp.bfloat16),
            jax.ShapeDtypeStruct((tiles // 3, 2 * tokens, features), jnp.bfloat16),
            jax.ShapeDtypeStruct((tiles // 3, 2 * tokens, features), jnp.float32),
            jax.ShapeDtypeStruct((tiles // 3, 2 * tokens, features), jnp.bfloat16),
        ],
        scratch_shapes=[pltpu.VMEM((tiles, 2 * tokens, HD), jnp.float32)],
        name="tile_attention_backward",
    )(mask, queries, *columns, *columns, attended, row_max, row_inverse, grad_attended)


def gather_over(piece, axis):
    count = lax.axis_size(axis)
    me = lax.axis_index(axis)
    received = [piece] + [cyclic(piece, axis, steps) for steps in range(1, count)]
    ordered = jnp.stack([received[(-k) % count] for k in range(count)])
    return jnp.roll(ordered, me, axis=0)


def scatter_parts(full, axis, dim):
    count = lax.axis_size(axis)
    me = lax.axis_index(axis)
    size = full.shape[dim] // count

    def part(index):
        return lax.dynamic_slice_in_dim(full, index * size, size, axis=dim)

    sent = [part((me + steps) % count).astype(jnp.bfloat16) for steps in range(1, count)]
    return part(me).astype(jnp.float32), sent


def scatter_finish(own, sent, axis):
    total = own
    for steps, piece in enumerate(sent, start=1):
        total = total + cyclic(piece, axis, steps).astype(jnp.float32)
    return total


def scatter_sum(full, axis, dim):
    count = lax.axis_size(axis)
    me = lax.axis_index(axis)
    size = full.shape[dim] // count

    def part(index):
        return lax.dynamic_slice_in_dim(full, index * size, size, axis=dim)

    total = part(me).astype(jnp.float32)
    for steps in range(1, count):
        sent = part((me + steps) % count).astype(jnp.bfloat16)
        total = total + cyclic(sent, axis, steps).astype(jnp.float32)
    return total


def body(queries, key_states, value_states, valid_mask, out_weight, out_cotangent):
    tile_rows, tile_columns, tokens, features = queries.shape
    assert tile_rows == 1 and tile_columns == 1
    model_width = out_weight.shape[1]
    q = queries[0, 0]
    flag_rows = jnp.zeros((FLAG_ROWS, features), jnp.bfloat16)
    flag_rows = flag_rows.at[0, :tokens].set(valid_mask[0, 0].astype(jnp.bfloat16))
    packed = jnp.concatenate([key_states[0, 0], value_states[0, 0], flag_rows], axis=0)

    with jax.named_scope("halo_exchange"):
        if lax.axis_size("fh") == 2:
            column = jnp.stack([cyclic(packed, "fh", 1), packed])
        else:
            column = jnp.stack([shifted(packed, "fh", 1), packed, shifted(packed, "fh", -1)])
        columns = (shifted(column, "wa", 1), column, shifted(column, "wa", -1))
    flags = jnp.concatenate([side[:, 2 * tokens, :tokens] for side in columns], axis=0)
    flags = flags.reshape(1, -1)
    mask = jnp.where(flags > 0, 0.0, MASKED / HD ** (-0.5)).astype(jnp.float32)

    with jax.named_scope("cotangent_gather"):
        cot_all = lax.all_gather(out_cotangent[0, 0], "ha", axis=0, tiled=True)

    with jax.named_scope("attention_forward"):
        attended, row_max, row_inverse = attention_forward(mask, q, columns)

    with jax.named_scope("output_projection"):
        projected = jnp.dot(attended, out_weight, preferred_element_type=jnp.float32)
        layer_out = lax.psum_scatter(
            projected.astype(jnp.bfloat16), "ha", scatter_dimension=0, tiled=True
        )

    with jax.named_scope("grad_attended"):
        grad_attended = lax.dot_general(
            cot_all, out_weight, (((1,), (1,)), ((), ())), preferred_element_type=jnp.float32
        ).astype(jnp.bfloat16)

    halving = lax.axis_size("fh") == 2 and lax.axis_size("wa") == 4
    with jax.named_scope("grad_weight"):
        if halving:
            rows = model_width // 8
            cot_blocks = cot_all.reshape(-1, 2, 2, 2, rows)
            weight_blocks = lax.dot_general(
                cot_blocks, attended, (((0,), (0,)), ((), ())), preferred_element_type=jnp.float32
            )
            weight_blocks = jnp.transpose(weight_blocks, (2, 0, 1, 3, 4))
            core = lax.axis_index("wa") % 2
            weight_own = lax.dynamic_index_in_dim(weight_blocks, core, 0, keepdims=False)
            weight_sent = lax.dynamic_index_in_dim(weight_blocks, 1 - core, 0, keepdims=False)
            weight_sent = weight_sent.astype(jnp.bfloat16)
            weight_own, weight_sent, grad_attended = lax.optimization_barrier(
                (weight_own, weight_sent, grad_attended)
            )
            weight_x = weight_own + partner(weight_sent, "wa", 1).astype(jnp.float32)
        else:
            weight_part = lax.dot_general(
                cot_all, attended, (((0,), (0,)), ((), ())), preferred_element_type=jnp.float32
            )
            weight_own, weight_sent = scatter_parts(weight_part, "fh", 0)
            weight_own, weight_sent, grad_attended = lax.optimization_barrier(
                (weight_own, weight_sent, grad_attended)
            )
            weight_rows = scatter_finish(weight_own, weight_sent, "fh")

    with jax.named_scope("attention_backward"):
        grad_q, left, partials, right = attention_backward(
            mask, q, columns, attended, row_max, row_inverse, grad_attended
        )

    with jax.named_scope("grad_weight"):
        if halving:
            row = lax.axis_index("fh")
            kept = lax.dynamic_index_in_dim(weight_x, row, 0, keepdims=False)
            sent = lax.dynamic_index_in_dim(weight_x, 1 - row, 0, keepdims=False)
            weight_f = kept + partner(sent.astype(jnp.bfloat16), "fh", 1).astype(jnp.float32)
            column = lax.axis_index("wa") // 2
            kept = lax.dynamic_index_in_dim(weight_f, column, 0, keepdims=False)
            sent = lax.dynamic_index_in_dim(weight_f, 1 - column, 0, keepdims=False)
            grad_weight = kept + partner(sent.astype(jnp.bfloat16), "wa", 2).astype(jnp.float32)
        else:
            grad_weight = scatter_sum(weight_rows, "wa", 0)

    with jax.named_scope("halo_reduction"):
        middle = (
            partials
            + shifted(left, "wa", -1).astype(jnp.float32)
            + shifted(right, "wa", 1).astype(jnp.float32)
        )
        middle_sides = middle.astype(jnp.bfloat16)
        if lax.axis_size("fh") == 2:
            own = middle[1] + cyclic(middle_sides[0], "fh", 1).astype(jnp.float32)
        else:
            own = (
                middle[1]
                + shifted(middle_sides[0], "fh", -1).astype(jnp.float32)
                + shifted(middle_sides[2], "fh", 1).astype(jnp.float32)
            )
    grad_keys = own[:tokens].astype(jnp.bfloat16)
    grad_values = own[tokens:].astype(jnp.bfloat16)
    expand = lambda x: x[None, None]
    return (
        expand(layer_out),
        expand(grad_q),
        expand(grad_keys),
        expand(grad_values),
        grad_weight,
    )


def solution(mesh):
    return jax.shard_map(
        body,
        mesh=mesh,
        in_specs=(
            P("fh", "wa", None, "ha"),
            P("fh", "wa", None, "ha"),
            P("fh", "wa", None, "ha"),
            P("fh", "wa", None),
            P("ha", None),
            P("fh", "wa", "ha", None),
        ),
        out_specs=(
            P("fh", "wa", "ha", None),
            P("fh", "wa", None, "ha"),
            P("fh", "wa", None, "ha"),
            P("fh", "wa", None, "ha"),
            P(("fh", "wa"), "ha"),
        ),
        check_vma=False,
    )
```

```python
import functools

import jax
import jax.numpy as jnp
from jax import lax
from jax.experimental import pallas as pl
from jax.experimental.pallas import tpu as pltpu
from jax.sharding import PartitionSpec as P

HD = 128
MASKED = -1e30
FORWARD_CHUNK = 384
BACKWARD_CHUNK = 384
FLAG_ROWS = 16
LOG2E = 1.4426950408889634


def shift_pairs(count, steps):
    return [(source, source + steps) for source in range(count) if 0 <= source + steps < count]


def shifted(value, axis, steps):
    return lax.ppermute(value, axis, shift_pairs(lax.axis_size(axis), steps))


def partner(value, axis, bit):
    count = lax.axis_size(axis)
    return lax.ppermute(value, axis, [(i, i ^ bit) for i in range(count)])


def cyclic(value, axis, steps):
    count = lax.axis_size(axis)
    return lax.ppermute(value, axis, [(i, (i + steps) % count) for i in range(count)])


def joined(refs):
    return jnp.concatenate([ref[...].reshape(-1, HD) for ref in refs], axis=0)


def raw_scores(mask_ref, q_ref, k):
    s = lax.dot_general(q_ref[...], k, (((1,), (1,)), ((), ())), preferred_element_type=jnp.float32)
    return s + mask_ref[...]


def forward_kernel(exp_scale, mask_ref, q_ref, kl, km, kr, vl, vm, vr, o_ref, m_ref, r_ref):
    s = raw_scores(mask_ref, q_ref, joined((kl, km, kr)))
    m = jnp.max(s, axis=1, keepdims=True)
    e = jnp.exp2((s - m) * exp_scale)
    inverse = 1.0 / jnp.sum(e, axis=1, keepdims=True)
    p = (e * inverse).astype(jnp.bfloat16)
    v = joined((vl, vm, vr))
    o_ref[...] = jnp.dot(p, v, preferred_element_type=jnp.float32).astype(o_ref.dtype)
    m_ref[...] = jnp.broadcast_to(m, m_ref.shape)
    r_ref[...] = jnp.broadcast_to(inverse, r_ref.shape)


def backward_kernel(
    scale, exp_scale, mask_ref, q_ref, kl, km, kr, vl, vm, vr, o_ref, m_ref, r_ref, do_ref,
    dq_ref, left_ref, mid_ref, right_ref, acc_ref
):
    chunk = pl.program_id(1)
    k = joined((kl, km, kr))
    v = joined((vl, vm, vr))
    s = raw_scores(mask_ref, q_ref, k)
    w = jnp.exp2((s - m_ref[:, :1]) * exp_scale) * r_ref[:, :1]
    p = w.astype(jnp.bfloat16)
    do = do_ref[...]
    row_dot = jnp.sum(
        do.astype(jnp.float32) * o_ref[...].astype(jnp.float32), axis=1, keepdims=True
    )
    dp = lax.dot_general(do, v, (((1,), (1,)), ((), ())), preferred_element_type=jnp.float32)
    ds = (w * (dp - row_dot)).astype(jnp.bfloat16)
    dq = jnp.dot(ds, k, preferred_element_type=jnp.float32) * scale
    dq_ref[...] = dq.astype(dq_ref.dtype)
    contract0 = (((0,), (0,)), ((), ()))
    dk = lax.dot_general(ds, q_ref[...], contract0, preferred_element_type=jnp.float32) * scale
    dv = lax.dot_general(p, do, contract0, preferred_element_type=jnp.float32)
    tiles, tokens = 3 * kl.shape[0], kl.shape[1]
    dk = dk.reshape(tiles, tokens, HD)
    dv = dv.reshape(tiles, tokens, HD)

    @pl.when(chunk == 0)
    def _():
        acc_ref[:, :tokens, :] = dk
        acc_ref[:, tokens:, :] = dv

    @pl.when(chunk > 0)
    def _():
        acc_ref[:, :tokens, :] += dk
        acc_ref[:, tokens:, :] += dv

    @pl.when(chunk == pl.num_programs(1) - 1)
    def _():
        third = tiles // 3
        left_ref[...] = acc_ref[:third].astype(left_ref.dtype)
        mid_ref[...] = acc_ref[third : 2 * third]
        right_ref[...] = acc_ref[2 * third :].astype(right_ref.dtype)


def attention_forward(mask, queries, columns):
    tokens, features = queries.shape
    tiles = 3 * columns[0].shape[0]
    heads = features // HD
    chunk = FORWARD_CHUNK
    chunks = tokens // chunk
    scale = HD ** (-0.5)
    return pl.pallas_call(
        functools.partial(forward_kernel, scale * LOG2E),
        grid=(heads, chunks),
        in_specs=[
            pl.BlockSpec((1, tiles * tokens), lambda h, c: (0, 0)),
            pl.BlockSpec((chunk, HD), lambda h, c: (c, h)),
            *[pl.BlockSpec((tiles // 3, tokens, HD), lambda h, c: (0, 0, h))] * 3,
            *[pl.BlockSpec((tiles // 3, tokens, HD), lambda h, c: (0, 1, h))] * 3,
        ],
        out_specs=[pl.BlockSpec((chunk, HD), lambda h, c: (c, h))] * 3,
        out_shape=[
            jax.ShapeDtypeStruct((tokens, features), jnp.bfloat16),
            jax.ShapeDtypeStruct((tokens, features), jnp.float32),
            jax.ShapeDtypeStruct((tokens, features), jnp.float32),
        ],
        name="tile_attention_forward",
    )(mask, queries, *columns, *columns)


def attention_backward(mask, queries, columns, attended, row_max, row_inverse, grad_attended):
    tokens, features = queries.shape
    tiles = 3 * columns[0].shape[0]
    heads = features // HD
    chunk = BACKWARD_CHUNK
    chunks = tokens // chunk
    scale = HD ** (-0.5)
    return pl.pallas_call(
        functools.partial(backward_kernel, scale, scale * LOG2E),
        grid=(heads, chunks),
        in_specs=[
            pl.BlockSpec((1, tiles * tokens), lambda h, c: (0, 0)),
            pl.BlockSpec((chunk, HD), lambda h, c: (c, h)),
            *[pl.BlockSpec((tiles // 3, tokens, HD), lambda h, c: (0, 0, h))] * 3,
            *[pl.BlockSpec((tiles // 3, tokens, HD), lambda h, c: (0, 1, h))] * 3,
            pl.BlockSpec((chunk, HD), lambda h, c: (c, h)),
            pl.BlockSpec((chunk, HD), lambda h, c: (c, h)),
            pl.BlockSpec((chunk, HD), lambda h, c: (c, h)),
            pl.BlockSpec((chunk, HD), lambda h, c: (c, h)),
        ],
        out_specs=[
            pl.BlockSpec((chunk, HD), lambda h, c: (c, h)),
            pl.BlockSpec((tiles // 3, 2 * tokens, HD), lambda h, c: (0, 0, h)),
            pl.BlockSpec((tiles // 3, 2 * tokens, HD), lambda h, c: (0, 0, h)),
            pl.BlockSpec((tiles // 3, 2 * tokens, HD), lambda h, c: (0, 0, h)),
        ],
        out_shape=[
            jax.ShapeDtypeStruct((tokens, features), jnp.bfloat16),
            jax.ShapeDtypeStruct((tiles // 3, 2 * tokens, features), jnp.bfloat16),
            jax.ShapeDtypeStruct((tiles // 3, 2 * tokens, features), jnp.float32),
            jax.ShapeDtypeStruct((tiles // 3, 2 * tokens, features), jnp.bfloat16),
        ],
        scratch_shapes=[pltpu.VMEM((tiles, 2 * tokens, HD), jnp.float32)],
        name="tile_attention_backward",
    )(mask, queries, *columns, *columns, attended, row_max, row_inverse, grad_attended)


def gather_over(piece, axis):
    count = lax.axis_size(axis)
    me = lax.axis_index(axis)
    received = [piece] + [cyclic(piece, axis, steps) for steps in range(1, count)]
    ordered = jnp.stack([received[(-k) % count] for k in range(count)])
    return jnp.roll(ordered, me, axis=0)


def scatter_parts(full, axis, dim):
    count = lax.axis_size(axis)
    me = lax.axis_index(axis)
    size = full.shape[dim] // count

    def part(index):
        return lax.dynamic_slice_in_dim(full, index * size, size, axis=dim)

    sent = [part((me + steps) % count).astype(jnp.bfloat16) for steps in range(1, count)]
    return part(me).astype(jnp.float32), sent


def scatter_finish(own, sent, axis):
    total = own
    for steps, piece in enumerate(sent, start=1):
        total = total + cyclic(piece, axis, steps).astype(jnp.float32)
    return total


def scatter_sum(full, axis, dim):
    count = lax.axis_size(axis)
    me = lax.axis_index(axis)
    size = full.shape[dim] // count

    def part(index):
        return lax.dynamic_slice_in_dim(full, index * size, size, axis=dim)

    total = part(me).astype(jnp.float32)
    for steps in range(1, count):
        sent = part((me + steps) % count).astype(jnp.bfloat16)
        total = total + cyclic(sent, axis, steps).astype(jnp.float32)
    return total


def body(queries, key_states, value_states, valid_mask, out_weight, out_cotangent):
    tile_rows, tile_columns, tokens, features = queries.shape
    assert tile_rows == 1 and tile_columns == 1
    model_width = out_weight.shape[1]
    q = queries[0, 0]
    flag_rows = jnp.zeros((FLAG_ROWS, features), jnp.bfloat16)
    flag_rows = flag_rows.at[0, :tokens].set(valid_mask[0, 0].astype(jnp.bfloat16))
    packed = jnp.concatenate([key_states[0, 0], value_states[0, 0], flag_rows], axis=0)

    with jax.named_scope("halo_exchange"):
        if lax.axis_size("fh") == 2:
            column = jnp.stack([cyclic(packed, "fh", 1), packed])
        else:
            column = jnp.stack([shifted(packed, "fh", 1), packed, shifted(packed, "fh", -1)])
        columns = (shifted(column, "wa", 1), column, shifted(column, "wa", -1))
    flags = jnp.concatenate([side[:, 2 * tokens, :tokens] for side in columns], axis=0)
    flags = flags.reshape(1, -1)
    mask = jnp.where(flags > 0, 0.0, MASKED / HD ** (-0.5)).astype(jnp.float32)

    with jax.named_scope("cotangent_gather"):
        cot_all = lax.all_gather(out_cotangent[0, 0], "ha", axis=0, tiled=True)

    with jax.named_scope("attention_forward"):
        attended, row_max, row_inverse = attention_forward(mask, q, columns)

    with jax.named_scope("output_projection"):
        projected = jnp.dot(attended, out_weight, preferred_element_type=jnp.float32)
        layer_out = lax.psum_scatter(
            projected.astype(jnp.bfloat16), "ha", scatter_dimension=0, tiled=True
        )

    with jax.named_scope("grad_attended"):
        grad_attended = lax.dot_general(
            cot_all, out_weight, (((1,), (1,)), ((), ())), preferred_element_type=jnp.float32
        ).astype(jnp.bfloat16)

    halving = lax.axis_size("fh") == 2 and lax.axis_size("wa") == 4
    with jax.named_scope("grad_weight"):
        if halving:
            rows = model_width // 8
            cot_blocks = cot_all.reshape(-1, 2, 2, 2, rows)
            weight_blocks = lax.dot_general(
                cot_blocks, attended, (((0,), (0,)), ((), ())), preferred_element_type=jnp.float32
            )
            weight_blocks = jnp.transpose(weight_blocks, (2, 0, 1, 3, 4))
            core = lax.axis_index("wa") % 2
            weight_own = lax.dynamic_index_in_dim(weight_blocks, core, 0, keepdims=False)
            weight_sent = lax.dynamic_index_in_dim(weight_blocks, 1 - core, 0, keepdims=False)
            weight_sent = weight_sent.astype(jnp.bfloat16)
            weight_x = weight_own + partner(weight_sent, "wa", 1).astype(jnp.float32)
        else:
            weight_part = lax.dot_general(
                cot_all, attended, (((0,), (0,)), ((), ())), preferred_element_type=jnp.float32
            )
            weight_own, weight_sent = scatter_parts(weight_part, "fh", 0)
            weight_own, weight_sent, grad_attended = lax.optimization_barrier(
                (weight_own, weight_sent, grad_attended)
            )
            weight_rows = scatter_finish(weight_own, weight_sent, "fh")

    with jax.named_scope("attention_backward"):
        grad_q, left, partials, right = attention_backward(
            mask, q, columns, attended, row_max, row_inverse, grad_attended
        )

    with jax.named_scope("grad_weight"):
        if halving:
            row = lax.axis_index("fh")
            kept = lax.dynamic_index_in_dim(weight_x, row, 0, keepdims=False)
            sent = lax.dynamic_index_in_dim(weight_x, 1 - row, 0, keepdims=False)
            weight_f = kept + partner(sent.astype(jnp.bfloat16), "fh", 1).astype(jnp.float32)
            column = lax.axis_index("wa") // 2
            kept = lax.dynamic_index_in_dim(weight_f, column, 0, keepdims=False)
            sent = lax.dynamic_index_in_dim(weight_f, 1 - column, 0, keepdims=False)
            grad_weight = kept + partner(sent.astype(jnp.bfloat16), "wa", 2).astype(jnp.float32)
        else:
            grad_weight = scatter_sum(weight_rows, "wa", 0)

    with jax.named_scope("halo_reduction"):
        middle = (
            partials
            + shifted(left, "wa", -1).astype(jnp.float32)
            + shifted(right, "wa", 1).astype(jnp.float32)
        )
        middle_sides = middle.astype(jnp.bfloat16)
        if lax.axis_size("fh") == 2:
            own = middle[1] + cyclic(middle_sides[0], "fh", 1).astype(jnp.float32)
        else:
            own = (
                middle[1]
                + shifted(middle_sides[0], "fh", -1).astype(jnp.float32)
                + shifted(middle_sides[2], "fh", 1).astype(jnp.float32)
            )
    grad_keys = own[:tokens].astype(jnp.bfloat16)
    grad_values = own[tokens:].astype(jnp.bfloat16)
    expand = lambda x: x[None, None]
    return (
        expand(layer_out),
        expand(grad_q),
        expand(grad_keys),
        expand(grad_values),
        grad_weight,
    )


def solution(mesh):
    return jax.shard_map(
        body,
        mesh=mesh,
        in_specs=(
            P("fh", "wa", None, "ha"),
            P("fh", "wa", None, "ha"),
            P("fh", "wa", None, "ha"),
            P("fh", "wa", None),
            P("ha", None),
            P("fh", "wa", "ha", None),
        ),
        out_specs=(
            P("fh", "wa", "ha", None),
            P("fh", "wa", None, "ha"),
            P("fh", "wa", None, "ha"),
            P("fh", "wa", None, "ha"),
            P(("fh", "wa"), "ha"),
        ),
        check_vma=False,
    )
```
